32 devices in a mesh: seq: 8 (over y, x, core), head: 4 (over z).
Axes of the slice: x: 2, y: 2, z: 4, core: 2. Of those that a mesh axis runs over, the one named last changes fastest.
Arguments:
- tokens: bfloat16 [8192, 1024], P(('seq', 'head')), may hold values from -6 to 6
- qkv_weight: bfloat16 [1024, 3, 1024], P(None, None, 'head'), may hold values from -0.1875 to 0.1875
- out_weight: bfloat16 [1024, 1024], P('head'), may hold values from -0.1875 to 0.1875
- up_weight: bfloat16 [1024, 2, 2816], P(None, None, 'head'), may hold values from -0.1875 to 0.1875
- down_weight: bfloat16 [2816, 1024], P('head'), may hold values from -0.109375 to 0.109375
- vocab_weight: bfloat16 [1024, 16384], P(None, 'head'), may hold values from -0.1875 to 0.1875
- persistent: bfloat16 [2, 16, 1024], P(None, None, 'head'), may hold values from -120 to 120
- norm_gains: float32 [3, 1024], replicated, may hold values from 0.5 to 1.5
- write_rate: float32 [8192, 8], P('seq', 'head'), may hold values from 0.02 to 0.2
- forget: float32 [128, 8], P('seq', 'head'), may hold values from 0 to 1
- momentum: float32 [128, 8], P('seq', 'head'), may hold values from 0.2 to 0.9
- prompt_spans: int32 [4], replicated, may hold values from 1 to 64, as said below
Outputs:
- logit_max: float32 [8192], P('seq')
- state_rms: float32 [4, 8], P(None, 'head')
The draws below stay inside these ranges and needn't reach their ends.
Inputs may be any that keep to these rules, and one draw needn't show every extreme that they name: Prompt p holds prompt_spans[p] consecutive spans of 64 tokens, the prompts packed in order from token 0; they sum to 128, and prompt 1 is the longest, with exactly 64 spans.
All inputs are finite; a program needn't handle non-finite values.
Results may differ from the reference program's by a relative error of at most 0.0047.
Values may be sent and summed in bfloat16 or wider, within the bound.
No kernel may reach another device: no remote copies, remote signals or barrier semaphores. Data moves between devices by JAX's collectives and lax.ppermute only.
A program may use at most 128 MiB of HBM per device.

```python
import math
import jax
import jax.numpy as jnp
from jax import lax

D = 1024
H = 8
HS = 128
FF = 2816
VOCAB = 16384
NPER = 16
SEG = 1024
CH = 64
TOK_DEV = 1024
TOKENS = 8192
MEMORY_SPANS = 128
N_SEQ = 8


def draw_persistent(key, part):
    key_base, key_values = jax.random.split(jax.random.fold_in(key, 11), 2)
    persist_keys = 0.3 * jax.random.normal(key_base, (NPER, D), jnp.float32)
    persist_values = jax.random.normal(key_values, (NPER, D), jnp.float32)
    persist_keys = jnp.clip(persist_keys, -120.0, 120.0)
    persist_values = jnp.clip(persist_values, -6.0, 6.0)
    return jnp.stack([persist_keys, persist_values], axis=0).astype(jnp.bfloat16)


def draw_forget(key, part):
    every_key = jax.random.split(jax.random.fold_in(key, 23), 6)
    slow_heads = jax.random.bernoulli(every_key[0], 0.5, (H,))
    slow_rate = jnp.exp(jax.random.uniform(every_key[1], (H,), jnp.float32, math.log(0.3), math.log(2.0))) / MEMORY_SPANS
    fast_rate = CH / jax.random.uniform(every_key[2], (H,), jnp.float32, 30.0, 50.0)
    jitter = jnp.exp(jax.random.uniform(every_key[3], (MEMORY_SPANS, H), jnp.float32, -0.7, 0.7))
    surge_groups = jax.random.bernoulli(every_key[4], 4.0 / MEMORY_SPANS, (MEMORY_SPANS, 1))
    surge_multiplier = jnp.where(surge_groups, jax.random.uniform(every_key[5], (MEMORY_SPANS, 1), jnp.float32, 0.5, 0.8), 1.0)
    learning_rates = jnp.where(slow_heads, slow_rate, fast_rate)[None, :] * jitter
    return (jnp.exp(-learning_rates) * surge_multiplier).astype(jnp.float32)


def draw_prompt_spans(key, part):
    key_lead, key_third = jax.random.split(jax.random.fold_in(key, 37), 2)
    half_spans = MEMORY_SPANS // 2
    seg_spans = SEG // CH
    leading = jax.random.randint(key_lead, (), 1, max(2, half_spans - 2), dtype=jnp.int32)
    leading = jnp.where((half_spans - leading) % seg_spans == 0, leading + 1, leading).astype(jnp.int32)
    remaining = (half_spans - leading).astype(jnp.int32)
    third = jax.random.randint(key_third, (), 1, remaining, dtype=jnp.int32)
    return jnp.stack([leading, jnp.array(half_spans, jnp.int32), third, remaining - third]).astype(jnp.int32)


def level_of(key, dims, shards, smallest, largest):
    loudness = 1.0
    for axis_at, blocks in shards:
        draws = jax.random.uniform(jax.random.fold_in(jax.random.fold_in(key, 6), axis_at), (blocks,), jnp.float32, smallest / len(shards), largest / len(shards))
        loudness = loudness * jnp.repeat(jnp.exp(draws), dims[axis_at] // blocks).reshape((-1,) + (1,) * (len(dims) - 1 - axis_at))
    return loudness


def normal_values(own_key, extent, width, limit, cuts=(), kind=jnp.bfloat16):
    values = width * jax.random.normal(own_key, extent, jnp.float32)
    if cuts:
        values = values * level_of(own_key, extent, cuts, -0.22, 0.18)
    return jnp.clip(values, -limit, limit).astype(kind)


def setup_inputs(seed: int = 0) -> dict:
    key_of = jax.random.split(jax.random.key(seed), 13)
    tokens = normal_values(key_of[0], (TOKENS, D), 1.0, 6.0, ((0, 32),))
    qkv_weight = normal_values(key_of[1], (D, 3, D), D ** -0.5, 0.1875, ((2, 4),))
    out_weight = normal_values(key_of[2], (D, D), D ** -0.5, 0.1875, ((0, 4),))
    up_weight = normal_values(key_of[3], (D, 2, FF), D ** -0.5, 0.1875, ((2, 4),))
    down_weight = normal_values(key_of[4], (FF, D), FF ** -0.5, 0.109375, ((0, 4),))
    vocab_weight = normal_values(key_of[5], (D, VOCAB), D ** -0.5, 0.1875, ((1, 4),))
    persistent = draw_persistent(jax.random.fold_in(key_of[12], 71), 0)
    norm_gains = jnp.clip(1.0 + 0.1 * jax.random.normal(key_of[7], (3, D), jnp.float32), 0.5, 1.5)
    write_rate = jnp.clip(jnp.exp(math.log(0.2) - 2.3025851 * jax.random.uniform(key_of[8], (TOKENS, H), jnp.float32) ** level_of(key_of[8], (TOKENS, H), ((0, 8), (1, 4)), -0.2, 0.2)), 0.02, 0.2)
    forget = draw_forget(jax.random.fold_in(key_of[12], 71), 0)
    momentum = jnp.clip(0.2 + 0.7 * jax.random.uniform(key_of[10], (MEMORY_SPANS, H), jnp.float32) ** level_of(key_of[10], (MEMORY_SPANS, H), ((0, 8), (1, 4)), -0.2, 0.2), 0.2, 0.9)
    prompt_spans = draw_prompt_spans(jax.random.fold_in(key_of[12], 71), 0)
    return dict(tokens=tokens, qkv_weight=qkv_weight, out_weight=out_weight, up_weight=up_weight, down_weight=down_weight, vocab_weight=vocab_weight, persistent=persistent, norm_gains=norm_gains, write_rate=write_rate, forget=forget, momentum=momentum, prompt_spans=prompt_spans)


eps_norm = 1e-05
eps_unit = 1e-06
score_scale = 10.0
masked_score = -1e+30

def rms_scale(values, gain):
    return values * lax.rsqrt(lax.optimization_barrier(jnp.mean(values * values, axis=-1, keepdims=True)) + eps_norm) * gain

def unit_rows(values):
    widened = values.astype(jnp.float32)
    return (widened * lax.rsqrt(lax.optimization_barrier(jnp.sum(widened * widened, axis=-1, keepdims=True)) + eps_unit)).astype(jnp.bfloat16)

def segment_starts(positions, prompt_spans):
    prompt_ends = jnp.cumsum(prompt_spans)
    first_tokens = (prompt_ends - prompt_spans) * CH
    reached = positions[:, None] >= first_tokens[None, :]
    prompt_first = lax.optimization_barrier(jnp.max(jnp.where(reached, first_tokens[None, :], 0), axis=1))
    return prompt_first + (positions - prompt_first) // SEG * SEG

def reference(tokens, qkv_weight, out_weight, up_weight, down_weight, vocab_weight, persistent, norm_gains, write_rate, forget, momentum, prompt_spans):
    widened = tokens.astype(jnp.float32)
    normed = rms_scale(widened, norm_gains[0]).astype(jnp.bfloat16)
    projected = jnp.dot(normed, qkv_weight.reshape(D, 3 * D), preferred_element_type=jnp.float32).astype(jnp.bfloat16)
    projected = projected.reshape(TOKENS, 3, H, HS)
    query_unit = unit_rows(projected[:, 0])
    key_unit = unit_rows(projected[:, 1])
    value_rows = projected[:, 2]
    positions = jnp.arange(TOKENS, dtype=jnp.int32)
    segment_start = segment_starts(positions, prompt_spans)
    padded_keys = jnp.concatenate([jnp.zeros((SEG, H, HS), jnp.bfloat16), key_unit], axis=0)
    padded_values = jnp.concatenate([jnp.zeros((SEG, H, HS), jnp.bfloat16), value_rows], axis=0)
    padded_segments = jnp.concatenate([jnp.full((SEG,), -1, jnp.int32), segment_start], axis=0)
    padded_positions = jnp.arange(TOKENS + SEG, dtype=jnp.int32) - SEG
    persist_keys = persistent[0].reshape(NPER, H, HS).astype(jnp.float32)
    persist_values = persistent[1].reshape(NPER, H, HS).astype(jnp.float32)

    def attend(block_index):
        first = (block_index * SEG).astype(jnp.int32)
        queries = lax.dynamic_slice_in_dim(query_unit, first, SEG, 0).astype(jnp.float32)
        keys_here = lax.dynamic_slice_in_dim(padded_keys, first, 2 * SEG, 0).astype(jnp.float32)
        values_here = lax.dynamic_slice_in_dim(padded_values, first, 2 * SEG, 0).astype(jnp.float32)
        key_segments = lax.dynamic_slice_in_dim(padded_segments, first, 2 * SEG, 0)
        key_positions = lax.dynamic_slice_in_dim(padded_positions, first, 2 * SEG, 0)
        query_segments = lax.dynamic_slice_in_dim(segment_start, first, SEG, 0)
        query_positions = first + jnp.arange(SEG, dtype=jnp.int32)
        allowed = (key_segments[None, :] == query_segments[:, None]) & (key_positions[None, :] <= query_positions[:, None]) & (key_positions[None, :] >= 0)
        scores = score_scale * jnp.einsum('qhd,khd->hqk', queries, keys_here)
        scores = jnp.where(allowed[None], scores, masked_score)
        extra = score_scale * jnp.einsum('qhd,phd->hqp', queries, persist_keys)
        top = jnp.maximum(lax.optimization_barrier(jnp.max(scores, axis=-1)), lax.optimization_barrier(jnp.max(extra, axis=-1)))[..., None]
        near = jnp.where(allowed[None], jnp.exp(scores - top), 0.0)
        far = jnp.exp(extra - top)
        total = lax.optimization_barrier(jnp.sum(near, axis=-1, keepdims=True)) + lax.optimization_barrier(jnp.sum(far, axis=-1, keepdims=True))
        near_weights = (near / total).astype(jnp.bfloat16).astype(jnp.float32)
        far_weights = (far / total).astype(jnp.bfloat16).astype(jnp.float32)
        return jnp.einsum('hqk,khd->qhd', near_weights, values_here) + jnp.einsum('hqp,phd->qhd', far_weights, persist_values)
    attended = lax.map(attend, jnp.arange(TOKENS // SEG, dtype=jnp.int32)).reshape(TOKENS, H, HS)
    prompt_ends = jnp.cumsum(prompt_spans)
    first_spans = prompt_ends - prompt_spans
    span_ids = jnp.arange(MEMORY_SPANS, dtype=jnp.int32)
    keep = jnp.where(jnp.any(span_ids[:, None] == first_spans[None, :], axis=1), 0.0, 1.0).astype(jnp.float32)
    causal = (jnp.arange(CH)[:, None] >= jnp.arange(CH)[None, :]).astype(jnp.float32)
    span_queries = query_unit.reshape(MEMORY_SPANS, CH, H, HS)
    span_keys = key_unit.reshape(MEMORY_SPANS, CH, H, HS)
    span_values = value_rows.reshape(MEMORY_SPANS, CH, H, HS)
    span_rates = write_rate.reshape(MEMORY_SPANS, CH, H)
    highest = lax.Precision.HIGHEST

    def advance(carry, inputs):
        memory, moment = carry
        queries, keys_here, values_here, learning_rates, keep_here, forget_here, momentum_here = inputs
        queries = queries.astype(jnp.float32)
        keys_here = keys_here.astype(jnp.float32)
        values_here = values_here.astype(jnp.float32)
        kept_memory = keep_here * memory
        kept_moment = keep_here * moment
        recalled = jnp.einsum('hij,thj->thi', kept_memory, queries, precision=highest)
        affinity = jnp.einsum('thd,shd->hts', queries, keys_here) * causal[None] * learning_rates.T[:, None, :]
        recalled = recalled + jnp.einsum('hts,shi->thi', affinity, values_here, precision=highest)
        written = jnp.einsum('thi,thj->hij', learning_rates[:, :, None] * values_here, keys_here, precision=highest)
        moment = momentum_here[:, None, None] * kept_moment + written
        memory = forget_here[:, None, None] * kept_memory + moment
        spread = jnp.sqrt(lax.optimization_barrier(jnp.mean(memory * memory, axis=(1, 2))))
        return ((memory, moment), (recalled, spread))
    zeros_state = jnp.zeros((H, HS, HS), jnp.float32)
    _, (recalled, spread) = lax.scan(advance, (zeros_state, zeros_state), (span_queries, span_keys, span_values, span_rates, keep, forget, momentum))
    recalled = recalled.reshape(TOKENS, H, HS)
    state_rms = jnp.take(spread, (prompt_ends - 1).astype(jnp.int32), axis=0)
    mixed = (attended + recalled).astype(jnp.bfloat16).reshape(TOKENS, D)
    residual = widened + jnp.dot(mixed, out_weight, preferred_element_type=jnp.float32)
    ffn_in = rms_scale(residual, norm_gains[1]).astype(jnp.bfloat16)
    gated = jnp.dot(ffn_in, up_weight.reshape(D, 2 * FF), preferred_element_type=jnp.float32)
    hidden = (jax.nn.silu(gated[:, :FF]) * gated[:, FF:]).astype(jnp.bfloat16)
    second = residual + jnp.dot(hidden, down_weight, preferred_element_type=jnp.float32)
    final = rms_scale(second, norm_gains[2]).astype(jnp.bfloat16)

    def row_maxima(block_index):
        rows_here = lax.dynamic_slice_in_dim(final, (block_index * TOK_DEV).astype(jnp.int32), TOK_DEV, 0)
        return lax.optimization_barrier(jnp.max(jnp.dot(rows_here, vocab_weight, preferred_element_type=jnp.float32), axis=1))
    logit_max = lax.map(row_maxima, jnp.arange(N_SEQ, dtype=jnp.int32)).reshape(TOKENS)
    return (logit_max, state_rms)
```

```python
import jax
import jax.numpy as jnp
from jax import lax
from jax.sharding import PartitionSpec as P

D = 1024
HS = 128
NPER = 16
SEG = 1024
CH = 64
SEQS = 4


eps_norm = 1e-05
eps_unit = 1e-06
score_scale = 10.0
masked_score = -1e30


def passed_along(array, axis, by):
    size = lax.axis_size(axis)
    pairs = [(i, i + by) for i in range(size) if 0 <= i + by < size]
    return lax.ppermute(array, axis, pairs)


def carried_in(part, axis, combine, identity):
    place = lax.axis_index(axis)
    gathered = jax.tree.map(lambda a: lax.all_gather(a, axis), part)
    state = jax.tree.map(lambda a, e: jnp.zeros_like(a) + jnp.asarray(e, a.dtype), part, identity)

    def one(step, state):
        return combine(
            state, jax.tree.map(lambda a: lax.dynamic_index_in_dim(a, step, 0, False), gathered)
        )

    return lax.fori_loop(0, place, one, state)


def rms_scale(values, gain):
    return values * lax.rsqrt(jnp.mean(values * values, axis=-1, keepdims=True) + eps_norm) * gain


def unit_rows(values):
    widened = values.astype(jnp.float32)
    return (
        widened * lax.rsqrt(jnp.sum(widened * widened, axis=-1, keepdims=True) + eps_unit)
    ).astype(jnp.bfloat16)


def segment_starts(positions, prompt_spans):
    prompt_ends = jnp.cumsum(prompt_spans)
    first_tokens = (prompt_ends - prompt_spans) * CH
    reached = positions[:, None] >= first_tokens[None, :]
    prompt_first = jnp.max(jnp.where(reached, first_tokens[None, :], 0), axis=1)
    return prompt_first + (positions - prompt_first) // SEG * SEG


def compose(later, earlier):
    return jnp.stack(
        [
            later[..., 0] * earlier[..., 0],
            later[..., 0] * earlier[..., 1] + later[..., 1] * earlier[..., 2],
            later[..., 2] * earlier[..., 2],
        ],
        axis=-1,
    )


def apply_map(coeffs, memory, moment):
    moved_memory = coeffs[:, 0, None, None] * memory + coeffs[:, 1, None, None] * moment
    return (moved_memory, coeffs[:, 2, None, None] * moment)


def chain_combine(earlier, later):
    moved_memory, moved_moment = apply_map(later[0], earlier[1], earlier[2])
    return (compose(later[0], earlier[0]), moved_memory + later[1], moved_moment + later[2])


def to_owners(local_rows, project):
    return project(lax.all_gather(local_rows, "head", axis=0, tiled=True), jnp.int32(0))


def from_owners(term, share_rows):
    return lax.psum_scatter(
        term(jnp.int32(0), share_rows * lax.axis_size("head")),
        "head",
        scatter_dimension=0,
        tiled=True,
    )


def local(
    tokens,
    qkv_weight,
    out_weight,
    up_weight,
    down_weight,
    vocab_weight,
    persistent,
    norm_gains,
    write_rate,
    forget,
    momentum,
    prompt_spans,
):
    share_rows = tokens.shape[0]
    head_count = lax.axis_size("head")
    seq_count = lax.axis_size("seq")
    block_rows = share_rows * head_count
    heads_here = write_rate.shape[1]
    current_width = heads_here * HS
    seq_index = lax.axis_index("seq")
    head_index = lax.axis_index("head")
    qkv_matrix = qkv_weight.reshape(D, 3 * current_width)
    highest = lax.Precision.HIGHEST

    def token_project(piece, start):
        normed = rms_scale(piece.astype(jnp.float32), norm_gains[0]).astype(jnp.bfloat16)
        projected = jnp.dot(normed, qkv_matrix, preferred_element_type=jnp.float32).astype(
            jnp.bfloat16
        )
        return projected

    gathered = to_owners(tokens, token_project)
    projected = gathered
    query_unit = unit_rows(projected[:, :current_width].reshape(block_rows, heads_here, HS))
    key_unit = unit_rows(
        projected[:, current_width : 2 * current_width].reshape(block_rows, heads_here, HS)
    )
    value_rows = projected[:, 2 * current_width :].reshape(block_rows, heads_here, HS)
    reach = SEG // block_rows
    moved_keys, moved_values = passed_along((key_unit, value_rows), "seq", 1)
    earlier_keys = [moved_keys]
    earlier_values = [moved_values]
    all_keys = jnp.concatenate(earlier_keys + [key_unit], axis=0)
    all_values = jnp.concatenate(earlier_values + [value_rows], axis=0)
    first_row = seq_index * block_rows
    query_positions = first_row + jnp.arange(block_rows, dtype=jnp.int32)
    key_positions = (
        first_row - reach * block_rows + jnp.arange((reach + 1) * block_rows, dtype=jnp.int32)
    )
    query_segments = segment_starts(query_positions, prompt_spans)
    key_segments = segment_starts(key_positions, prompt_spans)
    allowed = (
        (key_segments[None, :] == query_segments[:, None])
        & (key_positions[None, :] <= query_positions[:, None])
        & (key_positions[None, :] >= 0)
    )
    persist_keys = persistent[0].reshape(NPER, heads_here, HS)
    persist_values = persistent[1].reshape(NPER, heads_here, HS)
    scores = score_scale * jnp.einsum(
        "qhd,khd->hqk", query_unit, all_keys, preferred_element_type=jnp.float32
    )
    scores = jnp.where(allowed[None], scores, masked_score)
    extra = score_scale * jnp.einsum(
        "qhd,phd->hqp", query_unit, persist_keys, preferred_element_type=jnp.float32
    )
    top = jnp.maximum(jnp.max(scores, axis=-1), jnp.max(extra, axis=-1))[..., None]
    near = jnp.where(allowed[None], jnp.exp(scores - top), 0.0)
    far = jnp.exp(extra - top)
    total = jnp.sum(near, axis=-1, keepdims=True) + jnp.sum(far, axis=-1, keepdims=True)
    near_weights = (near / total).astype(jnp.bfloat16)
    far_weights = (far / total).astype(jnp.bfloat16)
    attended = jnp.einsum(
        "hqk,khd->qhd", near_weights, all_values, preferred_element_type=jnp.float32
    )
    attended = attended + jnp.einsum(
        "hqp,phd->qhd", far_weights, persist_values, preferred_element_type=jnp.float32
    )
    total_spans = block_rows // CH
    span_queries = query_unit.reshape(total_spans, CH, heads_here, HS)
    span_keys = key_unit.reshape(total_spans, CH, heads_here, HS)
    span_values = value_rows.reshape(total_spans, CH, heads_here, HS)
    span_rates = write_rate.reshape(total_spans, CH, heads_here)
    prompt_ends = jnp.cumsum(prompt_spans)
    first_spans = prompt_ends - prompt_spans
    span_ids = seq_index * total_spans + jnp.arange(total_spans, dtype=jnp.int32)
    keep = jnp.where(jnp.any(span_ids[:, None] == first_spans[None, :], axis=1), 0.0, 1.0).astype(
        jnp.float32
    )
    causal = (jnp.arange(CH)[:, None] >= jnp.arange(CH)[None, :]).astype(jnp.float32)
    values_wide = span_values.astype(jnp.float32)
    written = jnp.einsum(
        "cthi,cthj->chij",
        span_rates[..., None] * values_wide,
        span_keys.astype(jnp.float32),
        precision=highest,
    )
    affinity = jnp.einsum(
        "cthd,cshd->chts", span_queries, span_keys, preferred_element_type=jnp.float32
    )
    affinity = affinity * causal[None, None] * jnp.transpose(span_rates, (0, 2, 1))[:, :, None, :]
    local_recall = jnp.einsum("chts,cshi->cthi", affinity, values_wide, precision=highest)
    decay_memory = forget * keep[:, None]
    decay_moment = momentum * keep[:, None]
    identity_coeffs = jnp.tile(jnp.array([1.0, 0.0, 1.0], jnp.float32), (heads_here, 1))
    zero_state = jnp.zeros((heads_here, HS, HS), jnp.float32)

    def advance(carry, inputs):
        coeffs, memory, moment = carry
        current_written, memory_rate, moment_rate = inputs
        step_coeffs = jnp.stack([memory_rate, moment_rate, moment_rate], axis=-1)
        next_moment = moment_rate[:, None, None] * moment + current_written
        next_memory = (
            memory_rate[:, None, None] * memory
            + moment_rate[:, None, None] * moment
            + current_written
        )
        return ((compose(step_coeffs, coeffs), next_memory, next_moment), (coeffs, memory))

    (last_coeffs, last_memory, last_moment), (coeffs_before, memory_before) = lax.scan(
        advance, (identity_coeffs, zero_state, zero_state), (written, decay_memory, decay_moment)
    )
    _, incoming_memory, incoming_moment = carried_in(
        (last_coeffs, last_memory, last_moment),
        "seq",
        chain_combine,
        (identity_coeffs, zero_state, zero_state),
    )
    true_before = (
        memory_before
        + coeffs_before[..., 0, None, None] * incoming_memory[None]
        + coeffs_before[..., 1, None, None] * incoming_moment[None]
    )
    recalled = local_recall + jnp.einsum(
        "chij,cthj->cthi",
        true_before * keep[:, None, None, None],
        span_queries.astype(jnp.float32),
        precision=highest,
    )
    memory_after = jnp.concatenate([memory_before[1:], last_memory[None]], axis=0)
    coeffs_after = jnp.concatenate([coeffs_before[1:], last_coeffs[None]], axis=0)
    true_after = (
        memory_after
        + coeffs_after[..., 0, None, None] * incoming_memory[None]
        + coeffs_after[..., 1, None, None] * incoming_moment[None]
    )
    spread = jnp.sqrt(jnp.mean(true_after * true_after, axis=(2, 3)))
    hit_spans = span_ids[None, :] == (prompt_ends - 1)[:, None]
    state_slots = jnp.sum(jnp.where(hit_spans[:, :, None], spread[None], 0.0), axis=1)
    mixed = (
        (attended + recalled.reshape(block_rows, heads_here, HS))
        .astype(jnp.bfloat16)
        .reshape(block_rows, current_width)
    )
    ff_here = down_weight.shape[0]
    gate_up = up_weight.reshape(D, 2 * ff_here)

    def ffn_hidden(normed_rows):
        gated = jnp.dot(normed_rows, gate_up, preferred_element_type=jnp.float32)
        return (jax.nn.silu(gated[:, :ff_here]) * gated[:, ff_here:]).astype(jnp.bfloat16)

    def ffn_project(piece, start):
        return ffn_hidden(piece)

    def attn_term(start, count):
        return jnp.dot(mixed, out_weight, preferred_element_type=jnp.float32)

    residual = tokens.astype(jnp.float32) + from_owners(attn_term, share_rows)
    hidden = to_owners(rms_scale(residual, norm_gains[1]).astype(jnp.bfloat16), ffn_project)

    def down_term(start, count):
        return jnp.dot(hidden, down_weight, preferred_element_type=jnp.float32)

    second = residual + from_owners(down_term, share_rows)
    final = rms_scale(second, norm_gains[2]).astype(jnp.bfloat16)

    def vocab_maxima(piece, start):
        return jnp.max(jnp.dot(piece, vocab_weight, preferred_element_type=jnp.float32), axis=1)

    row_maxima = to_owners(final, vocab_maxima)
    logit_max = lax.pmax(row_maxima, "head")
    state_rms = lax.psum(state_slots, "seq")
    return (logit_max, state_rms)


def solution(mesh):
    in_specs = (
        P(("seq", "head"), None),
        P(None, None, "head"),
        P("head", None),
        P(None, None, "head"),
        P("head", None),
        P(None, "head"),
        P(None, None, "head"),
        P(),
        P("seq", "head"),
        P("seq", "head"),
        P("seq", "head"),
        P(),
    )
    out_specs = (P("seq"), P(None, "head"))
    return jax.shard_map(local, mesh=mesh, in_specs=in_specs, out_specs=out_specs, check_vma=False)
```

```python
import jax
import jax.numpy as jnp
from jax import lax
from jax.sharding import PartitionSpec as P

D = 1024
HS = 128
NPER = 16
SEG = 1024
CH = 64
SEQS = 4


eps_norm = 1e-05
eps_unit = 1e-06
score_scale = 10.0
masked_score = -1e30


def passed_along(array, axis, by):
    size = lax.axis_size(axis)
    pairs = [(i, i + by) for i in range(size) if 0 <= i + by < size]
    return lax.ppermute(array, axis, pairs)


def carried_in(part, axis, combine, identity):
    place = lax.axis_index(axis)
    gathered = jax.tree.map(lambda a: lax.all_gather(a, axis), part)
    state = jax.tree.map(lambda a, e: jnp.zeros_like(a) + jnp.asarray(e, a.dtype), part, identity)

    def one(step, state):
        return combine(
            state, jax.tree.map(lambda a: lax.dynamic_index_in_dim(a, step, 0, False), gathered)
        )

    return lax.fori_loop(0, place, one, state)


def rms_scale(values, gain):
    return values * lax.rsqrt(jnp.mean(values * values, axis=-1, keepdims=True) + eps_norm) * gain


def unit_rows(values):
    widened = values.astype(jnp.float32)
    return (
        widened * lax.rsqrt(jnp.sum(widened * widened, axis=-1, keepdims=True) + eps_unit)
    ).astype(jnp.bfloat16)


def segment_starts(positions, prompt_spans):
    prompt_ends = jnp.cumsum(prompt_spans)
    first_tokens = (prompt_ends - prompt_spans) * CH
    reached = positions[:, None] >= first_tokens[None, :]
    prompt_first = jnp.max(jnp.where(reached, first_tokens[None, :], 0), axis=1)
    return prompt_first + (positions - prompt_first) // SEG * SEG


def compose(later, earlier):
    return jnp.stack(
        [
            later[..., 0] * earlier[..., 0],
            later[..., 0] * earlier[..., 1] + later[..., 1] * earlier[..., 2],
            later[..., 2] * earlier[..., 2],
        ],
        axis=-1,
    )


def apply_map(coeffs, memory, moment):
    moved_memory = coeffs[:, 0, None, None] * memory + coeffs[:, 1, None, None] * moment
    return (moved_memory, coeffs[:, 2, None, None] * moment)


def chain_combine(earlier, later):
    moved_memory, moved_moment = apply_map(later[0], earlier[1], earlier[2])
    return (compose(later[0], earlier[0]), moved_memory + later[1], moved_moment + later[2])


def to_owners(local_rows, project):
    return project(lax.all_gather(local_rows, "head", axis=0, tiled=True), jnp.int32(0))


def from_owners(term, share_rows):
    return lax.psum_scatter(
        term(jnp.int32(0), share_rows * lax.axis_size("head")),
        "head",
        scatter_dimension=0,
        tiled=True,
    )


def local(
    tokens,
    qkv_weight,
    out_weight,
    up_weight,
    down_weight,
    vocab_weight,
    persistent,
    norm_gains,
    write_rate,
    forget,
    momentum,
    prompt_spans,
):
    share_rows = tokens.shape[0]
    head_count = lax.axis_size("head")
    seq_count = lax.axis_size("seq")
    block_rows = share_rows * head_count
    heads_here = write_rate.shape[1]
    current_width = heads_here * HS
    seq_index = lax.axis_index("seq")
    head_index = lax.axis_index("head")
    qkv_matrix = qkv_weight.reshape(D, 3 * current_width)
    highest = lax.Precision.HIGHEST

    def token_project(piece, start):
        normed = rms_scale(piece.astype(jnp.float32), norm_gains[0]).astype(jnp.bfloat16)
        projected = jnp.dot(normed, qkv_matrix, preferred_element_type=jnp.float32).astype(
            jnp.bfloat16
        )
        return projected

    gathered = to_owners(tokens, token_project)
    out_full = lax.all_gather(
        out_weight + (gathered[0, 0] * 0).astype(out_weight.dtype), "head", axis=0, tiled=True
    )
    projected = gathered
    query_unit = unit_rows(projected[:, :current_width].reshape(block_rows, heads_here, HS))
    key_unit = unit_rows(
        projected[:, current_width : 2 * current_width].reshape(block_rows, heads_here, HS)
    )
    value_rows = projected[:, 2 * current_width :].reshape(block_rows, heads_here, HS)
    reach = SEG // block_rows
    moved_keys, moved_values = passed_along((key_unit, value_rows), "seq", 1)
    earlier_keys = [moved_keys]
    earlier_values = [moved_values]
    all_keys = jnp.concatenate(earlier_keys + [key_unit], axis=0)
    all_values = jnp.concatenate(earlier_values + [value_rows], axis=0)
    first_row = seq_index * block_rows
    query_positions = first_row + jnp.arange(block_rows, dtype=jnp.int32)
    key_positions = (
        first_row - reach * block_rows + jnp.arange((reach + 1) * block_rows, dtype=jnp.int32)
    )
    query_segments = segment_starts(query_positions, prompt_spans)
    key_segments = segment_starts(key_positions, prompt_spans)
    allowed = (
        (key_segments[None, :] == query_segments[:, None])
        & (key_positions[None, :] <= query_positions[:, None])
        & (key_positions[None, :] >= 0)
    )
    persist_keys = persistent[0].reshape(NPER, heads_here, HS)
    persist_values = persistent[1].reshape(NPER, heads_here, HS)
    scores = score_scale * jnp.einsum(
        "qhd,khd->hqk", query_unit, all_keys, preferred_element_type=jnp.float32
    )
    scores = jnp.where(allowed[None], scores, masked_score)
    extra = score_scale * jnp.einsum(
        "qhd,phd->hqp", query_unit, persist_keys, preferred_element_type=jnp.float32
    )
    top = jnp.maximum(jnp.max(scores, axis=-1), jnp.max(extra, axis=-1))[..., None]
    near = jnp.where(allowed[None], jnp.exp(scores - top), 0.0)
    far = jnp.exp(extra - top)
    total = jnp.sum(near, axis=-1, keepdims=True) + jnp.sum(far, axis=-1, keepdims=True)
    near_weights = (near / total).astype(jnp.bfloat16)
    far_weights = (far / total).astype(jnp.bfloat16)
    attended = jnp.einsum(
        "hqk,khd->qhd", near_weights, all_values, preferred_element_type=jnp.float32
    )
    attended = attended + jnp.einsum(
        "hqp,phd->qhd", far_weights, persist_values, preferred_element_type=jnp.float32
    )
    total_spans = block_rows // CH
    span_queries = query_unit.reshape(total_spans, CH, heads_here, HS)
    span_keys = key_unit.reshape(total_spans, CH, heads_here, HS)
    span_values = value_rows.reshape(total_spans, CH, heads_here, HS)
    span_rates = write_rate.reshape(total_spans, CH, heads_here)
    prompt_ends = jnp.cumsum(prompt_spans)
    first_spans = prompt_ends - prompt_spans
    span_ids = seq_index * total_spans + jnp.arange(total_spans, dtype=jnp.int32)
    keep = jnp.where(jnp.any(span_ids[:, None] == first_spans[None, :], axis=1), 0.0, 1.0).astype(
        jnp.float32
    )
    causal = (jnp.arange(CH)[:, None] >= jnp.arange(CH)[None, :]).astype(jnp.float32)
    values_wide = span_values.astype(jnp.float32)
    written = jnp.einsum(
        "cthi,cthj->chij",
        span_rates[..., None] * values_wide,
        span_keys.astype(jnp.float32),
        precision=highest,
    )
    affinity = jnp.einsum(
        "cthd,cshd->chts", span_queries, span_keys, preferred_element_type=jnp.float32
    )
    affinity = affinity * causal[None, None] * jnp.transpose(span_rates, (0, 2, 1))[:, :, None, :]
    local_recall = jnp.einsum("chts,cshi->cthi", affinity, values_wide, precision=highest)
    decay_memory = forget * keep[:, None]
    decay_moment = momentum * keep[:, None]
    identity_coeffs = jnp.tile(jnp.array([1.0, 0.0, 1.0], jnp.float32), (heads_here, 1))
    zero_state = jnp.zeros((heads_here, HS, HS), jnp.float32)

    def advance(carry, inputs):
        coeffs, memory, moment = carry
        current_written, memory_rate, moment_rate = inputs
        step_coeffs = jnp.stack([memory_rate, moment_rate, moment_rate], axis=-1)
        next_moment = moment_rate[:, None, None] * moment + current_written
        next_memory = (
            memory_rate[:, None, None] * memory
            + moment_rate[:, None, None] * moment
            + current_written
        )
        return ((compose(step_coeffs, coeffs), next_memory, next_moment), (coeffs, memory))

    (last_coeffs, last_memory, last_moment), (coeffs_before, memory_before) = lax.scan(
        advance, (identity_coeffs, zero_state, zero_state), (written, decay_memory, decay_moment)
    )
    _, incoming_memory, incoming_moment = carried_in(
        (last_coeffs, last_memory, last_moment),
        "seq",
        chain_combine,
        (identity_coeffs, zero_state, zero_state),
    )
    true_before = (
        memory_before
        + coeffs_before[..., 0, None, None] * incoming_memory[None]
        + coeffs_before[..., 1, None, None] * incoming_moment[None]
    )
    recalled = local_recall + jnp.einsum(
        "chij,cthj->cthi",
        true_before * keep[:, None, None, None],
        span_queries.astype(jnp.float32),
        precision=highest,
    )
    memory_after = jnp.concatenate([memory_before[1:], last_memory[None]], axis=0)
    coeffs_after = jnp.concatenate([coeffs_before[1:], last_coeffs[None]], axis=0)
    true_after = (
        memory_after
        + coeffs_after[..., 0, None, None] * incoming_memory[None]
        + coeffs_after[..., 1, None, None] * incoming_moment[None]
    )
    spread = jnp.sqrt(jnp.mean(true_after * true_after, axis=(2, 3)))
    hit_spans = span_ids[None, :] == (prompt_ends - 1)[:, None]
    state_slots = jnp.sum(jnp.where(hit_spans[:, :, None], spread[None], 0.0), axis=1)
    mixed = (
        (attended + recalled.reshape(block_rows, heads_here, HS))
        .astype(jnp.bfloat16)
        .reshape(block_rows, current_width)
    )
    ff_here = down_weight.shape[0]
    gate_up = up_weight.reshape(D, 2 * ff_here)

    def ffn_hidden(normed_rows):
        gated = jnp.dot(normed_rows, gate_up, preferred_element_type=jnp.float32)
        return (jax.nn.silu(gated[:, :ff_here]) * gated[:, ff_here:]).astype(jnp.bfloat16)

    def ffn_project(piece, start):
        return ffn_hidden(piece)

    pieces = mixed.reshape(head_count, share_rows, current_width)
    swapped = lax.all_to_all(pieces, "head", 0, 0, tiled=False)
    mixed_rows = jnp.transpose(swapped, (1, 0, 2)).reshape(share_rows, head_count * current_width)
    residual = tokens.astype(jnp.float32) + jnp.dot(
        mixed_rows, out_full, preferred_element_type=jnp.float32
    )
    hidden = to_owners(rms_scale(residual, norm_gains[1]).astype(jnp.bfloat16), ffn_project)

    def down_term(start, count):
        return jnp.dot(hidden, down_weight, preferred_element_type=jnp.float32)

    second = residual + from_owners(down_term, share_rows)
    final = rms_scale(second, norm_gains[2]).astype(jnp.bfloat16)

    def vocab_maxima(piece, start):
        return jnp.max(jnp.dot(piece, vocab_weight, preferred_element_type=jnp.float32), axis=1)

    row_maxima = to_owners(final, vocab_maxima)
    logit_max = lax.pmax(row_maxima, "head")
    state_rms = jnp.sum(lax.all_gather(state_slots, "seq"), axis=0)
    return (logit_max, state_rms)


def solution(mesh):
    in_specs = (
        P(("seq", "head"), None),
        P(None, None, "head"),
        P("head", None),
        P(None, None, "head"),
        P("head", None),
        P(None, "head"),
        P(None, None, "head"),
        P(),
        P("seq", "head"),
        P("seq", "head"),
        P("seq", "head"),
        P(),
    )
    out_specs = (P("seq"), P(None, "head"))
    return jax.shard_map(local, mesh=mesh, in_specs=in_specs, out_specs=out_specs, check_vma=False)
```

```python
import jax
import jax.numpy as jnp
from jax import lax
from jax.sharding import PartitionSpec as P

D = 1024
HS = 128
NPER = 16
SEG = 1024
CH = 64
SEQS = 4


eps_norm = 1e-05
eps_unit = 1e-06
score_scale = 10.0
masked_score = -1e30


def passed_along(array, axis, by):
    size = lax.axis_size(axis)
    pairs = [(i, i + by) for i in range(size) if 0 <= i + by < size]
    return lax.ppermute(array, axis, pairs)


def carried_in(part, axis, combine, identity):
    place = lax.axis_index(axis)
    gathered = jax.tree.map(lambda a: lax.all_gather(a, axis), part)
    state = jax.tree.map(lambda a, e: jnp.zeros_like(a) + jnp.asarray(e, a.dtype), part, identity)

    def one(step, state):
        return combine(
            state, jax.tree.map(lambda a: lax.dynamic_index_in_dim(a, step, 0, False), gathered)
        )

    return lax.fori_loop(0, place, one, state)


def rms_scale(values, gain):
    return values * lax.rsqrt(jnp.mean(values * values, axis=-1, keepdims=True) + eps_norm) * gain


def unit_rows(values):
    widened = values.astype(jnp.float32)
    return (
        widened * lax.rsqrt(jnp.sum(widened * widened, axis=-1, keepdims=True) + eps_unit)
    ).astype(jnp.bfloat16)


def segment_starts(positions, prompt_spans):
    prompt_ends = jnp.cumsum(prompt_spans)
    first_tokens = (prompt_ends - prompt_spans) * CH
    reached = positions[:, None] >= first_tokens[None, :]
    prompt_first = jnp.max(jnp.where(reached, first_tokens[None, :], 0), axis=1)
    return prompt_first + (positions - prompt_first) // SEG * SEG


def compose(later, earlier):
    return jnp.stack(
        [
            later[..., 0] * earlier[..., 0],
            later[..., 0] * earlier[..., 1] + later[..., 1] * earlier[..., 2],
            later[..., 2] * earlier[..., 2],
        ],
        axis=-1,
    )


def apply_map(coeffs, memory, moment):
    moved_memory = coeffs[:, 0, None, None] * memory + coeffs[:, 1, None, None] * moment
    return (moved_memory, coeffs[:, 2, None, None] * moment)


def chain_combine(earlier, later):
    moved_memory, moved_moment = apply_map(later[0], earlier[1], earlier[2])
    return (compose(later[0], earlier[0]), moved_memory + later[1], moved_moment + later[2])


def to_owners(local_rows, project):
    return project(lax.all_gather(local_rows, "head", axis=0, tiled=True), jnp.int32(0))


def from_owners(term, share_rows):
    return lax.psum_scatter(
        term(jnp.int32(0), share_rows * lax.axis_size("head")),
        "head",
        scatter_dimension=0,
        tiled=True,
    )


def local(
    tokens,
    qkv_weight,
    out_weight,
    up_weight,
    down_weight,
    vocab_weight,
    persistent,
    norm_gains,
    write_rate,
    forget,
    momentum,
    prompt_spans,
):
    share_rows = tokens.shape[0]
    head_count = lax.axis_size("head")
    seq_count = lax.axis_size("seq")
    block_rows = share_rows * head_count
    heads_here = write_rate.shape[1]
    current_width = heads_here * HS
    seq_index = lax.axis_index("seq")
    head_index = lax.axis_index("head")
    qkv_matrix = qkv_weight.reshape(D, 3 * current_width)
    highest = lax.Precision.HIGHEST

    def token_project(piece, start):
        normed = rms_scale(piece.astype(jnp.float32), norm_gains[0]).astype(jnp.bfloat16)
        projected = jnp.dot(normed, qkv_matrix, preferred_element_type=jnp.float32).astype(
            jnp.bfloat16
        )
        return projected

    gathered = to_owners(tokens, token_project)
    out_full = lax.all_gather(
        out_weight + (gathered[0, 0] * 0).astype(out_weight.dtype), "head", axis=0, tiled=True
    )
    down_full = lax.all_gather(
        down_weight + (gathered[0, 1] * 0).astype(down_weight.dtype), "head", axis=0, tiled=True
    )
    projected = gathered
    query_unit = unit_rows(projected[:, :current_width].reshape(block_rows, heads_here, HS))
    key_unit = unit_rows(
        projected[:, current_width : 2 * current_width].reshape(block_rows, heads_here, HS)
    )
    value_rows = projected[:, 2 * current_width :].reshape(block_rows, heads_here, HS)
    reach = SEG // block_rows
    moved_keys, moved_values = passed_along((key_unit, value_rows), "seq", 1)
    earlier_keys = [moved_keys]
    earlier_values = [moved_values]
    all_keys = jnp.concatenate(earlier_keys + [key_unit], axis=0)
    all_values = jnp.concatenate(earlier_values + [value_rows], axis=0)
    first_row = seq_index * block_rows
    query_positions = first_row + jnp.arange(block_rows, dtype=jnp.int32)
    key_positions = (
        first_row - reach * block_rows + jnp.arange((reach + 1) * block_rows, dtype=jnp.int32)
    )
    query_segments = segment_starts(query_positions, prompt_spans)
    key_segments = segment_starts(key_positions, prompt_spans)
    allowed = (
        (key_segments[None, :] == query_segments[:, None])
        & (key_positions[None, :] <= query_positions[:, None])
        & (key_positions[None, :] >= 0)
    )
    persist_keys = persistent[0].reshape(NPER, heads_here, HS)
    persist_values = persistent[1].reshape(NPER, heads_here, HS)
    scores = score_scale * jnp.einsum(
        "qhd,khd->hqk", query_unit, all_keys, preferred_element_type=jnp.float32
    )
    scores = jnp.where(allowed[None], scores, masked_score)
    extra = score_scale * jnp.einsum(
        "qhd,phd->hqp", query_unit, persist_keys, preferred_element_type=jnp.float32
    )
    top = jnp.maximum(jnp.max(scores, axis=-1), jnp.max(extra, axis=-1))[..., None]
    near = jnp.where(allowed[None], jnp.exp(scores - top), 0.0)
    far = jnp.exp(extra - top)
    total = jnp.sum(near, axis=-1, keepdims=True) + jnp.sum(far, axis=-1, keepdims=True)
    near_weights = (near / total).astype(jnp.bfloat16)
    far_weights = (far / total).astype(jnp.bfloat16)
    attended = jnp.einsum(
        "hqk,khd->qhd", near_weights, all_values, preferred_element_type=jnp.float32
    )
    attended = attended + jnp.einsum(
        "hqp,phd->qhd", far_weights, persist_values, preferred_element_type=jnp.float32
    )
    total_spans = block_rows // CH
    span_queries = query_unit.reshape(total_spans, CH, heads_here, HS)
    span_keys = key_unit.reshape(total_spans, CH, heads_here, HS)
    span_values = value_rows.reshape(total_spans, CH, heads_here, HS)
    span_rates = write_rate.reshape(total_spans, CH, heads_here)
    prompt_ends = jnp.cumsum(prompt_spans)
    first_spans = prompt_ends - prompt_spans
    span_ids = seq_index * total_spans + jnp.arange(total_spans, dtype=jnp.int32)
    keep = jnp.where(jnp.any(span_ids[:, None] == first_spans[None, :], axis=1), 0.0, 1.0).astype(
        jnp.float32
    )
    causal = (jnp.arange(CH)[:, None] >= jnp.arange(CH)[None, :]).astype(jnp.float32)
    values_wide = span_values.astype(jnp.float32)
    written = jnp.einsum(
        "cthi,cthj->chij",
        span_rates[..., None] * values_wide,
        span_keys.astype(jnp.float32),
        precision=highest,
    )
    affinity = jnp.einsum(
        "cthd,cshd->chts", span_queries, span_keys, preferred_element_type=jnp.float32
    )
    affinity = affinity * causal[None, None] * jnp.transpose(span_rates, (0, 2, 1))[:, :, None, :]
    local_recall = jnp.einsum("chts,cshi->cthi", affinity, values_wide, precision=highest)
    decay_memory = forget * keep[:, None]
    decay_moment = momentum * keep[:, None]
    identity_coeffs = jnp.tile(jnp.array([1.0, 0.0, 1.0], jnp.float32), (heads_here, 1))
    zero_state = jnp.zeros((heads_here, HS, HS), jnp.float32)

    def advance(carry, inputs):
        coeffs, memory, moment = carry
        current_written, memory_rate, moment_rate = inputs
        step_coeffs = jnp.stack([memory_rate, moment_rate, moment_rate], axis=-1)
        next_moment = moment_rate[:, None, None] * moment + current_written
        next_memory = (
            memory_rate[:, None, None] * memory
            + moment_rate[:, None, None] * moment
            + current_written
        )
        return ((compose(step_coeffs, coeffs), next_memory, next_moment), (coeffs, memory))

    (last_coeffs, last_memory, last_moment), (coeffs_before, memory_before) = lax.scan(
        advance, (identity_coeffs, zero_state, zero_state), (written, decay_memory, decay_moment)
    )
    _, incoming_memory, incoming_moment = carried_in(
        (last_coeffs, last_memory, last_moment),
        "seq",
        chain_combine,
        (identity_coeffs, zero_state, zero_state),
    )
    true_before = (
        memory_before
        + coeffs_before[..., 0, None, None] * incoming_memory[None]
        + coeffs_before[..., 1, None, None] * incoming_moment[None]
    )
    recalled = local_recall + jnp.einsum(
        "chij,cthj->cthi",
        true_before * keep[:, None, None, None],
        span_queries.astype(jnp.float32),
        precision=highest,
    )
    memory_after = jnp.concatenate([memory_before[1:], last_memory[None]], axis=0)
    coeffs_after = jnp.concatenate([coeffs_before[1:], last_coeffs[None]], axis=0)
    true_after = (
        memory_after
        + coeffs_after[..., 0, None, None] * incoming_memory[None]
        + coeffs_after[..., 1, None, None] * incoming_moment[None]
    )
    spread = jnp.sqrt(jnp.mean(true_after * true_after, axis=(2, 3)))
    hit_spans = span_ids[None, :] == (prompt_ends - 1)[:, None]
    state_slots = jnp.sum(jnp.where(hit_spans[:, :, None], spread[None], 0.0), axis=1)
    mixed = (
        (attended + recalled.reshape(block_rows, heads_here, HS))
        .astype(jnp.bfloat16)
        .reshape(block_rows, current_width)
    )
    ff_here = down_weight.shape[0]
    gate_up = up_weight.reshape(D, 2 * ff_here)

    def ffn_hidden(normed_rows):
        gated = jnp.dot(normed_rows, gate_up, preferred_element_type=jnp.float32)
        return (jax.nn.silu(gated[:, :ff_here]) * gated[:, ff_here:]).astype(jnp.bfloat16)

    def ffn_project(piece, start):
        return ffn_hidden(piece)

    pieces = mixed.reshape(head_count, share_rows, current_width)
    swapped = lax.all_to_all(pieces, "head", 0, 0, tiled=False)
    mixed_rows = jnp.transpose(swapped, (1, 0, 2)).reshape(share_rows, head_count * current_width)
    residual = tokens.astype(jnp.float32) + jnp.dot(
        mixed_rows, out_full, preferred_element_type=jnp.float32
    )
    residual = residual + (down_full[0, 0] * 0).astype(jnp.float32)
    hidden = to_owners(rms_scale(residual, norm_gains[1]).astype(jnp.bfloat16), ffn_project)

    hidden_pieces = hidden.reshape(head_count, share_rows, ff_here)
    hidden_swapped = lax.all_to_all(hidden_pieces, "head", 0, 0, tiled=False)
    hidden_rows = jnp.transpose(hidden_swapped, (1, 0, 2)).reshape(share_rows, head_count * ff_here)
    second = residual + jnp.dot(hidden_rows, down_full, preferred_element_type=jnp.float32)
    final = rms_scale(second, norm_gains[2]).astype(jnp.bfloat16)

    def vocab_maxima(piece, start):
        return jnp.max(jnp.dot(piece, vocab_weight, preferred_element_type=jnp.float32), axis=1)

    row_maxima = to_owners(final, vocab_maxima)
    logit_max = lax.pmax(row_maxima, "head")
    state_rms = jnp.sum(lax.all_gather(state_slots, "seq"), axis=0)
    return (logit_max, state_rms)


def solution(mesh):
    in_specs = (
        P(("seq", "head"), None),
        P(None, None, "head"),
        P("head", None),
        P(None, None, "head"),
        P("head", None),
        P(None, "head"),
        P(None, None, "head"),
        P(),
        P("seq", "head"),
        P("seq", "head"),
        P("seq", "head"),
        P(),
    )
    out_specs = (P("seq"), P(None, "head"))
    return jax.shard_map(local, mesh=mesh, in_specs=in_specs, out_specs=out_specs, check_vma=False)
```

```python
import jax
import jax.numpy as jnp
from jax import lax
from jax.sharding import PartitionSpec as P

D = 1024
HS = 128
NPER = 16
SEG = 1024
CH = 64
SEQS = 4


eps_norm = 1e-05
eps_unit = 1e-06
score_scale = 10.0
masked_score = -1e30


def passed_along(array, axis, by):
    size = lax.axis_size(axis)
    pairs = [(i, i + by) for i in range(size) if 0 <= i + by < size]
    return lax.ppermute(array, axis, pairs)


def carried_in(part, axis, combine, identity):
    place = lax.axis_index(axis)
    gathered = jax.tree.map(lambda a: lax.all_gather(a, axis), part)
    state = jax.tree.map(lambda a, e: jnp.zeros_like(a) + jnp.asarray(e, a.dtype), part, identity)

    def one(step, state):
        return combine(
            state, jax.tree.map(lambda a: lax.dynamic_index_in_dim(a, step, 0, False), gathered)
        )

    return lax.fori_loop(0, place, one, state)


def rms_scale(values, gain):
    return values * lax.rsqrt(jnp.mean(values * values, axis=-1, keepdims=True) + eps_norm) * gain


def unit_rows(values):
    widened = values.astype(jnp.float32)
    return (
        widened * lax.rsqrt(jnp.sum(widened * widened, axis=-1, keepdims=True) + eps_unit)
    ).astype(jnp.bfloat16)


def segment_starts(positions, prompt_spans):
    prompt_ends = jnp.cumsum(prompt_spans)
    first_tokens = (prompt_ends - prompt_spans) * CH
    reached = positions[:, None] >= first_tokens[None, :]
    prompt_first = jnp.max(jnp.where(reached, first_tokens[None, :], 0), axis=1)
    return prompt_first + (positions - prompt_first) // SEG * SEG


def compose(later, earlier):
    return jnp.stack(
        [
            later[..., 0] * earlier[..., 0],
            later[..., 0] * earlier[..., 1] + later[..., 1] * earlier[..., 2],
            later[..., 2] * earlier[..., 2],
        ],
        axis=-1,
    )


def apply_map(coeffs, memory, moment):
    moved_memory = coeffs[:, 0, None, None] * memory + coeffs[:, 1, None, None] * moment
    return (moved_memory, coeffs[:, 2, None, None] * moment)


def chain_combine(earlier, later):
    moved_memory, moved_moment = apply_map(later[0], earlier[1], earlier[2])
    return (compose(later[0], earlier[0]), moved_memory + later[1], moved_moment + later[2])


def to_owners(local_rows, project):
    return project(lax.all_gather(local_rows, "head", axis=0, tiled=True), jnp.int32(0))


def from_owners(term, share_rows):
    return lax.psum_scatter(
        term(jnp.int32(0), share_rows * lax.axis_size("head")),
        "head",
        scatter_dimension=0,
        tiled=True,
    )


def local(
    tokens,
    qkv_weight,
    out_weight,
    up_weight,
    down_weight,
    vocab_weight,
    persistent,
    norm_gains,
    write_rate,
    forget,
    momentum,
    prompt_spans,
):
    share_rows = tokens.shape[0]
    head_count = lax.axis_size("head")
    seq_count = lax.axis_size("seq")
    block_rows = share_rows * head_count
    heads_here = write_rate.shape[1]
    current_width = heads_here * HS
    seq_index = lax.axis_index("seq")
    head_index = lax.axis_index("head")
    qkv_matrix = qkv_weight.reshape(D, 3 * current_width)
    highest = lax.Precision.HIGHEST

    def token_project(piece, start):
        normed = rms_scale(piece.astype(jnp.float32), norm_gains[0]).astype(jnp.bfloat16)
        projected = jnp.dot(normed, qkv_matrix, preferred_element_type=jnp.float32).astype(
            jnp.bfloat16
        )
        return projected

    gathered = to_owners(tokens, token_project)
    out_full = lax.all_gather(
        out_weight + (gathered[0, 0] * 0).astype(out_weight.dtype), "head", axis=0, tiled=True
    )
    projected = gathered
    query_unit = unit_rows(projected[:, :current_width].reshape(block_rows, heads_here, HS))
    key_unit = unit_rows(
        projected[:, current_width : 2 * current_width].reshape(block_rows, heads_here, HS)
    )
    value_rows = projected[:, 2 * current_width :].reshape(block_rows, heads_here, HS)
    reach = SEG // block_rows
    moved_keys, moved_values = passed_along((key_unit, value_rows), "seq", 1)
    earlier_keys = [moved_keys]
    earlier_values = [moved_values]
    all_keys = jnp.concatenate(earlier_keys + [key_unit], axis=0)
    all_values = jnp.concatenate(earlier_values + [value_rows], axis=0)
    first_row = seq_index * block_rows
    query_positions = first_row + jnp.arange(block_rows, dtype=jnp.int32)
    key_positions = (
        first_row - reach * block_rows + jnp.arange((reach + 1) * block_rows, dtype=jnp.int32)
    )
    query_segments = segment_starts(query_positions, prompt_spans)
    key_segments = segment_starts(key_positions, prompt_spans)
    allowed = (
        (key_segments[None, :] == query_segments[:, None])
        & (key_positions[None, :] <= query_positions[:, None])
        & (key_positions[None, :] >= 0)
    )
    persist_keys = persistent[0].reshape(NPER, heads_here, HS)
    persist_values = persistent[1].reshape(NPER, heads_here, HS)
    scores = score_scale * jnp.einsum(
        "qhd,khd->hqk", query_unit, all_keys, preferred_element_type=jnp.float32
    )
    scores = jnp.where(allowed[None], scores, masked_score)
    extra = score_scale * jnp.einsum(
        "qhd,phd->hqp", query_unit, persist_keys, preferred_element_type=jnp.float32
    )
    top = jnp.maximum(jnp.max(scores, axis=-1), jnp.max(extra, axis=-1))[..., None]
    near = jnp.where(allowed[None], jnp.exp(scores - top), 0.0)
    far = jnp.exp(extra - top)
    total = jnp.sum(near, axis=-1, keepdims=True) + jnp.sum(far, axis=-1, keepdims=True)
    near_weights = (near / total).astype(jnp.bfloat16)
    far_weights = (far / total).astype(jnp.bfloat16)
    attended = jnp.einsum(
        "hqk,khd->qhd", near_weights, all_values, preferred_element_type=jnp.float32
    )
    attended = attended + jnp.einsum(
        "hqp,phd->qhd", far_weights, persist_values, preferred_element_type=jnp.float32
    )
    total_spans = block_rows // CH
    span_queries = query_unit.reshape(total_spans, CH, heads_here, HS)
    span_keys = key_unit.reshape(total_spans, CH, heads_here, HS)
    span_values = value_rows.reshape(total_spans, CH, heads_here, HS)
    span_rates = write_rate.reshape(total_spans, CH, heads_here)
    prompt_ends = jnp.cumsum(prompt_spans)
    first_spans = prompt_ends - prompt_spans
    span_ids = seq_index * total_spans + jnp.arange(total_spans, dtype=jnp.int32)
    keep = jnp.where(jnp.any(span_ids[:, None] == first_spans[None, :], axis=1), 0.0, 1.0).astype(
        jnp.float32
    )
    causal = (jnp.arange(CH)[:, None] >= jnp.arange(CH)[None, :]).astype(jnp.float32)
    values_wide = span_values.astype(jnp.float32)
    written = jnp.einsum(
        "cthi,cthj->chij",
        span_rates[..., None] * values_wide,
        span_keys.astype(jnp.float32),
        precision=highest,
    )
    affinity = jnp.einsum(
        "cthd,cshd->chts", span_queries, span_keys, preferred_element_type=jnp.float32
    )
    affinity = affinity * causal[None, None] * jnp.transpose(span_rates, (0, 2, 1))[:, :, None, :]
    local_recall = jnp.einsum("chts,cshi->cthi", affinity, values_wide, precision=highest)
    decay_memory = forget * keep[:, None]
    decay_moment = momentum * keep[:, None]
    span_index = jnp.arange(total_spans)
    inside = (span_index[None, None, :] > span_index[None, :, None]) & (
        span_index[None, None, :] <= span_index[:, None, None]
    )
    lower = span_index[None, :] <= span_index[:, None]

    def range_products(rates):
        picked = jnp.where(inside[..., None], rates[None, None], 1.0)
        return jnp.where(lower[..., None], jnp.prod(picked, axis=2), 0.0)

    memory_span = range_products(decay_memory)
    moment_span = range_products(decay_moment)
    memory_coeffs = jnp.sum(memory_span[:, :, None, :] * moment_span[None, :, :, :], axis=1)
    memory_from_start = jnp.prod(jnp.where(lower[..., None], decay_memory[None], 1.0), axis=1)
    moment_from_start = jnp.prod(jnp.where(lower[..., None], decay_moment[None], 1.0), axis=1)
    memory_from_moment = jnp.sum(memory_span * moment_from_start[None], axis=1)
    coeffs_state = jnp.stack([memory_from_start, memory_from_moment, moment_from_start], axis=-1)
    identity_coeffs = jnp.tile(jnp.array([1.0, 0.0, 1.0], jnp.float32), (heads_here, 1))
    zero_state = jnp.zeros((heads_here, HS, HS), jnp.float32)
    memory_states = jnp.einsum("cjh,jhab->chab", memory_coeffs, written, precision=highest)
    last_moment = jnp.einsum("jh,jhab->hab", moment_span[-1], written, precision=highest)
    last_memory = memory_states[-1]
    last_coeffs = coeffs_state[-1]
    memory_before = jnp.concatenate([zero_state[None], memory_states[:-1]], axis=0)
    coeffs_before = jnp.concatenate([identity_coeffs[None], coeffs_state[:-1]], axis=0)

    coeff_rows = jnp.zeros((heads_here, 8, HS), jnp.float32).at[:, 0, :3].set(last_coeffs)
    packed = jnp.concatenate([last_memory, last_moment, coeff_rows], axis=1)
    every = lax.all_gather(packed, "seq")
    every_memory = every[:, :, :HS]
    every_moment = every[:, :, HS : 2 * HS]
    every_coeffs = every[:, :, 2 * HS, :3]
    block_index = jnp.arange(seq_count)
    between = (block_index[None, None, :] > block_index[None, :, None]) & (
        block_index[None, None, :] < block_index[:, None, None]
    )
    earlier = block_index[None, :] < block_index[:, None]

    def block_products(rates):
        picked = jnp.where(between[..., None], rates[None, None], 1.0)
        return jnp.prod(picked, axis=2)

    keep_memory = block_products(every_coeffs[..., 0])
    keep_moment = block_products(every_coeffs[..., 2])
    at_b = block_index[:, None, None, None]
    at_j = block_index[None, :, None, None]
    at_k = block_index[None, None, :, None]
    at_i = block_index[None, None, None, :]
    later_memory = jnp.prod(
        jnp.where(((at_i > at_k) & (at_i < at_b))[..., None], every_coeffs[None, None, None, :, :, 0], 1.0),
        axis=3,
    )
    earlier_moment = jnp.prod(
        jnp.where(((at_i > at_j) & (at_i < at_k))[..., None], every_coeffs[None, None, None, :, :, 2], 1.0),
        axis=3,
    )
    cross = jnp.sum(
        jnp.where(
            between[..., None],
            later_memory * every_coeffs[None, None, :, :, 1] * earlier_moment,
            0.0,
        ),
        axis=2,
    )
    row_memory = lax.dynamic_index_in_dim(jnp.where(earlier[..., None], keep_memory, 0.0), seq_index, 0, False)
    row_cross = lax.dynamic_index_in_dim(jnp.where(earlier[..., None], cross, 0.0), seq_index, 0, False)
    row_moment = lax.dynamic_index_in_dim(jnp.where(earlier[..., None], keep_moment, 0.0), seq_index, 0, False)
    incoming_memory = jnp.sum(
        row_memory[:, :, None, None] * every_memory + row_cross[:, :, None, None] * every_moment, axis=0
    )
    incoming_moment = jnp.sum(row_moment[:, :, None, None] * every_moment, axis=0)
    true_before = (
        memory_before
        + coeffs_before[..., 0, None, None] * incoming_memory[None]
        + coeffs_before[..., 1, None, None] * incoming_moment[None]
    )
    recalled = local_recall + jnp.einsum(
        "chij,cthj->cthi",
        true_before * keep[:, None, None, None],
        span_queries.astype(jnp.float32),
        precision=highest,
    )
    memory_after = memory_states
    coeffs_after = coeffs_state
    true_after = (
        memory_after
        + coeffs_after[..., 0, None, None] * incoming_memory[None]
        + coeffs_after[..., 1, None, None] * incoming_moment[None]
    )
    spread = jnp.sqrt(jnp.mean(true_after * true_after, axis=(2, 3)))
    hit_spans = span_ids[None, :] == (prompt_ends - 1)[:, None]
    state_slots = jnp.sum(jnp.where(hit_spans[:, :, None], spread[None], 0.0), axis=1)
    mixed = (
        (attended + recalled.reshape(block_rows, heads_here, HS))
        .astype(jnp.bfloat16)
        .reshape(block_rows, current_width)
    )
    ff_here = down_weight.shape[0]
    gate_up = up_weight.reshape(D, 2 * ff_here)

    def ffn_hidden(normed_rows):
        gated = jnp.dot(normed_rows, gate_up, preferred_element_type=jnp.float32)
        return (jax.nn.silu(gated[:, :ff_here]) * gated[:, ff_here:]).astype(jnp.bfloat16)

    def ffn_project(piece, start):
        return ffn_hidden(piece)

    pieces = mixed.reshape(head_count, share_rows, current_width)
    swapped = lax.all_to_all(pieces, "head", 0, 0, tiled=False)
    mixed_rows = jnp.transpose(swapped, (1, 0, 2)).reshape(share_rows, head_count * current_width)
    residual = tokens.astype(jnp.float32) + jnp.dot(
        mixed_rows, out_full, preferred_element_type=jnp.float32
    )
    hidden = to_owners(rms_scale(residual, norm_gains[1]).astype(jnp.bfloat16), ffn_project)

    def down_term(start, count):
        return jnp.dot(hidden, down_weight, preferred_element_type=jnp.float32)

    second = residual + from_owners(down_term, share_rows)
    final = rms_scale(second, norm_gains[2]).astype(jnp.bfloat16)

    def vocab_maxima(piece, start):
        return jnp.max(jnp.dot(piece, vocab_weight, preferred_element_type=jnp.float32), axis=1)

    row_maxima = to_owners(final, vocab_maxima)
    logit_max = lax.pmax(row_maxima, "head")
    state_rms = jnp.sum(lax.all_gather(state_slots, "seq"), axis=0)
    return (logit_max, state_rms)


def solution(mesh):
    in_specs = (
        P(("seq", "head"), None),
        P(None, None, "head"),
        P("head", None),
        P(None, None, "head"),
        P("head", None),
        P(None, "head"),
        P(None, None, "head"),
        P(),
        P("seq", "head"),
        P("seq", "head"),
        P("seq", "head"),
        P(),
    )
    out_specs = (P("seq"), P(None, "head"))
    return jax.shard_map(local, mesh=mesh, in_specs=in_specs, out_specs=out_specs, check_vma=False)
```

```python
import jax
import jax.numpy as jnp
from jax import lax
from jax.sharding import PartitionSpec as P

D = 1024
HS = 128
NPER = 16
SEG = 1024
CH = 64
SEQS = 4


eps_norm = 1e-05
eps_unit = 1e-06
score_scale = 10.0
masked_score = -1e30


def passed_along(array, axis, by):
    size = lax.axis_size(axis)
    pairs = [(i, i + by) for i in range(size) if 0 <= i + by < size]
    return lax.ppermute(array, axis, pairs)


def carried_in(part, axis, combine, identity):
    place = lax.axis_index(axis)
    gathered = jax.tree.map(lambda a: lax.all_gather(a, axis), part)
    state = jax.tree.map(lambda a, e: jnp.zeros_like(a) + jnp.asarray(e, a.dtype), part, identity)

    def one(step, state):
        return combine(
            state, jax.tree.map(lambda a: lax.dynamic_index_in_dim(a, step, 0, False), gathered)
        )

    return lax.fori_loop(0, place, one, state)


def rms_scale(values, gain):
    return values * lax.rsqrt(jnp.mean(values * values, axis=-1, keepdims=True) + eps_norm) * gain


def unit_rows(values):
    widened = values.astype(jnp.float32)
    return (
        widened * lax.rsqrt(jnp.sum(widened * widened, axis=-1, keepdims=True) + eps_unit)
    ).astype(jnp.bfloat16)


def segment_starts(positions, prompt_spans):
    prompt_ends = jnp.cumsum(prompt_spans)
    first_tokens = (prompt_ends - prompt_spans) * CH
    reached = positions[:, None] >= first_tokens[None, :]
    prompt_first = jnp.max(jnp.where(reached, first_tokens[None, :], 0), axis=1)
    return prompt_first + (positions - prompt_first) // SEG * SEG


def compose(later, earlier):
    return jnp.stack(
        [
            later[..., 0] * earlier[..., 0],
            later[..., 0] * earlier[..., 1] + later[..., 1] * earlier[..., 2],
            later[..., 2] * earlier[..., 2],
        ],
        axis=-1,
    )


def apply_map(coeffs, memory, moment):
    moved_memory = coeffs[:, 0, None, None] * memory + coeffs[:, 1, None, None] * moment
    return (moved_memory, coeffs[:, 2, None, None] * moment)


def chain_combine(earlier, later):
    moved_memory, moved_moment = apply_map(later[0], earlier[1], earlier[2])
    return (compose(later[0], earlier[0]), moved_memory + later[1], moved_moment + later[2])


def to_owners(local_rows, project):
    return project(lax.all_gather(local_rows, "head", axis=0, tiled=True), jnp.int32(0))


def from_owners(term, share_rows):
    return lax.psum_scatter(
        term(jnp.int32(0), share_rows * lax.axis_size("head")),
        "head",
        scatter_dimension=0,
        tiled=True,
    )


def local(
    tokens,
    qkv_weight,
    out_weight,
    up_weight,
    down_weight,
    vocab_weight,
    persistent,
    norm_gains,
    write_rate,
    forget,
    momentum,
    prompt_spans,
):
    share_rows = tokens.shape[0]
    head_count = lax.axis_size("head")
    seq_count = lax.axis_size("seq")
    block_rows = share_rows * head_count
    heads_here = write_rate.shape[1]
    current_width = heads_here * HS
    seq_index = lax.axis_index("seq")
    head_index = lax.axis_index("head")
    qkv_blocks = qkv_weight.reshape(D, 3, heads_here, HS)
    highest = lax.Precision.HIGHEST

    def token_project(piece, start):
        normed = rms_scale(piece.astype(jnp.float32), norm_gains[0]).astype(jnp.bfloat16)
        return jnp.einsum(
            "td,dshe->shte", normed, qkv_blocks, preferred_element_type=jnp.float32
        ).astype(jnp.bfloat16)

    projected = to_owners(tokens, token_project)
    out_full = lax.all_gather(
        out_weight + (projected[0, 0, 0, 0] * 0).astype(out_weight.dtype), "head", axis=0, tiled=True
    )
    query_unit = unit_rows(projected[0])
    key_unit = unit_rows(projected[1])
    value_rows = projected[2]
    moved_keys, moved_values = passed_along((key_unit, value_rows), "seq", 1)
    all_keys = jnp.concatenate([moved_keys, key_unit], axis=1)
    all_values = jnp.concatenate([moved_values, value_rows], axis=1)
    first_row = seq_index * block_rows
    query_positions = first_row + jnp.arange(block_rows, dtype=jnp.int32)
    key_positions = first_row - block_rows + jnp.arange(2 * block_rows, dtype=jnp.int32)
    query_segments = segment_starts(query_positions, prompt_spans)
    allowed = (key_positions[None, :] >= query_segments[:, None]) & (
        key_positions[None, :] <= query_positions[:, None]
    )
    persist_keys = persistent[0].reshape(NPER, heads_here, HS)
    persist_values = persistent[1].reshape(NPER, heads_here, HS)
    scores = score_scale * jnp.einsum(
        "hqd,hkd->hqk", query_unit, all_keys, preferred_element_type=jnp.float32
    )
    scores = jnp.where(allowed[None], scores, masked_score)
    extra = score_scale * jnp.einsum(
        "hqd,phd->hqp", query_unit, persist_keys, preferred_element_type=jnp.float32
    )
    top = jnp.maximum(jnp.max(scores, axis=-1), jnp.max(extra, axis=-1))[..., None]
    near = jnp.where(allowed[None], jnp.exp(scores - top), 0.0)
    far = jnp.exp(extra - top)
    total = jnp.sum(near, axis=-1, keepdims=True) + jnp.sum(far, axis=-1, keepdims=True)
    near_weights = (near / total).astype(jnp.bfloat16)
    far_weights = (far / total).astype(jnp.bfloat16)
    attended = jnp.einsum(
        "hqk,hkd->hqd", near_weights, all_values, preferred_element_type=jnp.float32
    )
    attended = attended + jnp.einsum(
        "hqp,phd->hqd", far_weights, persist_values, preferred_element_type=jnp.float32
    )
    total_spans = block_rows // CH
    span_queries = query_unit.reshape(heads_here, total_spans, CH, HS)
    span_keys = key_unit.reshape(heads_here, total_spans, CH, HS)
    span_values = value_rows.reshape(heads_here, total_spans, CH, HS)
    span_rates = jnp.transpose(write_rate).reshape(heads_here, total_spans, CH)
    prompt_ends = jnp.cumsum(prompt_spans)
    first_spans = prompt_ends - prompt_spans
    span_ids = seq_index * total_spans + jnp.arange(total_spans, dtype=jnp.int32)
    keep = jnp.where(jnp.any(span_ids[:, None] == first_spans[None, :], axis=1), 0.0, 1.0).astype(
        jnp.float32
    )
    causal = (jnp.arange(CH)[:, None] >= jnp.arange(CH)[None, :]).astype(jnp.float32)
    values_wide = span_values.astype(jnp.float32)
    written = jnp.einsum(
        "hcti,hctj->hcij",
        span_rates[..., None] * values_wide,
        span_keys.astype(jnp.float32),
        precision=highest,
    )
    affinity = jnp.einsum(
        "hctd,hcsd->hcts", span_queries, span_keys, preferred_element_type=jnp.float32
    )
    affinity = affinity * causal[None, None] * span_rates[:, :, None, :]
    local_recall = jnp.einsum("hcts,hcsi->hcti", affinity, values_wide, precision=highest)
    decay_memory = forget * keep[:, None]
    decay_moment = momentum * keep[:, None]
    span_index = jnp.arange(total_spans)
    inside = (span_index[None, None, :] > span_index[None, :, None]) & (
        span_index[None, None, :] <= span_index[:, None, None]
    )
    lower = span_index[None, :] <= span_index[:, None]

    def range_products(rates):
        picked = jnp.where(inside[..., None], rates[None, None], 1.0)
        return jnp.where(lower[..., None], jnp.prod(picked, axis=2), 0.0)

    memory_span = range_products(decay_memory)
    moment_span = range_products(decay_moment)
    memory_coeffs = jnp.sum(memory_span[:, :, None, :] * moment_span[None, :, :, :], axis=1)
    memory_from_start = jnp.prod(jnp.where(lower[..., None], decay_memory[None], 1.0), axis=1)
    moment_from_start = jnp.prod(jnp.where(lower[..., None], decay_moment[None], 1.0), axis=1)
    memory_from_moment = jnp.sum(memory_span * moment_from_start[None], axis=1)
    coeffs_state = jnp.stack([memory_from_start, memory_from_moment, moment_from_start], axis=-1)
    identity_coeffs = jnp.tile(jnp.array([1.0, 0.0, 1.0], jnp.float32), (heads_here, 1))
    zero_state = jnp.zeros((heads_here, HS, HS), jnp.float32)
    memory_states = jnp.einsum("cjh,hjab->hcab", memory_coeffs, written, precision=highest)
    last_moment = jnp.einsum("jh,hjab->hab", moment_span[-1], written, precision=highest)
    last_memory = memory_states[:, -1]
    last_coeffs = coeffs_state[-1]
    memory_before = jnp.concatenate([zero_state[:, None], memory_states[:, :-1]], axis=1)
    coeffs_before = jnp.transpose(
        jnp.concatenate([identity_coeffs[None], coeffs_state[:-1]], axis=0), (1, 0, 2)
    )

    coeff_rows = jnp.zeros((heads_here, 8, HS), jnp.float32).at[:, 0, :3].set(last_coeffs)
    packed = jnp.concatenate([last_memory, last_moment, coeff_rows], axis=1)
    every = lax.all_gather(packed, "seq")
    every_memory = every[:, :, :HS]
    every_moment = every[:, :, HS : 2 * HS]
    every_coeffs = every[:, :, 2 * HS, :3]
    block_index = jnp.arange(seq_count)
    between = (block_index[None, None, :] > block_index[None, :, None]) & (
        block_index[None, None, :] < block_index[:, None, None]
    )
    earlier = block_index[None, :] < block_index[:, None]

    def block_products(rates):
        picked = jnp.where(between[..., None], rates[None, None], 1.0)
        return jnp.prod(picked, axis=2)

    keep_memory = block_products(every_coeffs[..., 0])
    keep_moment = block_products(every_coeffs[..., 2])
    at_b = block_index[:, None, None, None]
    at_j = block_index[None, :, None, None]
    at_k = block_index[None, None, :, None]
    at_i = block_index[None, None, None, :]
    later_memory = jnp.prod(
        jnp.where(((at_i > at_k) & (at_i < at_b))[..., None], every_coeffs[None, None, None, :, :, 0], 1.0),
        axis=3,
    )
    earlier_moment = jnp.prod(
        jnp.where(((at_i > at_j) & (at_i < at_k))[..., None], every_coeffs[None, None, None, :, :, 2], 1.0),
        axis=3,
    )
    cross = jnp.sum(
        jnp.where(
            between[..., None],
            later_memory * every_coeffs[None, None, :, :, 1] * earlier_moment,
            0.0,
        ),
        axis=2,
    )
    row_memory = lax.dynamic_index_in_dim(jnp.where(earlier[..., None], keep_memory, 0.0), seq_index, 0, False)
    row_cross = lax.dynamic_index_in_dim(jnp.where(earlier[..., None], cross, 0.0), seq_index, 0, False)
    row_moment = lax.dynamic_index_in_dim(jnp.where(earlier[..., None], keep_moment, 0.0), seq_index, 0, False)
    incoming_memory = jnp.sum(
        row_memory[:, :, None, None] * every_memory + row_cross[:, :, None, None] * every_moment, axis=0
    )
    incoming_moment = jnp.sum(row_moment[:, :, None, None] * every_moment, axis=0)
    true_before = (
        memory_before
        + coeffs_before[..., 0, None, None] * incoming_memory[:, None]
        + coeffs_before[..., 1, None, None] * incoming_moment[:, None]
    )
    recalled = local_recall + jnp.einsum(
        "hcij,hctj->hcti",
        true_before * keep[None, :, None, None],
        span_queries.astype(jnp.float32),
        precision=highest,
    )
    memory_after = memory_states
    coeffs_after = jnp.transpose(coeffs_state, (1, 0, 2))
    true_after = (
        memory_after
        + coeffs_after[..., 0, None, None] * incoming_memory[:, None]
        + coeffs_after[..., 1, None, None] * incoming_moment[:, None]
    )
    spread = jnp.sqrt(jnp.mean(true_after * true_after, axis=(2, 3)))
    hit_spans = span_ids[None, :] == (prompt_ends - 1)[:, None]
    state_slots = jnp.sum(jnp.where(hit_spans[:, None, :], spread[None], 0.0), axis=2)
    mixed = (attended + recalled.reshape(heads_here, block_rows, HS)).astype(jnp.bfloat16)
    ff_here = down_weight.shape[0]
    gate_up = up_weight.reshape(D, 2 * ff_here)

    def ffn_hidden(normed_rows):
        gated = jnp.dot(normed_rows, gate_up, preferred_element_type=jnp.float32)
        return (jax.nn.silu(gated[:, :ff_here]) * gated[:, ff_here:]).astype(jnp.bfloat16)

    def ffn_project(piece, start):
        return ffn_hidden(piece)

    pieces = jnp.transpose(mixed.reshape(heads_here, head_count, share_rows, HS), (1, 0, 2, 3))
    swapped = lax.all_to_all(pieces, "head", 0, 0, tiled=False)
    mixed_rows = jnp.transpose(swapped, (2, 0, 1, 3)).reshape(share_rows, head_count * current_width)
    residual = tokens.astype(jnp.float32) + jnp.dot(
        mixed_rows, out_full, preferred_element_type=jnp.float32
    )
    hidden = to_owners(rms_scale(residual, norm_gains[1]).astype(jnp.bfloat16), ffn_project)

    def down_term(start, count):
        return jnp.dot(hidden, down_weight, preferred_element_type=jnp.float32)

    second = residual + from_owners(down_term, share_rows)
    final = rms_scale(second, norm_gains[2]).astype(jnp.bfloat16)

    def vocab_maxima(piece, start):
        return jnp.max(jnp.dot(piece, vocab_weight, preferred_element_type=jnp.float32), axis=1)

    row_maxima = to_owners(final, vocab_maxima)
    logit_max = lax.pmax(row_maxima, "head")
    state_rms = jnp.sum(lax.all_gather(state_slots, "seq"), axis=0)
    return (logit_max, state_rms)


def solution(mesh):
    in_specs = (
        P(("seq", "head"), None),
        P(None, None, "head"),
        P("head", None),
        P(None, None, "head"),
        P("head", None),
        P(None, "head"),
        P(None, None, "head"),
        P(),
        P("seq", "head"),
        P("seq", "head"),
        P("seq", "head"),
        P(),
    )
    out_specs = (P("seq"), P(None, "head"))
    return jax.shard_map(local, mesh=mesh, in_specs=in_specs, out_specs=out_specs, check_vma=False)
```

```python
import jax
import jax.numpy as jnp
from jax import lax
from jax.sharding import PartitionSpec as P

D = 1024
HS = 128
NPER = 16
SEG = 1024
CH = 64
SEQS = 4


eps_norm = 1e-05
eps_unit = 1e-06
score_scale = 10.0
masked_score = -1e30


def passed_along(array, axis, by):
    size = lax.axis_size(axis)
    pairs = [(i, i + by) for i in range(size) if 0 <= i + by < size]
    return lax.ppermute(array, axis, pairs)


def carried_in(part, axis, combine, identity):
    place = lax.axis_index(axis)
    gathered = jax.tree.map(lambda a: lax.all_gather(a, axis), part)
    state = jax.tree.map(lambda a, e: jnp.zeros_like(a) + jnp.asarray(e, a.dtype), part, identity)

    def one(step, state):
        return combine(
            state, jax.tree.map(lambda a: lax.dynamic_index_in_dim(a, step, 0, False), gathered)
        )

    return lax.fori_loop(0, place, one, state)


def rms_scale(values, gain):
    return values * lax.rsqrt(jnp.mean(values * values, axis=-1, keepdims=True) + eps_norm) * gain


def unit_rows(values):
    widened = values.astype(jnp.float32)
    return (
        widened * lax.rsqrt(jnp.sum(widened * widened, axis=-1, keepdims=True) + eps_unit)
    ).astype(jnp.bfloat16)


def segment_starts(positions, prompt_spans):
    prompt_ends = jnp.cumsum(prompt_spans)
    first_tokens = (prompt_ends - prompt_spans) * CH
    reached = positions[:, None] >= first_tokens[None, :]
    prompt_first = jnp.max(jnp.where(reached, first_tokens[None, :], 0), axis=1)
    return prompt_first + (positions - prompt_first) // SEG * SEG


def compose(later, earlier):
    return jnp.stack(
        [
            later[..., 0] * earlier[..., 0],
            later[..., 0] * earlier[..., 1] + later[..., 1] * earlier[..., 2],
            later[..., 2] * earlier[..., 2],
        ],
        axis=-1,
    )


def apply_map(coeffs, memory, moment):
    moved_memory = coeffs[:, 0, None, None] * memory + coeffs[:, 1, None, None] * moment
    return (moved_memory, coeffs[:, 2, None, None] * moment)


def chain_combine(earlier, later):
    moved_memory, moved_moment = apply_map(later[0], earlier[1], earlier[2])
    return (compose(later[0], earlier[0]), moved_memory + later[1], moved_moment + later[2])


def to_owners(local_rows, project):
    return project(lax.all_gather(local_rows, "head", axis=0, tiled=True), jnp.int32(0))


def from_owners(term, share_rows):
    return lax.psum_scatter(
        term(jnp.int32(0), share_rows * lax.axis_size("head")),
        "head",
        scatter_dimension=0,
        tiled=True,
    )


def local(
    tokens,
    qkv_weight,
    out_weight,
    up_weight,
    down_weight,
    vocab_weight,
    persistent,
    norm_gains,
    write_rate,
    forget,
    momentum,
    prompt_spans,
):
    share_rows = tokens.shape[0]
    head_count = lax.axis_size("head")
    seq_count = lax.axis_size("seq")
    block_rows = share_rows * head_count
    heads_here = write_rate.shape[1]
    current_width = heads_here * HS
    seq_index = lax.axis_index("seq")
    head_index = lax.axis_index("head")
    qkv_blocks = qkv_weight.reshape(D, 3, heads_here, HS)
    highest = lax.Precision.HIGHEST

    def token_project(piece, start):
        normed = rms_scale(piece.astype(jnp.float32), norm_gains[0]).astype(jnp.bfloat16)
        return jnp.einsum(
            "td,dshe->shte", normed, qkv_blocks, preferred_element_type=jnp.float32
        ).astype(jnp.bfloat16)

    gathered_tokens = lax.all_gather(tokens, "head", axis=0, tiled=True)
    out_full = lax.all_gather(
        out_weight + (gathered_tokens[0, 0] * 0).astype(out_weight.dtype), "head", axis=0, tiled=True
    )
    projected = token_project(gathered_tokens, 0)
    query_unit = unit_rows(projected[0])
    key_unit = unit_rows(projected[1])
    value_rows = projected[2]
    moved_keys, moved_values = passed_along((key_unit, value_rows), "seq", 1)
    all_keys = jnp.concatenate([moved_keys, key_unit], axis=1)
    all_values = jnp.concatenate([moved_values, value_rows], axis=1)
    first_row = seq_index * block_rows
    query_positions = first_row + jnp.arange(block_rows, dtype=jnp.int32)
    key_positions = first_row - block_rows + jnp.arange(2 * block_rows, dtype=jnp.int32)
    query_segments = segment_starts(query_positions, prompt_spans)
    allowed = (key_positions[None, :] >= query_segments[:, None]) & (
        key_positions[None, :] <= query_positions[:, None]
    )
    persist_keys = persistent[0].reshape(NPER, heads_here, HS)
    persist_values = persistent[1].reshape(NPER, heads_here, HS)
    scores = score_scale * jnp.einsum(
        "hqd,hkd->hqk", query_unit, all_keys, preferred_element_type=jnp.float32
    )
    scores = jnp.where(allowed[None], scores, masked_score)
    extra = score_scale * jnp.einsum(
        "hqd,phd->hqp", query_unit, persist_keys, preferred_element_type=jnp.float32
    )
    top = jnp.maximum(jnp.max(scores, axis=-1), jnp.max(extra, axis=-1))[..., None]
    near = jnp.where(allowed[None], jnp.exp(scores - top), 0.0)
    far = jnp.exp(extra - top)
    total = jnp.sum(near, axis=-1, keepdims=True) + jnp.sum(far, axis=-1, keepdims=True)
    near_weights = (near / total).astype(jnp.bfloat16)
    far_weights = (far / total).astype(jnp.bfloat16)
    attended = jnp.einsum(
        "hqk,hkd->hqd", near_weights, all_values, preferred_element_type=jnp.float32
    )
    attended = attended + jnp.einsum(
        "hqp,phd->hqd", far_weights, persist_values, preferred_element_type=jnp.float32
    )
    total_spans = block_rows // CH
    span_queries = query_unit.reshape(heads_here, total_spans, CH, HS)
    span_keys = key_unit.reshape(heads_here, total_spans, CH, HS)
    span_values = value_rows.reshape(heads_here, total_spans, CH, HS)
    span_rates = jnp.transpose(write_rate).reshape(heads_here, total_spans, CH)
    prompt_ends = jnp.cumsum(prompt_spans)
    first_spans = prompt_ends - prompt_spans
    span_ids = seq_index * total_spans + jnp.arange(total_spans, dtype=jnp.int32)
    keep = jnp.where(jnp.any(span_ids[:, None] == first_spans[None, :], axis=1), 0.0, 1.0).astype(
        jnp.float32
    )
    causal = (jnp.arange(CH)[:, None] >= jnp.arange(CH)[None, :]).astype(jnp.float32)
    values_wide = span_values.astype(jnp.float32)
    written = jnp.einsum(
        "hcti,hctj->hcij",
        span_rates[..., None] * values_wide,
        span_keys.astype(jnp.float32),
        precision=highest,
    )
    affinity = jnp.einsum(
        "hctd,hcsd->hcts", span_queries, span_keys, preferred_element_type=jnp.float32
    )
    affinity = affinity * causal[None, None] * span_rates[:, :, None, :]
    local_recall = jnp.einsum("hcts,hcsi->hcti", affinity, values_wide, precision=highest)
    decay_memory = forget * keep[:, None]
    decay_moment = momentum * keep[:, None]
    span_index = jnp.arange(total_spans)
    inside = (span_index[None, None, :] > span_index[None, :, None]) & (
        span_index[None, None, :] <= span_index[:, None, None]
    )
    lower = span_index[None, :] <= span_index[:, None]

    def range_products(rates):
        picked = jnp.where(inside[..., None], rates[None, None], 1.0)
        return jnp.where(lower[..., None], jnp.prod(picked, axis=2), 0.0)

    memory_span = range_products(decay_memory)
    moment_span = range_products(decay_moment)
    memory_coeffs = jnp.sum(memory_span[:, :, None, :] * moment_span[None, :, :, :], axis=1)
    memory_from_start = jnp.prod(jnp.where(lower[..., None], decay_memory[None], 1.0), axis=1)
    moment_from_start = jnp.prod(jnp.where(lower[..., None], decay_moment[None], 1.0), axis=1)
    memory_from_moment = jnp.sum(memory_span * moment_from_start[None], axis=1)
    coeffs_state = jnp.stack([memory_from_start, memory_from_moment, moment_from_start], axis=-1)
    identity_coeffs = jnp.tile(jnp.array([1.0, 0.0, 1.0], jnp.float32), (heads_here, 1))
    zero_state = jnp.zeros((heads_here, HS, HS), jnp.float32)
    memory_states = jnp.einsum("cjh,hjab->hcab", memory_coeffs, written, precision=highest)
    last_moment = jnp.einsum("jh,hjab->hab", moment_span[-1], written, precision=highest)
    last_memory = memory_states[:, -1]
    last_coeffs = coeffs_state[-1]
    memory_before = jnp.concatenate([zero_state[:, None], memory_states[:, :-1]], axis=1)
    coeffs_before = jnp.transpose(
        jnp.concatenate([identity_coeffs[None], coeffs_state[:-1]], axis=0), (1, 0, 2)
    )

    coeff_rows = jnp.zeros((heads_here, 8, HS), jnp.float32).at[:, 0, :3].set(last_coeffs)
    packed = jnp.concatenate([last_memory, last_moment, coeff_rows], axis=1)
    packed = packed + (out_full[0, 0] * 0).astype(jnp.float32)
    every = lax.all_gather(packed, "seq")
    every_memory = every[:, :, :HS]
    every_moment = every[:, :, HS : 2 * HS]
    every_coeffs = every[:, :, 2 * HS, :3]
    block_index = jnp.arange(seq_count)
    between = (block_index[None, None, :] > block_index[None, :, None]) & (
        block_index[None, None, :] < block_index[:, None, None]
    )
    earlier = block_index[None, :] < block_index[:, None]

    def block_products(rates):
        picked = jnp.where(between[..., None], rates[None, None], 1.0)
        return jnp.prod(picked, axis=2)

    keep_memory = block_products(every_coeffs[..., 0])
    keep_moment = block_products(every_coeffs[..., 2])
    at_b = block_index[:, None, None, None]
    at_j = block_index[None, :, None, None]
    at_k = block_index[None, None, :, None]
    at_i = block_index[None, None, None, :]
    later_memory = jnp.prod(
        jnp.where(((at_i > at_k) & (at_i < at_b))[..., None], every_coeffs[None, None, None, :, :, 0], 1.0),
        axis=3,
    )
    earlier_moment = jnp.prod(
        jnp.where(((at_i > at_j) & (at_i < at_k))[..., None], every_coeffs[None, None, None, :, :, 2], 1.0),
        axis=3,
    )
    cross = jnp.sum(
        jnp.where(
            between[..., None],
            later_memory * every_coeffs[None, None, :, :, 1] * earlier_moment,
            0.0,
        ),
        axis=2,
    )
    row_memory = lax.dynamic_index_in_dim(jnp.where(earlier[..., None], keep_memory, 0.0), seq_index, 0, False)
    row_cross = lax.dynamic_index_in_dim(jnp.where(earlier[..., None], cross, 0.0), seq_index, 0, False)
    row_moment = lax.dynamic_index_in_dim(jnp.where(earlier[..., None], keep_moment, 0.0), seq_index, 0, False)
    incoming_memory = jnp.sum(
        row_memory[:, :, None, None] * every_memory + row_cross[:, :, None, None] * every_moment, axis=0
    )
    incoming_moment = jnp.sum(row_moment[:, :, None, None] * every_moment, axis=0)
    true_before = (
        memory_before
        + coeffs_before[..., 0, None, None] * incoming_memory[:, None]
        + coeffs_before[..., 1, None, None] * incoming_moment[:, None]
    )
    recalled = local_recall + jnp.einsum(
        "hcij,hctj->hcti",
        true_before * keep[None, :, None, None],
        span_queries.astype(jnp.float32),
        precision=highest,
    )
    memory_after = memory_states
    coeffs_after = jnp.transpose(coeffs_state, (1, 0, 2))
    true_after = (
        memory_after
        + coeffs_after[..., 0, None, None] * incoming_memory[:, None]
        + coeffs_after[..., 1, None, None] * incoming_moment[:, None]
    )
    spread = jnp.sqrt(jnp.mean(true_after * true_after, axis=(2, 3)))
    hit_spans = span_ids[None, :] == (prompt_ends - 1)[:, None]
    state_slots = jnp.sum(jnp.where(hit_spans[:, None, :], spread[None], 0.0), axis=2)
    mixed = (attended + recalled.reshape(heads_here, block_rows, HS)).astype(jnp.bfloat16)
    ff_here = down_weight.shape[0]
    gate_up = up_weight.reshape(D, 2 * ff_here)

    def ffn_hidden(normed_rows):
        gated = jnp.dot(normed_rows, gate_up, preferred_element_type=jnp.float32)
        return (jax.nn.silu(gated[:, :ff_here]) * gated[:, ff_here:]).astype(jnp.bfloat16)

    def ffn_project(piece, start):
        return ffn_hidden(piece)

    pieces = jnp.transpose(mixed.reshape(heads_here, head_count, share_rows, HS), (1, 0, 2, 3))
    swapped = lax.all_to_all(pieces, "head", 0, 0, tiled=False)
    mixed_rows = jnp.transpose(swapped, (2, 0, 1, 3)).reshape(share_rows, head_count * current_width)
    residual = tokens.astype(jnp.float32) + jnp.dot(
        mixed_rows, out_full, preferred_element_type=jnp.float32
    )
    hidden = to_owners(rms_scale(residual, norm_gains[1]).astype(jnp.bfloat16), ffn_project)

    def down_term(start, count):
        return jnp.dot(hidden, down_weight, preferred_element_type=jnp.float32)

    second = residual + from_owners(down_term, share_rows)
    final = rms_scale(second, norm_gains[2]).astype(jnp.bfloat16)

    def vocab_maxima(piece, start):
        return jnp.max(jnp.dot(piece, vocab_weight, preferred_element_type=jnp.float32), axis=1)

    row_maxima = to_owners(final, vocab_maxima)
    logit_max = lax.pmax(row_maxima, "head")
    state_rms = jnp.sum(lax.all_gather(state_slots, "seq"), axis=0)
    return (logit_max, state_rms)


def solution(mesh):
    in_specs = (
        P(("seq", "head"), None),
        P(None, None, "head"),
        P("head", None),
        P(None, None, "head"),
        P("head", None),
        P(None, "head"),
        P(None, None, "head"),
        P(),
        P("seq", "head"),
        P("seq", "head"),
        P("seq", "head"),
        P(),
    )
    out_specs = (P("seq"), P(None, "head"))
    return jax.shard_map(local, mesh=mesh, in_specs=in_specs, out_specs=out_specs, check_vma=False)
```

```python
import jax
import jax.numpy as jnp
from jax import lax
from jax.sharding import PartitionSpec as P

D = 1024
HS = 128
NPER = 16
SEG = 1024
CH = 64
SEQS = 4


eps_norm = 1e-05
eps_unit = 1e-06
score_scale = 10.0
masked_score = -1e30


def passed_along(array, axis, by):
    size = lax.axis_size(axis)
    pairs = [(i, i + by) for i in range(size) if 0 <= i + by < size]
    return lax.ppermute(array, axis, pairs)


def carried_in(part, axis, combine, identity):
    place = lax.axis_index(axis)
    gathered = jax.tree.map(lambda a: lax.all_gather(a, axis), part)
    state = jax.tree.map(lambda a, e: jnp.zeros_like(a) + jnp.asarray(e, a.dtype), part, identity)

    def one(step, state):
        return combine(
            state, jax.tree.map(lambda a: lax.dynamic_index_in_dim(a, step, 0, False), gathered)
        )

    return lax.fori_loop(0, place, one, state)


def rms_scale(values, gain):
    return values * lax.rsqrt(jnp.mean(values * values, axis=-1, keepdims=True) + eps_norm) * gain


def unit_rows(values):
    widened = values.astype(jnp.float32)
    return (
        widened * lax.rsqrt(jnp.sum(widened * widened, axis=-1, keepdims=True) + eps_unit)
    ).astype(jnp.bfloat16)


def segment_starts(positions, prompt_spans):
    prompt_ends = jnp.cumsum(prompt_spans)
    first_tokens = (prompt_ends - prompt_spans) * CH
    reached = positions[:, None] >= first_tokens[None, :]
    prompt_first = jnp.max(jnp.where(reached, first_tokens[None, :], 0), axis=1)
    return prompt_first + (positions - prompt_first) // SEG * SEG


def compose(later, earlier):
    return jnp.stack(
        [
            later[..., 0] * earlier[..., 0],
            later[..., 0] * earlier[..., 1] + later[..., 1] * earlier[..., 2],
            later[..., 2] * earlier[..., 2],
        ],
        axis=-1,
    )


def apply_map(coeffs, memory, moment):
    moved_memory = coeffs[:, 0, None, None] * memory + coeffs[:, 1, None, None] * moment
    return (moved_memory, coeffs[:, 2, None, None] * moment)


def chain_combine(earlier, later):
    moved_memory, moved_moment = apply_map(later[0], earlier[1], earlier[2])
    return (compose(later[0], earlier[0]), moved_memory + later[1], moved_moment + later[2])


def to_owners(local_rows, project):
    return project(lax.all_gather(local_rows, "head", axis=0, tiled=True), jnp.int32(0))


def from_owners(term, share_rows):
    return lax.psum_scatter(
        term(jnp.int32(0), share_rows * lax.axis_size("head")),
        "head",
        scatter_dimension=0,
        tiled=True,
    )


def local(
    tokens,
    qkv_weight,
    out_weight,
    up_weight,
    down_weight,
    vocab_weight,
    persistent,
    norm_gains,
    write_rate,
    forget,
    momentum,
    prompt_spans,
):
    share_rows = tokens.shape[0]
    head_count = lax.axis_size("head")
    seq_count = lax.axis_size("seq")
    block_rows = share_rows * head_count
    heads_here = write_rate.shape[1]
    current_width = heads_here * HS
    seq_index = lax.axis_index("seq")
    head_index = lax.axis_index("head")
    qkv_blocks = qkv_weight.reshape(D, 3, heads_here, HS)
    highest = lax.Precision.HIGHEST

    def token_project(piece, start):
        normed = rms_scale(piece.astype(jnp.float32), norm_gains[0]).astype(jnp.bfloat16)
        return jnp.einsum(
            "td,dshe->shte", normed, qkv_blocks, preferred_element_type=jnp.float32
        ).astype(jnp.bfloat16)

    projected = to_owners(tokens, token_project)
    out_full = lax.all_gather(
        out_weight + (projected[0, 0, 0, 0] * 0).astype(out_weight.dtype), "head", axis=0, tiled=True
    )
    query_unit = unit_rows(projected[0])
    key_unit = unit_rows(projected[1])
    value_rows = projected[2]
    moved_keys, moved_values = passed_along((key_unit, value_rows), "seq", 1)
    all_keys = jnp.concatenate([moved_keys, key_unit], axis=1)
    all_values = jnp.concatenate([moved_values, value_rows], axis=1)
    first_row = seq_index * block_rows
    query_positions = first_row + jnp.arange(block_rows, dtype=jnp.int32)
    key_positions = first_row - block_rows + jnp.arange(2 * block_rows, dtype=jnp.int32)
    query_segments = segment_starts(query_positions, prompt_spans)
    allowed = (key_positions[None, :] >= query_segments[:, None]) & (
        key_positions[None, :] <= query_positions[:, None]
    )
    persist_keys = persistent[0].reshape(NPER, heads_here, HS)
    persist_values = persistent[1].reshape(NPER, heads_here, HS)
    scores = score_scale * jnp.einsum(
        "hqd,hkd->hqk", query_unit, all_keys, preferred_element_type=jnp.float32
    )
    scores = jnp.where(allowed[None], scores, masked_score)
    extra = score_scale * jnp.einsum(
        "hqd,phd->hqp", query_unit, persist_keys, preferred_element_type=jnp.float32
    )
    top = jnp.maximum(jnp.max(scores, axis=-1), jnp.max(extra, axis=-1))[..., None]
    near = jnp.where(allowed[None], jnp.exp(scores - top), 0.0)
    far = jnp.exp(extra - top)
    total = jnp.sum(near, axis=-1, keepdims=True) + jnp.sum(far, axis=-1, keepdims=True)
    near_weights = (near / total).astype(jnp.bfloat16)
    far_weights = (far / total).astype(jnp.bfloat16)
    attended = jnp.einsum(
        "hqk,hkd->hqd", near_weights, all_values, preferred_element_type=jnp.float32
    )
    attended = attended + jnp.einsum(
        "hqp,phd->hqd", far_weights, persist_values, preferred_element_type=jnp.float32
    )
    total_spans = block_rows // CH
    span_queries = query_unit.reshape(heads_here, total_spans, CH, HS)
    span_keys = key_unit.reshape(heads_here, total_spans, CH, HS)
    span_values = value_rows.reshape(heads_here, total_spans, CH, HS)
    span_rates = jnp.transpose(write_rate).reshape(heads_here, total_spans, CH)
    prompt_ends = jnp.cumsum(prompt_spans)
    first_spans = prompt_ends - prompt_spans
    span_ids = seq_index * total_spans + jnp.arange(total_spans, dtype=jnp.int32)
    keep = jnp.where(jnp.any(span_ids[:, None] == first_spans[None, :], axis=1), 0.0, 1.0).astype(
        jnp.float32
    )
    causal = (jnp.arange(CH)[:, None] >= jnp.arange(CH)[None, :]).astype(jnp.float32)
    values_wide = span_values.astype(jnp.float32)
    written = jnp.einsum(
        "hcti,hctj->hcij",
        span_rates[..., None] * values_wide,
        span_keys.astype(jnp.float32),
        precision=highest,
    )
    affinity = jnp.einsum(
        "hctd,hcsd->hcts", span_queries, span_keys, preferred_element_type=jnp.float32
    )
    affinity = affinity * causal[None, None] * span_rates[:, :, None, :]
    local_recall = jnp.einsum("hcts,hcsi->hcti", affinity, values_wide, precision=highest)
    decay_memory = forget * keep[:, None]
    decay_moment = momentum * keep[:, None]
    span_index = jnp.arange(total_spans)
    inside = (span_index[None, None, :] > span_index[None, :, None]) & (
        span_index[None, None, :] <= span_index[:, None, None]
    )
    lower = span_index[None, :] <= span_index[:, None]

    def range_products(rates):
        picked = jnp.where(inside[..., None], rates[None, None], 1.0)
        return jnp.where(lower[..., None], jnp.prod(picked, axis=2), 0.0)

    memory_span = range_products(decay_memory)
    moment_span = range_products(decay_moment)
    memory_coeffs = jnp.sum(memory_span[:, :, None, :] * moment_span[None, :, :, :], axis=1)
    memory_from_start = jnp.prod(jnp.where(lower[..., None], decay_memory[None], 1.0), axis=1)
    moment_from_start = jnp.prod(jnp.where(lower[..., None], decay_moment[None], 1.0), axis=1)
    memory_from_moment = jnp.sum(memory_span * moment_from_start[None], axis=1)
    coeffs_state = jnp.stack([memory_from_start, memory_from_moment, moment_from_start], axis=-1)
    identity_coeffs = jnp.tile(jnp.array([1.0, 0.0, 1.0], jnp.float32), (heads_here, 1))
    zero_state = jnp.zeros((heads_here, HS, HS), jnp.float32)
    memory_states = jnp.einsum("cjh,hjab->hcab", memory_coeffs, written, precision=highest)
    last_moment = jnp.einsum("jh,hjab->hab", moment_span[-1], written, precision=highest)
    last_memory = memory_states[:, -1]
    last_coeffs = coeffs_state[-1]
    memory_before = jnp.concatenate([zero_state[:, None], memory_states[:, :-1]], axis=1)
    coeffs_before = jnp.transpose(
        jnp.concatenate([identity_coeffs[None], coeffs_state[:-1]], axis=0), (1, 0, 2)
    )

    def pack(state):
        coeff_rows = jnp.zeros((heads_here, 8, HS), jnp.float32).at[:, 0, :3].set(state[0])
        return jnp.concatenate([state[1], state[2], coeff_rows], axis=1)

    def unpack(packed):
        return (packed[:, 2 * HS, :3], packed[:, :HS], packed[:, HS : 2 * HS])

    identity_state = (identity_coeffs, zero_state, zero_state)
    identity_packed = pack(identity_state)

    def moved_by(packed, distance):
        moved = passed_along(packed, "seq", distance)
        return jnp.where(seq_index >= distance, moved, identity_packed)

    prefix = moved_by(pack((last_coeffs, last_memory, last_moment)), 1)
    distance = 1
    while distance < seq_count:
        prefix = pack(chain_combine(unpack(moved_by(prefix, distance)), unpack(prefix)))
        distance *= 2
    _, incoming_memory, incoming_moment = unpack(prefix)
    true_before = (
        memory_before
        + coeffs_before[..., 0, None, None] * incoming_memory[:, None]
        + coeffs_before[..., 1, None, None] * incoming_moment[:, None]
    )
    recalled = local_recall + jnp.einsum(
        "hcij,hctj->hcti",
        true_before * keep[None, :, None, None],
        span_queries.astype(jnp.float32),
        precision=highest,
    )
    memory_after = memory_states
    coeffs_after = jnp.transpose(coeffs_state, (1, 0, 2))
    true_after = (
        memory_after
        + coeffs_after[..., 0, None, None] * incoming_memory[:, None]
        + coeffs_after[..., 1, None, None] * incoming_moment[:, None]
    )
    spread = jnp.sqrt(jnp.mean(true_after * true_after, axis=(2, 3)))
    hit_spans = span_ids[None, :] == (prompt_ends - 1)[:, None]
    state_slots = jnp.sum(jnp.where(hit_spans[:, None, :], spread[None], 0.0), axis=2)
    mixed = (attended + recalled.reshape(heads_here, block_rows, HS)).astype(jnp.bfloat16)
    ff_here = down_weight.shape[0]
    gate_up = up_weight.reshape(D, 2 * ff_here)

    def ffn_hidden(normed_rows):
        gated = jnp.dot(normed_rows, gate_up, preferred_element_type=jnp.float32)
        return (jax.nn.silu(gated[:, :ff_here]) * gated[:, ff_here:]).astype(jnp.bfloat16)

    def ffn_project(piece, start):
        return ffn_hidden(piece)

    pieces = jnp.transpose(mixed.reshape(heads_here, head_count, share_rows, HS), (1, 0, 2, 3))
    swapped = lax.all_to_all(pieces, "head", 0, 0, tiled=False)
    mixed_rows = jnp.transpose(swapped, (2, 0, 1, 3)).reshape(share_rows, head_count * current_width)
    residual = tokens.astype(jnp.float32) + jnp.dot(
        mixed_rows, out_full, preferred_element_type=jnp.float32
    )
    hidden = to_owners(rms_scale(residual, norm_gains[1]).astype(jnp.bfloat16), ffn_project)

    def down_term(start, count):
        return jnp.dot(hidden, down_weight, preferred_element_type=jnp.float32)

    second = residual + from_owners(down_term, share_rows)
    final = rms_scale(second, norm_gains[2]).astype(jnp.bfloat16)

    def vocab_maxima(piece, start):
        return jnp.max(jnp.dot(piece, vocab_weight, preferred_element_type=jnp.float32), axis=1)

    row_maxima = to_owners(final, vocab_maxima)
    logit_max = lax.pmax(row_maxima, "head")
    state_rms = jnp.sum(lax.all_gather(state_slots, "seq"), axis=0)
    return (logit_max, state_rms)


def solution(mesh):
    in_specs = (
        P(("seq", "head"), None),
        P(None, None, "head"),
        P("head", None),
        P(None, None, "head"),
        P("head", None),
        P(None, "head"),
        P(None, None, "head"),
        P(),
        P("seq", "head"),
        P("seq", "head"),
        P("seq", "head"),
        P(),
    )
    out_specs = (P("seq"), P(None, "head"))
    return jax.shard_map(local, mesh=mesh, in_specs=in_specs, out_specs=out_specs, check_vma=False)
```

```python
import jax
import jax.numpy as jnp
from jax import lax
from jax.sharding import PartitionSpec as P

D = 1024
HS = 128
NPER = 16
SEG = 1024
CH = 64
SEQS = 4


eps_norm = 1e-05
eps_unit = 1e-06
score_scale = 10.0
masked_score = -1e30


def passed_along(array, axis, by):
    size = lax.axis_size(axis)
    pairs = [(i, i + by) for i in range(size) if 0 <= i + by < size]
    return lax.ppermute(array, axis, pairs)


def carried_in(part, axis, combine, identity):
    place = lax.axis_index(axis)
    gathered = jax.tree.map(lambda a: lax.all_gather(a, axis), part)
    state = jax.tree.map(lambda a, e: jnp.zeros_like(a) + jnp.asarray(e, a.dtype), part, identity)

    def one(step, state):
        return combine(
            state, jax.tree.map(lambda a: lax.dynamic_index_in_dim(a, step, 0, False), gathered)
        )

    return lax.fori_loop(0, place, one, state)


def rms_scale(values, gain):
    return values * lax.rsqrt(jnp.mean(values * values, axis=-1, keepdims=True) + eps_norm) * gain


def unit_rows(values):
    widened = values.astype(jnp.float32)
    return (
        widened * lax.rsqrt(jnp.sum(widened * widened, axis=-1, keepdims=True) + eps_unit)
    ).astype(jnp.bfloat16)


def segment_starts(positions, prompt_spans):
    prompt_ends = jnp.cumsum(prompt_spans)
    first_tokens = (prompt_ends - prompt_spans) * CH
    reached = positions[:, None] >= first_tokens[None, :]
    prompt_first = jnp.max(jnp.where(reached, first_tokens[None, :], 0), axis=1)
    return prompt_first + (positions - prompt_first) // SEG * SEG


def compose(later, earlier):
    return jnp.stack(
        [
            later[..., 0] * earlier[..., 0],
            later[..., 0] * earlier[..., 1] + later[..., 1] * earlier[..., 2],
            later[..., 2] * earlier[..., 2],
        ],
        axis=-1,
    )


def apply_map(coeffs, memory, moment):
    moved_memory = coeffs[:, 0, None, None] * memory + coeffs[:, 1, None, None] * moment
    return (moved_memory, coeffs[:, 2, None, None] * moment)


def chain_combine(earlier, later):
    moved_memory, moved_moment = apply_map(later[0], earlier[1], earlier[2])
    return (compose(later[0], earlier[0]), moved_memory + later[1], moved_moment + later[2])


def to_owners(local_rows, project):
    return project(lax.all_gather(local_rows, "head", axis=0, tiled=True), jnp.int32(0))


def from_owners(term, share_rows):
    return lax.psum_scatter(
        term(jnp.int32(0), share_rows * lax.axis_size("head")),
        "head",
        scatter_dimension=0,
        tiled=True,
    )


def local(
    tokens,
    qkv_weight,
    out_weight,
    up_weight,
    down_weight,
    vocab_weight,
    persistent,
    norm_gains,
    write_rate,
    forget,
    momentum,
    prompt_spans,
):
    share_rows = tokens.shape[0]
    head_count = lax.axis_size("head")
    seq_count = lax.axis_size("seq")
    block_rows = share_rows * head_count
    heads_here = write_rate.shape[1]
    current_width = heads_here * HS
    seq_index = lax.axis_index("seq")
    head_index = lax.axis_index("head")
    qkv_blocks = qkv_weight.reshape(D, 3, heads_here, HS)
    highest = lax.Precision.HIGHEST

    def token_project(piece, start):
        normed = rms_scale(piece.astype(jnp.float32), norm_gains[0]).astype(jnp.bfloat16)
        return jnp.einsum(
            "td,dshe->shte", normed, qkv_blocks, preferred_element_type=jnp.float32
        ).astype(jnp.bfloat16)

    projected = to_owners(tokens, token_project)
    out_full = lax.all_gather(
        out_weight + (projected[0, 0, 0, 0] * 0).astype(out_weight.dtype), "head", axis=0, tiled=True
    )
    query_unit = unit_rows(projected[0])
    key_unit = unit_rows(projected[1])
    value_rows = projected[2]
    moved_keys, moved_values = passed_along((key_unit, value_rows), "seq", 1)
    all_keys = jnp.concatenate([moved_keys, key_unit], axis=1)
    all_values = jnp.concatenate([moved_values, value_rows], axis=1)
    first_row = seq_index * block_rows
    query_positions = first_row + jnp.arange(block_rows, dtype=jnp.int32)
    key_positions = first_row - block_rows + jnp.arange(2 * block_rows, dtype=jnp.int32)
    query_segments = segment_starts(query_positions, prompt_spans)
    allowed = (key_positions[None, :] >= query_segments[:, None]) & (
        key_positions[None, :] <= query_positions[:, None]
    )
    persist_keys = persistent[0].reshape(NPER, heads_here, HS)
    persist_values = persistent[1].reshape(NPER, heads_here, HS)
    scores = score_scale * jnp.einsum(
        "hqd,hkd->hqk", query_unit, all_keys, preferred_element_type=jnp.float32
    )
    scores = jnp.where(allowed[None], scores, masked_score)
    extra = score_scale * jnp.einsum(
        "hqd,phd->hqp", query_unit, persist_keys, preferred_element_type=jnp.float32
    )
    top = jnp.maximum(jnp.max(scores, axis=-1), jnp.max(extra, axis=-1))[..., None]
    near = jnp.where(allowed[None], jnp.exp(scores - top), 0.0)
    far = jnp.exp(extra - top)
    total = jnp.sum(near, axis=-1, keepdims=True) + jnp.sum(far, axis=-1, keepdims=True)
    near_weights = (near / total).astype(jnp.bfloat16)
    far_weights = (far / total).astype(jnp.bfloat16)
    attended = jnp.einsum(
        "hqk,hkd->hqd", near_weights, all_values, preferred_element_type=jnp.float32
    )
    attended = attended + jnp.einsum(
        "hqp,phd->hqd", far_weights, persist_values, preferred_element_type=jnp.float32
    )
    total_spans = block_rows // CH
    span_queries = query_unit.reshape(heads_here, total_spans, CH, HS)
    span_keys = key_unit.reshape(heads_here, total_spans, CH, HS)
    span_values = value_rows.reshape(heads_here, total_spans, CH, HS)
    span_rates = jnp.transpose(write_rate).reshape(heads_here, total_spans, CH)
    prompt_ends = jnp.cumsum(prompt_spans)
    first_spans = prompt_ends - prompt_spans
    span_ids = seq_index * total_spans + jnp.arange(total_spans, dtype=jnp.int32)
    keep = jnp.where(jnp.any(span_ids[:, None] == first_spans[None, :], axis=1), 0.0, 1.0).astype(
        jnp.float32
    )
    causal = (jnp.arange(CH)[:, None] >= jnp.arange(CH)[None, :]).astype(jnp.float32)
    values_wide = span_values.astype(jnp.float32)
    written = jnp.einsum(
        "hcti,hctj->hcij",
        span_rates[..., None] * values_wide,
        span_keys.astype(jnp.float32),
        precision=highest,
    )
    affinity = jnp.einsum(
        "hctd,hcsd->hcts", span_queries, span_keys, preferred_element_type=jnp.float32
    )
    affinity = affinity * causal[None, None] * span_rates[:, :, None, :]
    local_recall = jnp.einsum("hcts,hcsi->hcti", affinity, values_wide, precision=highest)
    decay_memory = forget * keep[:, None]
    decay_moment = momentum * keep[:, None]
    span_index = jnp.arange(total_spans)
    inside = (span_index[None, None, :] > span_index[None, :, None]) & (
        span_index[None, None, :] <= span_index[:, None, None]
    )
    lower = span_index[None, :] <= span_index[:, None]

    def range_products(rates):
        picked = jnp.where(inside[..., None], rates[None, None], 1.0)
        return jnp.where(lower[..., None], jnp.prod(picked, axis=2), 0.0)

    memory_span = range_products(decay_memory)
    moment_span = range_products(decay_moment)
    memory_coeffs = jnp.sum(memory_span[:, :, None, :] * moment_span[None, :, :, :], axis=1)
    memory_from_start = jnp.prod(jnp.where(lower[..., None], decay_memory[None], 1.0), axis=1)
    moment_from_start = jnp.prod(jnp.where(lower[..., None], decay_moment[None], 1.0), axis=1)
    memory_from_moment = jnp.sum(memory_span * moment_from_start[None], axis=1)
    coeffs_state = jnp.stack([memory_from_start, memory_from_moment, moment_from_start], axis=-1)
    identity_coeffs = jnp.tile(jnp.array([1.0, 0.0, 1.0], jnp.float32), (heads_here, 1))
    zero_state = jnp.zeros((heads_here, HS, HS), jnp.float32)
    memory_states = jnp.einsum("cjh,hjab->hcab", memory_coeffs, written, precision=highest)
    last_moment = jnp.einsum("jh,hjab->hab", moment_span[-1], written, precision=highest)
    last_memory = memory_states[:, -1]
    last_coeffs = coeffs_state[-1]
    memory_before = jnp.concatenate([zero_state[:, None], memory_states[:, :-1]], axis=1)
    coeffs_before = jnp.transpose(
        jnp.concatenate([identity_coeffs[None], coeffs_state[:-1]], axis=0), (1, 0, 2)
    )

    def pack(state):
        coeff_rows = jnp.zeros((heads_here, 8, HS), jnp.float32).at[:, 0, :3].set(state[0])
        return jnp.concatenate([state[1], state[2], coeff_rows], axis=1)

    def unpack(packed):
        return (packed[:, 2 * HS, :3], packed[:, :HS], packed[:, HS : 2 * HS])

    identity_state = (identity_coeffs, zero_state, zero_state)
    identity_packed = pack(identity_state)

    def moved_by(packed, distance):
        moved = passed_along(packed, "seq", distance)
        return jnp.where(seq_index >= distance, moved, identity_packed)

    prefix = moved_by(pack((last_coeffs, last_memory, last_moment)), 1)
    distance = 1
    while distance < seq_count:
        prefix = pack(chain_combine(unpack(moved_by(prefix, distance)), unpack(prefix)))
        distance *= 2
    _, incoming_memory, incoming_moment = unpack(prefix)
    true_before = (
        memory_before
        + coeffs_before[..., 0, None, None] * incoming_memory[:, None]
        + coeffs_before[..., 1, None, None] * incoming_moment[:, None]
    )
    recalled = local_recall + jnp.einsum(
        "hcij,hctj->hcti",
        true_before * keep[None, :, None, None],
        span_queries.astype(jnp.float32),
        precision=highest,
    )
    memory_after = memory_states
    coeffs_after = jnp.transpose(coeffs_state, (1, 0, 2))
    true_after = (
        memory_after
        + coeffs_after[..., 0, None, None] * incoming_memory[:, None]
        + coeffs_after[..., 1, None, None] * incoming_moment[:, None]
    )
    spread = jnp.sqrt(jnp.mean(true_after * true_after, axis=(2, 3)))
    hit_spans = span_ids[None, :] == (prompt_ends - 1)[:, None]
    state_slots = jnp.sum(jnp.where(hit_spans[:, None, :], spread[None], 0.0), axis=2)
    mixed = (attended + recalled.reshape(heads_here, block_rows, HS)).astype(jnp.bfloat16)
    ff_here = down_weight.shape[0]
    gate_up = up_weight.reshape(D, 2 * ff_here)

    def ffn_hidden(normed_rows):
        gated = jnp.dot(normed_rows, gate_up, preferred_element_type=jnp.float32)
        return (jax.nn.silu(gated[:, :ff_here]) * gated[:, ff_here:]).astype(jnp.bfloat16)

    def ffn_project(piece, start):
        return ffn_hidden(piece)

    pieces = jnp.transpose(mixed.reshape(heads_here, head_count, share_rows, HS), (1, 0, 2, 3))
    swapped = lax.all_to_all(pieces, "head", 0, 0, tiled=False)
    mixed_rows = jnp.transpose(swapped, (2, 0, 1, 3)).reshape(share_rows, head_count * current_width)
    residual = tokens.astype(jnp.float32) + jnp.dot(
        mixed_rows, out_full, preferred_element_type=jnp.float32
    )
    hidden = to_owners(rms_scale(residual, norm_gains[1]).astype(jnp.bfloat16), ffn_project)

    def down_term(start, count):
        return jnp.dot(hidden, down_weight, preferred_element_type=jnp.float32)

    down_sum = lax.psum_scatter(
        down_term(0, 0).astype(jnp.bfloat16), "head", scatter_dimension=0, tiled=True
    )
    second = residual + down_sum.astype(jnp.float32)
    final = rms_scale(second, norm_gains[2]).astype(jnp.bfloat16)

    def vocab_maxima(piece, start):
        return jnp.max(jnp.dot(piece, vocab_weight, preferred_element_type=jnp.float32), axis=1)

    row_maxima = to_owners(final, vocab_maxima)
    logit_max = lax.pmax(row_maxima, "head")
    state_rms = jnp.sum(lax.all_gather(state_slots, "seq"), axis=0)
    return (logit_max, state_rms)


def solution(mesh):
    in_specs = (
        P(("seq", "head"), None),
        P(None, None, "head"),
        P("head", None),
        P(None, None, "head"),
        P("head", None),
        P(None, "head"),
        P(None, None, "head"),
        P(),
        P("seq", "head"),
        P("seq", "head"),
        P("seq", "head"),
        P(),
    )
    out_specs = (P("seq"), P(None, "head"))
    return jax.shard_map(local, mesh=mesh, in_specs=in_specs, out_specs=out_specs, check_vma=False)
```

```python
import jax
import jax.numpy as jnp
from jax import lax
from jax.sharding import PartitionSpec as P

D = 1024
HS = 128
NPER = 16
SEG = 1024
CH = 64
SEQS = 4


eps_norm = 1e-05
eps_unit = 1e-06
score_scale = 10.0
masked_score = -1e30


def passed_along(array, axis, by):
    size = lax.axis_size(axis)
    pairs = [(i, i + by) for i in range(size) if 0 <= i + by < size]
    return lax.ppermute(array, axis, pairs)


def carried_in(part, axis, combine, identity):
    place = lax.axis_index(axis)
    gathered = jax.tree.map(lambda a: lax.all_gather(a, axis), part)
    state = jax.tree.map(lambda a, e: jnp.zeros_like(a) + jnp.asarray(e, a.dtype), part, identity)

    def one(step, state):
        return combine(
            state, jax.tree.map(lambda a: lax.dynamic_index_in_dim(a, step, 0, False), gathered)
        )

    return lax.fori_loop(0, place, one, state)


def rms_scale(values, gain):
    return values * lax.rsqrt(jnp.mean(values * values, axis=-1, keepdims=True) + eps_norm) * gain


def unit_rows(values):
    widened = values.astype(jnp.float32)
    return (
        widened * lax.rsqrt(jnp.sum(widened * widened, axis=-1, keepdims=True) + eps_unit)
    ).astype(jnp.bfloat16)


def segment_starts(positions, prompt_spans):
    prompt_ends = jnp.cumsum(prompt_spans)
    first_tokens = (prompt_ends - prompt_spans) * CH
    reached = positions[:, None] >= first_tokens[None, :]
    prompt_first = jnp.max(jnp.where(reached, first_tokens[None, :], 0), axis=1)
    return prompt_first + (positions - prompt_first) // SEG * SEG


def compose(later, earlier):
    return jnp.stack(
        [
            later[..., 0] * earlier[..., 0],
            later[..., 0] * earlier[..., 1] + later[..., 1] * earlier[..., 2],
            later[..., 2] * earlier[..., 2],
        ],
        axis=-1,
    )


def apply_map(coeffs, memory, moment):
    moved_memory = coeffs[:, 0, None, None] * memory + coeffs[:, 1, None, None] * moment
    return (moved_memory, coeffs[:, 2, None, None] * moment)


def chain_combine(earlier, later):
    moved_memory, moved_moment = apply_map(later[0], earlier[1], earlier[2])
    return (compose(later[0], earlier[0]), moved_memory + later[1], moved_moment + later[2])


def to_owners(local_rows, project):
    return project(lax.all_gather(local_rows, "head", axis=0, tiled=True), jnp.int32(0))


def from_owners(term, share_rows):
    return lax.psum_scatter(
        term(jnp.int32(0), share_rows * lax.axis_size("head")),
        "head",
        scatter_dimension=0,
        tiled=True,
    )


def local(
    tokens,
    qkv_weight,
    out_weight,
    up_weight,
    down_weight,
    vocab_weight,
    persistent,
    norm_gains,
    write_rate,
    forget,
    momentum,
    prompt_spans,
):
    share_rows = tokens.shape[0]
    head_count = lax.axis_size("head")
    seq_count = lax.axis_size("seq")
    block_rows = share_rows * head_count
    heads_here = write_rate.shape[1]
    current_width = heads_here * HS
    seq_index = lax.axis_index("seq")
    head_index = lax.axis_index("head")
    qkv_blocks = qkv_weight.reshape(D, 3, heads_here, HS)
    highest = lax.Precision.HIGHEST

    def token_project(piece, start):
        normed = rms_scale(piece.astype(jnp.float32), norm_gains[0]).astype(jnp.bfloat16)
        return jnp.einsum(
            "td,dshe->shte", normed, qkv_blocks, preferred_element_type=jnp.float32
        ).astype(jnp.bfloat16)

    projected = to_owners(tokens, token_project)
    out_full = lax.all_gather(
        out_weight + (projected[0, 0, 0, 0] * 0).astype(out_weight.dtype), "head", axis=0, tiled=True
    )
    query_unit = unit_rows(projected[0])
    key_unit = unit_rows(projected[1])
    value_rows = projected[2]
    moved_keys, moved_values = passed_along(jnp.stack([key_unit, value_rows]), "seq", 1)
    all_keys = jnp.concatenate([moved_keys, key_unit], axis=1)
    all_values = jnp.concatenate([moved_values, value_rows], axis=1)
    first_row = seq_index * block_rows
    query_positions = first_row + jnp.arange(block_rows, dtype=jnp.int32)
    key_positions = first_row - block_rows + jnp.arange(2 * block_rows, dtype=jnp.int32)
    query_segments = segment_starts(query_positions, prompt_spans)
    allowed = (key_positions[None, :] >= query_segments[:, None]) & (
        key_positions[None, :] <= query_positions[:, None]
    )
    persist_keys = persistent[0].reshape(NPER, heads_here, HS)
    persist_values = persistent[1].reshape(NPER, heads_here, HS)
    scores = score_scale * jnp.einsum(
        "hqd,hkd->hqk", query_unit, all_keys, preferred_element_type=jnp.float32
    )
    scores = jnp.where(allowed[None], scores, masked_score)
    extra = score_scale * jnp.einsum(
        "hqd,phd->hqp", query_unit, persist_keys, preferred_element_type=jnp.float32
    )
    top = jnp.maximum(jnp.max(scores, axis=-1), jnp.max(extra, axis=-1))[..., None]
    near = jnp.where(allowed[None], jnp.exp(scores - top), 0.0)
    far = jnp.exp(extra - top)
    total = jnp.sum(near, axis=-1, keepdims=True) + jnp.sum(far, axis=-1, keepdims=True)
    near_weights = (near / total).astype(jnp.bfloat16)
    far_weights = (far / total).astype(jnp.bfloat16)
    attended = jnp.einsum(
        "hqk,hkd->hqd", near_weights, all_values, preferred_element_type=jnp.float32
    )
    attended = attended + jnp.einsum(
        "hqp,phd->hqd", far_weights, persist_values, preferred_element_type=jnp.float32
    )
    total_spans = block_rows // CH
    span_queries = query_unit.reshape(heads_here, total_spans, CH, HS)
    span_keys = key_unit.reshape(heads_here, total_spans, CH, HS)
    span_values = value_rows.reshape(heads_here, total_spans, CH, HS)
    span_rates = jnp.transpose(write_rate).reshape(heads_here, total_spans, CH)
    prompt_ends = jnp.cumsum(prompt_spans)
    first_spans = prompt_ends - prompt_spans
    span_ids = seq_index * total_spans + jnp.arange(total_spans, dtype=jnp.int32)
    keep = jnp.where(jnp.any(span_ids[:, None] == first_spans[None, :], axis=1), 0.0, 1.0).astype(
        jnp.float32
    )
    causal = (jnp.arange(CH)[:, None] >= jnp.arange(CH)[None, :]).astype(jnp.float32)
    values_wide = span_values.astype(jnp.float32)
    written = jnp.einsum(
        "hcti,hctj->hcij",
        span_rates[..., None] * values_wide,
        span_keys.astype(jnp.float32),
        precision=highest,
    )
    affinity = jnp.einsum(
        "hctd,hcsd->hcts", span_queries, span_keys, preferred_element_type=jnp.float32
    )
    affinity = affinity * causal[None, None] * span_rates[:, :, None, :]
    local_recall = jnp.einsum("hcts,hcsi->hcti", affinity, values_wide, precision=highest)
    decay_memory = forget * keep[:, None]
    decay_moment = momentum * keep[:, None]
    span_index = jnp.arange(total_spans)
    inside = (span_index[None, None, :] > span_index[None, :, None]) & (
        span_index[None, None, :] <= span_index[:, None, None]
    )
    lower = span_index[None, :] <= span_index[:, None]

    def range_products(rates):
        picked = jnp.where(inside[..., None], rates[None, None], 1.0)
        return jnp.where(lower[..., None], jnp.prod(picked, axis=2), 0.0)

    memory_span = range_products(decay_memory)
    moment_span = range_products(decay_moment)
    memory_coeffs = jnp.sum(memory_span[:, :, None, :] * moment_span[None, :, :, :], axis=1)
    memory_from_start = jnp.prod(jnp.where(lower[..., None], decay_memory[None], 1.0), axis=1)
    moment_from_start = jnp.prod(jnp.where(lower[..., None], decay_moment[None], 1.0), axis=1)
    memory_from_moment = jnp.sum(memory_span * moment_from_start[None], axis=1)
    coeffs_state = jnp.stack([memory_from_start, memory_from_moment, moment_from_start], axis=-1)
    identity_coeffs = jnp.tile(jnp.array([1.0, 0.0, 1.0], jnp.float32), (heads_here, 1))
    zero_state = jnp.zeros((heads_here, HS, HS), jnp.float32)
    memory_states = jnp.einsum("cjh,hjab->hcab", memory_coeffs, written, precision=highest)
    last_moment = jnp.einsum("jh,hjab->hab", moment_span[-1], written, precision=highest)
    last_memory = memory_states[:, -1]
    last_coeffs = coeffs_state[-1]
    memory_before = jnp.concatenate([zero_state[:, None], memory_states[:, :-1]], axis=1)
    coeffs_before = jnp.transpose(
        jnp.concatenate([identity_coeffs[None], coeffs_state[:-1]], axis=0), (1, 0, 2)
    )

    def pack(state):
        coeff_rows = jnp.zeros((heads_here, 8, HS), jnp.float32).at[:, 0, :3].set(state[0])
        return jnp.concatenate([state[1], state[2], coeff_rows], axis=1)

    def unpack(packed):
        return (packed[:, 2 * HS, :3], packed[:, :HS], packed[:, HS : 2 * HS])

    identity_state = (identity_coeffs, zero_state, zero_state)
    identity_packed = pack(identity_state)

    def moved_by(packed, distance):
        moved = passed_along(packed, "seq", distance)
        return jnp.where(seq_index >= distance, moved, identity_packed)

    prefix = moved_by(pack((last_coeffs, last_memory, last_moment)), 1)
    distance = 1
    while distance < seq_count:
        prefix = pack(chain_combine(unpack(moved_by(prefix, distance)), unpack(prefix)))
        distance *= 2
    _, incoming_memory, incoming_moment = unpack(prefix)
    true_before = (
        memory_before
        + coeffs_before[..., 0, None, None] * incoming_memory[:, None]
        + coeffs_before[..., 1, None, None] * incoming_moment[:, None]
    )
    recalled = local_recall + jnp.einsum(
        "hcij,hctj->hcti",
        true_before * keep[None, :, None, None],
        span_queries.astype(jnp.float32),
        precision=highest,
    )
    memory_after = memory_states
    coeffs_after = jnp.transpose(coeffs_state, (1, 0, 2))
    true_after = (
        memory_after
        + coeffs_after[..., 0, None, None] * incoming_memory[:, None]
        + coeffs_after[..., 1, None, None] * incoming_moment[:, None]
    )
    spread = jnp.sqrt(jnp.mean(true_after * true_after, axis=(2, 3)))
    hit_spans = span_ids[None, :] == (prompt_ends - 1)[:, None]
    state_slots = jnp.sum(jnp.where(hit_spans[:, None, :], spread[None], 0.0), axis=2)
    mixed = (attended + recalled.reshape(heads_here, block_rows, HS)).astype(jnp.bfloat16)
    ff_here = down_weight.shape[0]
    gate_up = up_weight.reshape(D, 2 * ff_here)

    state_rms = jnp.sum(lax.all_gather(state_slots, "seq"), axis=0)

    def ffn_hidden(normed_rows):
        normed_rows = normed_rows + (state_rms[0, 0] * 0).astype(normed_rows.dtype)
        gated = jnp.dot(normed_rows, gate_up, preferred_element_type=jnp.float32)
        return (jax.nn.silu(gated[:, :ff_here]) * gated[:, ff_here:]).astype(jnp.bfloat16)

    def ffn_project(piece, start):
        return ffn_hidden(piece)

    pieces = jnp.transpose(mixed.reshape(heads_here, head_count, share_rows, HS), (1, 0, 2, 3))
    swapped = lax.all_to_all(pieces, "head", 0, 0, tiled=False)
    mixed_rows = jnp.transpose(swapped, (2, 0, 1, 3)).reshape(share_rows, head_count * current_width)
    residual = tokens.astype(jnp.float32) + jnp.dot(
        mixed_rows, out_full, preferred_element_type=jnp.float32
    )
    hidden = to_owners(rms_scale(residual, norm_gains[1]).astype(jnp.bfloat16), ffn_project)

    def down_term(start, count):
        return jnp.dot(hidden, down_weight, preferred_element_type=jnp.float32)

    down_sum = lax.psum_scatter(
        down_term(0, 0).astype(jnp.bfloat16), "head", scatter_dimension=0, tiled=True
    )
    second = residual + down_sum.astype(jnp.float32)
    final = rms_scale(second, norm_gains[2]).astype(jnp.bfloat16)

    def vocab_maxima(piece, start):
        return jnp.max(jnp.dot(piece, vocab_weight, preferred_element_type=jnp.float32), axis=1)

    row_maxima = to_owners(final, vocab_maxima)
    logit_max = lax.pmax(row_maxima, "head")
    return (logit_max, state_rms)


def solution(mesh):
    in_specs = (
        P(("seq", "head"), None),
        P(None, None, "head"),
        P("head", None),
        P(None, None, "head"),
        P("head", None),
        P(None, "head"),
        P(None, None, "head"),
        P(),
        P("seq", "head"),
        P("seq", "head"),
        P("seq", "head"),
        P(),
    )
    out_specs = (P("seq"), P(None, "head"))
    return jax.shard_map(local, mesh=mesh, in_specs=in_specs, out_specs=out_specs, check_vma=False)
```

```python
import jax
import jax.numpy as jnp
from jax import lax
from jax.sharding import PartitionSpec as P

D = 1024
HS = 128
NPER = 16
SEG = 1024
CH = 64
SEQS = 4


eps_norm = 1e-05
eps_unit = 1e-06
score_scale = 10.0
masked_score = -1e30


def passed_along(array, axis, by):
    size = lax.axis_size(axis)
    pairs = [(i, i + by) for i in range(size) if 0 <= i + by < size]
    return lax.ppermute(array, axis, pairs)


def carried_in(part, axis, combine, identity):
    place = lax.axis_index(axis)
    gathered = jax.tree.map(lambda a: lax.all_gather(a, axis), part)
    state = jax.tree.map(lambda a, e: jnp.zeros_like(a) + jnp.asarray(e, a.dtype), part, identity)

    def one(step, state):
        return combine(
            state, jax.tree.map(lambda a: lax.dynamic_index_in_dim(a, step, 0, False), gathered)
        )

    return lax.fori_loop(0, place, one, state)


def rms_scale(values, gain):
    return values * lax.rsqrt(jnp.mean(values * values, axis=-1, keepdims=True) + eps_norm) * gain


def unit_rows(values):
    widened = values.astype(jnp.float32)
    return (
        widened * lax.rsqrt(jnp.sum(widened * widened, axis=-1, keepdims=True) + eps_unit)
    ).astype(jnp.bfloat16)


def segment_starts(positions, prompt_spans):
    prompt_ends = jnp.cumsum(prompt_spans)
    first_tokens = (prompt_ends - prompt_spans) * CH
    reached = positions[:, None] >= first_tokens[None, :]
    prompt_first = jnp.max(jnp.where(reached, first_tokens[None, :], 0), axis=1)
    return prompt_first + (positions - prompt_first) // SEG * SEG


def compose(later, earlier):
    return jnp.stack(
        [
            later[..., 0] * earlier[..., 0],
            later[..., 0] * earlier[..., 1] + later[..., 1] * earlier[..., 2],
            later[..., 2] * earlier[..., 2],
        ],
        axis=-1,
    )


def apply_map(coeffs, memory, moment):
    moved_memory = coeffs[:, 0, None, None] * memory + coeffs[:, 1, None, None] * moment
    return (moved_memory, coeffs[:, 2, None, None] * moment)


def chain_combine(earlier, later):
    moved_memory, moved_moment = apply_map(later[0], earlier[1], earlier[2])
    return (compose(later[0], earlier[0]), moved_memory + later[1], moved_moment + later[2])


def to_owners(local_rows, project):
    return project(lax.all_gather(local_rows, "head", axis=0, tiled=True), jnp.int32(0))


def from_owners(term, share_rows):
    return lax.psum_scatter(
        term(jnp.int32(0), share_rows * lax.axis_size("head")),
        "head",
        scatter_dimension=0,
        tiled=True,
    )


def local(
    tokens,
    qkv_weight,
    out_weight,
    up_weight,
    down_weight,
    vocab_weight,
    persistent,
    norm_gains,
    write_rate,
    forget,
    momentum,
    prompt_spans,
):
    share_rows = tokens.shape[0]
    head_count = lax.axis_size("head")
    seq_count = lax.axis_size("seq")
    block_rows = share_rows * head_count
    heads_here = write_rate.shape[1]
    current_width = heads_here * HS
    seq_index = lax.axis_index("seq")
    head_index = lax.axis_index("head")
    qkv_blocks = qkv_weight.reshape(D, 3, heads_here, HS)
    highest = lax.Precision.HIGHEST

    def token_project(piece, start):
        normed = rms_scale(piece.astype(jnp.float32), norm_gains[0]).astype(jnp.bfloat16)
        return jnp.einsum(
            "td,dshe->shte", normed, qkv_blocks, preferred_element_type=jnp.float32
        ).astype(jnp.bfloat16)

    projected = to_owners(tokens, token_project)
    out_full = lax.all_gather(
        out_weight + (projected[0, 0, 0, 0] * 0).astype(out_weight.dtype), "head", axis=0, tiled=True
    )
    query_unit = unit_rows(projected[0])
    key_unit = unit_rows(projected[1])
    value_rows = projected[2]
    moved_keys, moved_values = passed_along((key_unit, value_rows), "seq", 1)
    all_keys = jnp.concatenate([moved_keys, key_unit], axis=1)
    all_values = jnp.concatenate([moved_values, value_rows], axis=1)
    first_row = seq_index * block_rows
    query_positions = first_row + jnp.arange(block_rows, dtype=jnp.int32)
    key_positions = first_row - block_rows + jnp.arange(2 * block_rows, dtype=jnp.int32)
    query_segments = segment_starts(query_positions, prompt_spans)
    allowed = (key_positions[None, :] >= query_segments[:, None]) & (
        key_positions[None, :] <= query_positions[:, None]
    )
    persist_keys = persistent[0].reshape(NPER, heads_here, HS)
    persist_values = persistent[1].reshape(NPER, heads_here, HS)
    scores = score_scale * jnp.einsum(
        "hqd,hkd->hqk", query_unit, all_keys, preferred_element_type=jnp.float32
    )
    scores = jnp.where(allowed[None], scores, masked_score)
    extra = score_scale * jnp.einsum(
        "hqd,phd->hqp", query_unit, persist_keys, preferred_element_type=jnp.float32
    )
    top = jnp.maximum(jnp.max(scores, axis=-1), jnp.max(extra, axis=-1))[..., None]
    near = jnp.where(allowed[None], jnp.exp(scores - top), 0.0)
    far = jnp.exp(extra - top)
    total = jnp.sum(near, axis=-1, keepdims=True) + jnp.sum(far, axis=-1, keepdims=True)
    near_weights = (near / total).astype(jnp.bfloat16)
    far_weights = (far / total).astype(jnp.bfloat16)
    attended = jnp.einsum(
        "hqk,hkd->hqd", near_weights, all_values, preferred_element_type=jnp.float32
    )
    attended = attended + jnp.einsum(
        "hqp,phd->hqd", far_weights, persist_values, preferred_element_type=jnp.float32
    )
    total_spans = block_rows // CH
    span_queries = query_unit.reshape(heads_here, total_spans, CH, HS)
    span_keys = key_unit.reshape(heads_here, total_spans, CH, HS)
    span_values = value_rows.reshape(heads_here, total_spans, CH, HS)
    span_rates = jnp.transpose(write_rate).reshape(heads_here, total_spans, CH)
    prompt_ends = jnp.cumsum(prompt_spans)
    first_spans = prompt_ends - prompt_spans
    span_ids = seq_index * total_spans + jnp.arange(total_spans, dtype=jnp.int32)
    keep = jnp.where(jnp.any(span_ids[:, None] == first_spans[None, :], axis=1), 0.0, 1.0).astype(
        jnp.float32
    )
    causal = (jnp.arange(CH)[:, None] >= jnp.arange(CH)[None, :]).astype(jnp.float32)
    values_wide = span_values.astype(jnp.float32)
    written = jnp.einsum(
        "hcti,hctj->hcij",
        span_rates[..., None] * values_wide,
        span_keys.astype(jnp.float32),
        precision=highest,
    )
    affinity = jnp.einsum(
        "hctd,hcsd->hcts", span_queries, span_keys, preferred_element_type=jnp.float32
    )
    affinity = affinity * causal[None, None] * span_rates[:, :, None, :]
    local_recall = jnp.einsum("hcts,hcsi->hcti", affinity, values_wide, precision=highest)
    decay_memory = forget * keep[:, None]
    decay_moment = momentum * keep[:, None]
    span_index = jnp.arange(total_spans)
    inside = (span_index[None, None, :] > span_index[None, :, None]) & (
        span_index[None, None, :] <= span_index[:, None, None]
    )
    lower = span_index[None, :] <= span_index[:, None]

    def range_products(rates):
        picked = jnp.where(inside[..., None], rates[None, None], 1.0)
        return jnp.where(lower[..., None], jnp.prod(picked, axis=2), 0.0)

    memory_span = range_products(decay_memory)
    moment_span = range_products(decay_moment)
    memory_coeffs = jnp.sum(memory_span[:, :, None, :] * moment_span[None, :, :, :], axis=1)
    memory_from_start = jnp.prod(jnp.where(lower[..., None], decay_memory[None], 1.0), axis=1)
    moment_from_start = jnp.prod(jnp.where(lower[..., None], decay_moment[None], 1.0), axis=1)
    memory_from_moment = jnp.sum(memory_span * moment_from_start[None], axis=1)
    coeffs_state = jnp.stack([memory_from_start, memory_from_moment, moment_from_start], axis=-1)
    identity_coeffs = jnp.tile(jnp.array([1.0, 0.0, 1.0], jnp.float32), (heads_here, 1))
    zero_state = jnp.zeros((heads_here, HS, HS), jnp.float32)
    memory_states = jnp.einsum("cjh,hjab->hcab", memory_coeffs, written, precision=highest)
    last_moment = jnp.einsum("jh,hjab->hab", moment_span[-1], written, precision=highest)
    last_memory = memory_states[:, -1]
    last_coeffs = coeffs_state[-1]
    memory_before = jnp.concatenate([zero_state[:, None], memory_states[:, :-1]], axis=1)
    coeffs_before = jnp.transpose(
        jnp.concatenate([identity_coeffs[None], coeffs_state[:-1]], axis=0), (1, 0, 2)
    )

    def pack(state):
        coeff_rows = jnp.zeros((heads_here, 8, HS), jnp.float32).at[:, 0, :3].set(state[0])
        return jnp.concatenate([state[1], state[2], coeff_rows], axis=1)

    def unpack(packed):
        return (packed[:, 2 * HS, :3], packed[:, :HS], packed[:, HS : 2 * HS])

    identity_state = (identity_coeffs, zero_state, zero_state)
    identity_packed = pack(identity_state)

    def moved_by(packed, distance):
        moved = passed_along(packed, "seq", distance)
        return jnp.where(seq_index >= distance, moved, identity_packed)

    prefix = moved_by(pack((last_coeffs, last_memory, last_moment)), 1)
    distance = 1
    while distance < seq_count:
        prefix = pack(chain_combine(unpack(moved_by(prefix, distance)), unpack(prefix)))
        distance *= 2
    _, incoming_memory, incoming_moment = unpack(prefix)
    true_before = (
        memory_before
        + coeffs_before[..., 0, None, None] * incoming_memory[:, None]
        + coeffs_before[..., 1, None, None] * incoming_moment[:, None]
    )
    recalled = local_recall + jnp.einsum(
        "hcij,hctj->hcti",
        true_before * keep[None, :, None, None],
        span_queries.astype(jnp.float32),
        precision=highest,
    )
    memory_after = memory_states
    coeffs_after = jnp.transpose(coeffs_state, (1, 0, 2))
    true_after = (
        memory_after
        + coeffs_after[..., 0, None, None] * incoming_memory[:, None]
        + coeffs_after[..., 1, None, None] * incoming_moment[:, None]
    )
    spread = jnp.sqrt(jnp.mean(true_after * true_after, axis=(2, 3)))
    hit_spans = span_ids[None, :] == (prompt_ends - 1)[:, None]
    state_slots = jnp.sum(jnp.where(hit_spans[:, None, :], spread[None], 0.0), axis=2)
    mixed = (attended + recalled.reshape(heads_here, block_rows, HS)).astype(jnp.bfloat16)
    ff_here = down_weight.shape[0]
    gate_up = up_weight.reshape(D, 2 * ff_here)

    def ffn_hidden(normed_rows):
        gated = jnp.dot(normed_rows, gate_up, preferred_element_type=jnp.float32)
        return (jax.nn.silu(gated[:, :ff_here]) * gated[:, ff_here:]).astype(jnp.bfloat16)

    def ffn_project(piece, start):
        return ffn_hidden(piece)

    pieces = jnp.transpose(mixed.reshape(heads_here, head_count, share_rows, HS), (1, 0, 2, 3))
    swapped = lax.all_to_all(pieces, "head", 0, 0, tiled=False)
    mixed_rows = jnp.transpose(swapped, (2, 0, 1, 3)).reshape(share_rows, head_count * current_width)
    residual = tokens.astype(jnp.float32) + jnp.dot(
        mixed_rows, out_full, preferred_element_type=jnp.float32
    )
    def vocab_maxima(piece, start):
        return jnp.max(jnp.dot(piece, vocab_weight, preferred_element_type=jnp.float32), axis=1)

    def second_half(rows):
        hidden = to_owners(rms_scale(rows, norm_gains[1]).astype(jnp.bfloat16), ffn_project)
        down_sum = lax.psum_scatter(
            jnp.dot(hidden, down_weight, preferred_element_type=jnp.float32).astype(jnp.bfloat16),
            "head",
            scatter_dimension=0,
            tiled=True,
        )
        second = rows + down_sum.astype(jnp.float32)
        final = rms_scale(second, norm_gains[2]).astype(jnp.bfloat16)
        return to_owners(final, vocab_maxima).reshape(head_count, 1, -1)

    half_rows = share_rows // 2
    row_maxima = jnp.concatenate(
        [second_half(residual[:half_rows]), second_half(residual[half_rows:])], axis=1
    ).reshape(block_rows)
    logit_max = lax.pmax(row_maxima, "head")
    state_rms = jnp.sum(lax.all_gather(state_slots, "seq"), axis=0)
    return (logit_max, state_rms)


def solution(mesh):
    in_specs = (
        P(("seq", "head"), None),
        P(None, None, "head"),
        P("head", None),
        P(None, None, "head"),
        P("head", None),
        P(None, "head"),
        P(None, None, "head"),
        P(),
        P("seq", "head"),
        P("seq", "head"),
        P("seq", "head"),
        P(),
    )
    out_specs = (P("seq"), P(None, "head"))
    return jax.shard_map(local, mesh=mesh, in_specs=in_specs, out_specs=out_specs, check_vma=False)
```

```python
import jax
import jax.numpy as jnp
from jax import lax
from jax.sharding import PartitionSpec as P

D = 1024
HS = 128
NPER = 16
SEG = 1024
CH = 64
SEQS = 4


eps_norm = 1e-05
eps_unit = 1e-06
score_scale = 10.0
masked_score = -1e30


def passed_along(array, axis, by):
    size = lax.axis_size(axis)
    pairs = [(i, i + by) for i in range(size) if 0 <= i + by < size]
    return lax.ppermute(array, axis, pairs)


def carried_in(part, axis, combine, identity):
    place = lax.axis_index(axis)
    gathered = jax.tree.map(lambda a: lax.all_gather(a, axis), part)
    state = jax.tree.map(lambda a, e: jnp.zeros_like(a) + jnp.asarray(e, a.dtype), part, identity)

    def one(step, state):
        return combine(
            state, jax.tree.map(lambda a: lax.dynamic_index_in_dim(a, step, 0, False), gathered)
        )

    return lax.fori_loop(0, place, one, state)


def rms_scale(values, gain):
    return values * lax.rsqrt(jnp.mean(values * values, axis=-1, keepdims=True) + eps_norm) * gain


def unit_rows(values):
    widened = values.astype(jnp.float32)
    return (
        widened * lax.rsqrt(jnp.sum(widened * widened, axis=-1, keepdims=True) + eps_unit)
    ).astype(jnp.bfloat16)


def segment_starts(positions, prompt_spans):
    prompt_ends = jnp.cumsum(prompt_spans)
    first_tokens = (prompt_ends - prompt_spans) * CH
    reached = positions[:, None] >= first_tokens[None, :]
    prompt_first = jnp.max(jnp.where(reached, first_tokens[None, :], 0), axis=1)
    return prompt_first + (positions - prompt_first) // SEG * SEG


def compose(later, earlier):
    return jnp.stack(
        [
            later[..., 0] * earlier[..., 0],
            later[..., 0] * earlier[..., 1] + later[..., 1] * earlier[..., 2],
            later[..., 2] * earlier[..., 2],
        ],
        axis=-1,
    )


def apply_map(coeffs, memory, moment):
    moved_memory = coeffs[:, 0, None, None] * memory + coeffs[:, 1, None, None] * moment
    return (moved_memory, coeffs[:, 2, None, None] * moment)


def chain_combine(earlier, later):
    moved_memory, moved_moment = apply_map(later[0], earlier[1], earlier[2])
    return (compose(later[0], earlier[0]), moved_memory + later[1], moved_moment + later[2])


def to_owners(local_rows, project):
    return project(lax.all_gather(local_rows, "head", axis=0, tiled=True), jnp.int32(0))


def from_owners(term, share_rows):
    return lax.psum_scatter(
        term(jnp.int32(0), share_rows * lax.axis_size("head")),
        "head",
        scatter_dimension=0,
        tiled=True,
    )


def local(
    tokens,
    qkv_weight,
    out_weight,
    up_weight,
    down_weight,
    vocab_weight,
    persistent,
    norm_gains,
    write_rate,
    forget,
    momentum,
    prompt_spans,
):
    share_rows = tokens.shape[0]
    head_count = lax.axis_size("head")
    seq_count = lax.axis_size("seq")
    block_rows = share_rows * head_count
    heads_here = write_rate.shape[1]
    current_width = heads_here * HS
    seq_index = lax.axis_index("seq")
    head_index = lax.axis_index("head")
    qkv_blocks = qkv_weight.reshape(D, 3, heads_here, HS)
    highest = lax.Precision.HIGHEST

    def token_project(piece, start):
        normed = rms_scale(piece.astype(jnp.float32), norm_gains[0]).astype(jnp.bfloat16)
        return jnp.einsum(
            "td,dshe->shte", normed, qkv_blocks, preferred_element_type=jnp.float32
        ).astype(jnp.bfloat16)

    projected = to_owners(tokens, token_project)
    out_full = lax.all_gather(
        out_weight + (projected[0, 0, 0, 0] * 0).astype(out_weight.dtype), "head", axis=0, tiled=True
    )
    query_unit = unit_rows(projected[0])
    key_unit = unit_rows(projected[1])
    value_rows = projected[2]
    moved_keys, moved_values = passed_along((key_unit, value_rows), "seq", 1)
    all_keys = jnp.concatenate([moved_keys, key_unit], axis=1)
    all_values = jnp.concatenate([moved_values, value_rows], axis=1)
    first_row = seq_index * block_rows
    query_positions = first_row + jnp.arange(block_rows, dtype=jnp.int32)
    key_positions = first_row - block_rows + jnp.arange(2 * block_rows, dtype=jnp.int32)
    query_segments = segment_starts(query_positions, prompt_spans)
    allowed = (key_positions[None, :] >= query_segments[:, None]) & (
        key_positions[None, :] <= query_positions[:, None]
    )
    persist_keys = persistent[0].reshape(NPER, heads_here, HS)
    persist_values = persistent[1].reshape(NPER, heads_here, HS)
    scores = score_scale * jnp.einsum(
        "hqd,hkd->hqk", query_unit, all_keys, preferred_element_type=jnp.float32
    )
    scores = jnp.where(allowed[None], scores, masked_score)
    extra = score_scale * jnp.einsum(
        "hqd,phd->hqp", query_unit, persist_keys, preferred_element_type=jnp.float32
    )
    top = jnp.maximum(jnp.max(scores, axis=-1), jnp.max(extra, axis=-1))[..., None]
    near = jnp.where(allowed[None], jnp.exp(scores - top), 0.0)
    far = jnp.exp(extra - top)
    total = jnp.sum(near, axis=-1, keepdims=True) + jnp.sum(far, axis=-1, keepdims=True)
    near_weights = (near / total).astype(jnp.bfloat16)
    far_weights = (far / total).astype(jnp.bfloat16)
    attended = jnp.einsum(
        "hqk,hkd->hqd", near_weights, all_values, preferred_element_type=jnp.float32
    )
    attended = attended + jnp.einsum(
        "hqp,phd->hqd", far_weights, persist_values, preferred_element_type=jnp.float32
    )
    total_spans = block_rows // CH
    span_queries = query_unit.reshape(heads_here, total_spans, CH, HS)
    span_keys = key_unit.reshape(heads_here, total_spans, CH, HS)
    span_values = value_rows.reshape(heads_here, total_spans, CH, HS)
    span_rates = jnp.transpose(write_rate).reshape(heads_here, total_spans, CH)
    prompt_ends = jnp.cumsum(prompt_spans)
    first_spans = prompt_ends - prompt_spans
    span_ids = seq_index * total_spans + jnp.arange(total_spans, dtype=jnp.int32)
    keep = jnp.where(jnp.any(span_ids[:, None] == first_spans[None, :], axis=1), 0.0, 1.0).astype(
        jnp.float32
    )
    causal = (jnp.arange(CH)[:, None] >= jnp.arange(CH)[None, :]).astype(jnp.float32)
    values_wide = span_values.astype(jnp.float32)
    written = jnp.einsum(
        "hcti,hctj->hcij",
        span_rates[..., None] * values_wide,
        span_keys.astype(jnp.float32),
        precision=highest,
    )
    affinity = jnp.einsum(
        "hctd,hcsd->hcts", span_queries, span_keys, preferred_element_type=jnp.float32
    )
    affinity = affinity * causal[None, None] * span_rates[:, :, None, :]
    local_recall = jnp.einsum("hcts,hcsi->hcti", affinity, values_wide, precision=highest)
    decay_memory = forget * keep[:, None]
    decay_moment = momentum * keep[:, None]
    span_index = jnp.arange(total_spans)
    inside = (span_index[None, None, :] > span_index[None, :, None]) & (
        span_index[None, None, :] <= span_index[:, None, None]
    )
    lower = span_index[None, :] <= span_index[:, None]

    def range_products(rates):
        picked = jnp.where(inside[..., None], rates[None, None], 1.0)
        return jnp.where(lower[..., None], jnp.prod(picked, axis=2), 0.0)

    memory_span = range_products(decay_memory)
    moment_span = range_products(decay_moment)
    memory_coeffs = jnp.sum(memory_span[:, :, None, :] * moment_span[None, :, :, :], axis=1)
    memory_from_start = jnp.prod(jnp.where(lower[..., None], decay_memory[None], 1.0), axis=1)
    moment_from_start = jnp.prod(jnp.where(lower[..., None], decay_moment[None], 1.0), axis=1)
    memory_from_moment = jnp.sum(memory_span * moment_from_start[None], axis=1)
    coeffs_state = jnp.stack([memory_from_start, memory_from_moment, moment_from_start], axis=-1)
    identity_coeffs = jnp.tile(jnp.array([1.0, 0.0, 1.0], jnp.float32), (heads_here, 1))
    zero_state = jnp.zeros((heads_here, HS, HS), jnp.float32)
    memory_states = jnp.einsum("cjh,hjab->hcab", memory_coeffs, written, precision=highest)
    last_moment = jnp.einsum("jh,hjab->hab", moment_span[-1], written, precision=highest)
    last_memory = memory_states[:, -1]
    last_coeffs = coeffs_state[-1]
    memory_before = jnp.concatenate([zero_state[:, None], memory_states[:, :-1]], axis=1)
    coeffs_before = jnp.transpose(
        jnp.concatenate([identity_coeffs[None], coeffs_state[:-1]], axis=0), (1, 0, 2)
    )

    def pack(state):
        coeff_rows = jnp.zeros((heads_here, 8, HS), jnp.float32).at[:, 0, :3].set(state[0])
        return jnp.concatenate([state[1], state[2], coeff_rows], axis=1)

    def unpack(packed):
        return (packed[:, 2 * HS, :3], packed[:, :HS], packed[:, HS : 2 * HS])

    identity_state = (identity_coeffs, zero_state, zero_state)
    identity_packed = pack(identity_state)

    def moved_by(packed, distance):
        moved = passed_along(packed, "seq", distance)
        return jnp.where(seq_index >= distance, moved, identity_packed)

    prefix = moved_by(pack((last_coeffs, last_memory, last_moment)), 1)
    distance = 1
    while distance < seq_count:
        prefix = pack(chain_combine(unpack(moved_by(prefix, distance)), unpack(prefix)))
        distance *= 2
    _, incoming_memory, incoming_moment = unpack(prefix)
    true_before = (
        memory_before
        + coeffs_before[..., 0, None, None] * incoming_memory[:, None]
        + coeffs_before[..., 1, None, None] * incoming_moment[:, None]
    )
    recalled = local_recall + jnp.einsum(
        "hcij,hctj->hcti",
        true_before * keep[None, :, None, None],
        span_queries.astype(jnp.float32),
        precision=highest,
    )
    memory_after = memory_states
    coeffs_after = jnp.transpose(coeffs_state, (1, 0, 2))
    true_after = (
        memory_after
        + coeffs_after[..., 0, None, None] * incoming_memory[:, None]
        + coeffs_after[..., 1, None, None] * incoming_moment[:, None]
    )
    spread = jnp.sqrt(jnp.mean(true_after * true_after, axis=(2, 3)))
    hit_spans = span_ids[None, :] == (prompt_ends - 1)[:, None]
    state_slots = jnp.sum(jnp.where(hit_spans[:, None, :], spread[None], 0.0), axis=2)
    mixed = (attended + recalled.reshape(heads_here, block_rows, HS)).astype(jnp.bfloat16)
    ff_here = down_weight.shape[0]
    gate_up = up_weight.reshape(D, 2 * ff_here)

    state_rms = jnp.sum(lax.all_gather(state_slots, "seq"), axis=0)

    def ffn_hidden(normed_rows):
        normed_rows = normed_rows + (state_rms[0, 0] * 0).astype(normed_rows.dtype)
        gated = jnp.dot(normed_rows, gate_up, preferred_element_type=jnp.float32)
        return (jax.nn.silu(gated[:, :ff_here]) * gated[:, ff_here:]).astype(jnp.bfloat16)

    def ffn_project(piece, start):
        return ffn_hidden(piece)

    pieces = jnp.transpose(mixed.reshape(heads_here, head_count, share_rows, HS), (1, 0, 2, 3))
    swapped = lax.all_to_all(pieces, "head", 0, 0, tiled=False)
    mixed_rows = jnp.transpose(swapped, (2, 0, 1, 3)).reshape(share_rows, head_count * current_width)
    residual = tokens.astype(jnp.float32) + jnp.dot(
        mixed_rows, out_full, preferred_element_type=jnp.float32
    )
    hidden = to_owners(rms_scale(residual, norm_gains[1]).astype(jnp.bfloat16), ffn_project)

    def down_term(start, count):
        return jnp.dot(hidden, down_weight, preferred_element_type=jnp.float32)

    down_sum = lax.psum_scatter(
        down_term(0, 0).astype(jnp.bfloat16), "head", scatter_dimension=0, tiled=True
    )
    second = residual + down_sum.astype(jnp.float32)
    final = rms_scale(second, norm_gains[2]).astype(jnp.bfloat16)

    def vocab_maxima(piece, start):
        return jnp.max(jnp.dot(piece, vocab_weight, preferred_element_type=jnp.float32), axis=1)

    row_maxima = to_owners(final, vocab_maxima)
    logit_max = lax.pmax(row_maxima, "head")
    return (logit_max, state_rms)


def solution(mesh):
    in_specs = (
        P(("seq", "head"), None),
        P(None, None, "head"),
        P("head", None),
        P(None, None, "head"),
        P("head", None),
        P(None, "head"),
        P(None, None, "head"),
        P(),
        P("seq", "head"),
        P("seq", "head"),
        P("seq", "head"),
        P(),
    )
    out_specs = (P("seq"), P(None, "head"))
    return jax.shard_map(local, mesh=mesh, in_specs=in_specs, out_specs=out_specs, check_vma=False)
```

```python
import jax
import jax.numpy as jnp
from jax import lax
from jax.sharding import PartitionSpec as P

D = 1024
HS = 128
NPER = 16
SEG = 1024
CH = 64
SEQS = 4


eps_norm = 1e-05
eps_unit = 1e-06
score_scale = 10.0
masked_score = -1e30


def passed_along(array, axis, by):
    size = lax.axis_size(axis)
    pairs = [(i, i + by) for i in range(size) if 0 <= i + by < size]
    return lax.ppermute(array, axis, pairs)


def carried_in(part, axis, combine, identity):
    place = lax.axis_index(axis)
    gathered = jax.tree.map(lambda a: lax.all_gather(a, axis), part)
    state = jax.tree.map(lambda a, e: jnp.zeros_like(a) + jnp.asarray(e, a.dtype), part, identity)

    def one(step, state):
        return combine(
            state, jax.tree.map(lambda a: lax.dynamic_index_in_dim(a, step, 0, False), gathered)
        )

    return lax.fori_loop(0, place, one, state)


def rms_scale(values, gain):
    return values * lax.rsqrt(jnp.mean(values * values, axis=-1, keepdims=True) + eps_norm) * gain


def unit_rows(values):
    widened = values.astype(jnp.float32)
    return (
        widened * lax.rsqrt(jnp.sum(widened * widened, axis=-1, keepdims=True) + eps_unit)
    ).astype(jnp.bfloat16)


def segment_starts(positions, prompt_spans):
    prompt_ends = jnp.cumsum(prompt_spans)
    first_tokens = (prompt_ends - prompt_spans) * CH
    reached = positions[:, None] >= first_tokens[None, :]
    prompt_first = jnp.max(jnp.where(reached, first_tokens[None, :], 0), axis=1)
    return prompt_first + (positions - prompt_first) // SEG * SEG


def compose(later, earlier):
    return jnp.stack(
        [
            later[..., 0] * earlier[..., 0],
            later[..., 0] * earlier[..., 1] + later[..., 1] * earlier[..., 2],
            later[..., 2] * earlier[..., 2],
        ],
        axis=-1,
    )


def apply_map(coeffs, memory, moment):
    moved_memory = coeffs[:, 0, None, None] * memory + coeffs[:, 1, None, None] * moment
    return (moved_memory, coeffs[:, 2, None, None] * moment)


def chain_combine(earlier, later):
    moved_memory, moved_moment = apply_map(later[0], earlier[1], earlier[2])
    return (compose(later[0], earlier[0]), moved_memory + later[1], moved_moment + later[2])


def to_owners(local_rows, project):
    return project(lax.all_gather(local_rows, "head", axis=0, tiled=True), jnp.int32(0))


def from_owners(term, share_rows):
    return lax.psum_scatter(
        term(jnp.int32(0), share_rows * lax.axis_size("head")),
        "head",
        scatter_dimension=0,
        tiled=True,
    )


def local(
    tokens,
    qkv_weight,
    out_weight,
    up_weight,
    down_weight,
    vocab_weight,
    persistent,
    norm_gains,
    write_rate,
    forget,
    momentum,
    prompt_spans,
):
    share_rows = tokens.shape[0]
    head_count = lax.axis_size("head")
    seq_count = lax.axis_size("seq")
    block_rows = share_rows * head_count
    heads_here = write_rate.shape[1]
    current_width = heads_here * HS
    seq_index = lax.axis_index("seq")
    head_index = lax.axis_index("head")
    qkv_blocks = qkv_weight.reshape(D, 3, heads_here, HS)
    highest = lax.Precision.HIGHEST

    def token_project(piece, start):
        normed = rms_scale(piece.astype(jnp.float32), norm_gains[0]).astype(jnp.bfloat16)
        return jnp.einsum(
            "td,dshe->shte", normed, qkv_blocks, preferred_element_type=jnp.float32
        ).astype(jnp.bfloat16)

    projected = to_owners(tokens, token_project)
    out_full = lax.all_gather(
        out_weight + (projected[0, 0, 0, 0] * 0).astype(out_weight.dtype), "head", axis=0, tiled=True
    )
    query_unit = unit_rows(projected[0])
    key_unit = unit_rows(projected[1])
    value_rows = projected[2]
    moved_keys, moved_values = passed_along((key_unit, value_rows), "seq", 1)
    all_keys = jnp.concatenate([moved_keys, key_unit], axis=1)
    all_values = jnp.concatenate([moved_values, value_rows], axis=1)
    first_row = seq_index * block_rows
    query_positions = first_row + jnp.arange(block_rows, dtype=jnp.int32)
    key_positions = first_row - block_rows + jnp.arange(2 * block_rows, dtype=jnp.int32)
    query_segments = segment_starts(query_positions, prompt_spans)
    allowed = (key_positions[None, :] >= query_segments[:, None]) & (
        key_positions[None, :] <= query_positions[:, None]
    )
    persist_keys = persistent[0].reshape(NPER, heads_here, HS)
    persist_values = persistent[1].reshape(NPER, heads_here, HS)
    scores = score_scale * jnp.einsum(
        "hqd,hkd->hqk", query_unit, all_keys, preferred_element_type=jnp.float32
    )
    scores = jnp.where(allowed[None], scores, masked_score)
    extra = score_scale * jnp.einsum(
        "hqd,phd->hqp", query_unit, persist_keys, preferred_element_type=jnp.float32
    )
    top = jnp.maximum(jnp.max(scores, axis=-1), jnp.max(extra, axis=-1))[..., None]
    near = jnp.where(allowed[None], jnp.exp(scores - top), 0.0)
    far = jnp.exp(extra - top)
    total = jnp.sum(near, axis=-1, keepdims=True) + jnp.sum(far, axis=-1, keepdims=True)
    near_weights = (near / total).astype(jnp.bfloat16)
    far_weights = (far / total).astype(jnp.bfloat16)
    attended = jnp.einsum(
        "hqk,hkd->hqd", near_weights, all_values, preferred_element_type=jnp.float32
    )
    attended = attended + jnp.einsum(
        "hqp,phd->hqd", far_weights, persist_values, preferred_element_type=jnp.float32
    )
    total_spans = block_rows // CH
    span_queries = query_unit.reshape(heads_here, total_spans, CH, HS)
    span_keys = key_unit.reshape(heads_here, total_spans, CH, HS)
    span_values = value_rows.reshape(heads_here, total_spans, CH, HS)
    span_rates = jnp.transpose(write_rate).reshape(heads_here, total_spans, CH)
    prompt_ends = jnp.cumsum(prompt_spans)
    first_spans = prompt_ends - prompt_spans
    span_ids = seq_index * total_spans + jnp.arange(total_spans, dtype=jnp.int32)
    keep = jnp.where(jnp.any(span_ids[:, None] == first_spans[None, :], axis=1), 0.0, 1.0).astype(
        jnp.float32
    )
    causal = (jnp.arange(CH)[:, None] >= jnp.arange(CH)[None, :]).astype(jnp.float32)
    values_wide = span_values.astype(jnp.float32)
    written = jnp.einsum(
        "hcti,hctj->hcij",
        span_rates[..., None] * values_wide,
        span_keys.astype(jnp.float32),
        precision=highest,
    )
    affinity = jnp.einsum(
        "hctd,hcsd->hcts", span_queries, span_keys, preferred_element_type=jnp.float32
    )
    affinity = affinity * causal[None, None] * span_rates[:, :, None, :]
    local_recall = jnp.einsum("hcts,hcsi->hcti", affinity, values_wide, precision=highest)
    decay_memory = forget * keep[:, None]
    decay_moment = momentum * keep[:, None]
    span_index = jnp.arange(total_spans)
    inside = (span_index[None, None, :] > span_index[None, :, None]) & (
        span_index[None, None, :] <= span_index[:, None, None]
    )
    lower = span_index[None, :] <= span_index[:, None]

    def range_products(rates):
        picked = jnp.where(inside[..., None], rates[None, None], 1.0)
        return jnp.where(lower[..., None], jnp.prod(picked, axis=2), 0.0)

    memory_span = range_products(decay_memory)
    moment_span = range_products(decay_moment)
    memory_coeffs = jnp.sum(memory_span[:, :, None, :] * moment_span[None, :, :, :], axis=1)
    memory_from_start = jnp.prod(jnp.where(lower[..., None], decay_memory[None], 1.0), axis=1)
    moment_from_start = jnp.prod(jnp.where(lower[..., None], decay_moment[None], 1.0), axis=1)
    memory_from_moment = jnp.sum(memory_span * moment_from_start[None], axis=1)
    coeffs_state = jnp.stack([memory_from_start, memory_from_moment, moment_from_start], axis=-1)
    identity_coeffs = jnp.tile(jnp.array([1.0, 0.0, 1.0], jnp.float32), (heads_here, 1))
    zero_state = jnp.zeros((heads_here, HS, HS), jnp.float32)
    memory_states = jnp.einsum("cjh,hjab->hcab", memory_coeffs, written, precision=highest)
    last_moment = jnp.einsum("jh,hjab->hab", moment_span[-1], written, precision=highest)
    last_memory = memory_states[:, -1]
    last_coeffs = coeffs_state[-1]
    memory_before = jnp.concatenate([zero_state[:, None], memory_states[:, :-1]], axis=1)
    coeffs_before = jnp.transpose(
        jnp.concatenate([identity_coeffs[None], coeffs_state[:-1]], axis=0), (1, 0, 2)
    )

    def pack(state):
        coeff_rows = jnp.zeros((heads_here, 8, HS), jnp.float32).at[:, 0, :3].set(state[0])
        return jnp.concatenate([state[1], state[2], coeff_rows], axis=1)

    def unpack(packed):
        return (packed[:, 2 * HS, :3], packed[:, :HS], packed[:, HS : 2 * HS])

    identity_state = (identity_coeffs, zero_state, zero_state)
    identity_packed = pack(identity_state)

    def moved_by(packed, distance):
        moved = passed_along(packed, "seq", distance)
        return jnp.where(seq_index >= distance, moved, identity_packed)

    prefix = moved_by(pack((last_coeffs, last_memory, last_moment)), 1)
    distance = 1
    while distance < seq_count:
        prefix = pack(chain_combine(unpack(moved_by(prefix, distance)), unpack(prefix)))
        distance *= 2
    _, incoming_memory, incoming_moment = unpack(prefix)
    true_before = (
        memory_before
        + coeffs_before[..., 0, None, None] * incoming_memory[:, None]
        + coeffs_before[..., 1, None, None] * incoming_moment[:, None]
    )
    recalled = local_recall + jnp.einsum(
        "hcij,hctj->hcti",
        true_before * keep[None, :, None, None],
        span_queries.astype(jnp.float32),
        precision=highest,
    )
    memory_after = memory_states
    coeffs_after = jnp.transpose(coeffs_state, (1, 0, 2))
    true_after = (
        memory_after
        + coeffs_after[..., 0, None, None] * incoming_memory[:, None]
        + coeffs_after[..., 1, None, None] * incoming_moment[:, None]
    )
    spread = jnp.sqrt(jnp.mean(true_after * true_after, axis=(2, 3)))
    hit_spans = span_ids[None, :] == (prompt_ends - 1)[:, None]
    state_slots = jnp.sum(jnp.where(hit_spans[:, None, :], spread[None], 0.0), axis=2)
    mixed = (attended + recalled.reshape(heads_here, block_rows, HS)).astype(jnp.bfloat16)
    ff_here = down_weight.shape[0]
    gate_up = up_weight.reshape(D, 2 * ff_here)

    state_rms = jnp.sum(lax.all_gather(state_slots, "seq"), axis=0)

    def ffn_hidden(normed_rows):
        normed_rows = normed_rows + (state_rms[0, 0] * 0).astype(normed_rows.dtype)
        gated = jnp.dot(normed_rows, gate_up, preferred_element_type=jnp.float32)
        return (jax.nn.silu(gated[:, :ff_here]) * gated[:, ff_here:]).astype(jnp.bfloat16)

    def ffn_project(piece, start):
        return ffn_hidden(piece)

    pieces = jnp.transpose(mixed.reshape(heads_here, head_count, share_rows, HS), (1, 0, 2, 3))
    swapped = lax.all_to_all(pieces, "head", 0, 0, tiled=False)
    mixed_rows = jnp.transpose(swapped, (2, 0, 1, 3)).reshape(share_rows, head_count * current_width)
    residual = tokens.astype(jnp.float32) + jnp.dot(
        mixed_rows, out_full, preferred_element_type=jnp.float32
    )
    hidden = to_owners(rms_scale(residual, norm_gains[1]).astype(jnp.bfloat16), ffn_project)

    def down_term(start, count):
        return jnp.dot(hidden, down_weight, preferred_element_type=jnp.float32)

    down_sum = lax.psum_scatter(
        down_term(0, 0).astype(jnp.bfloat16), "head", scatter_dimension=0, tiled=True
    )
    second = residual + down_sum.astype(jnp.float32)
    final = rms_scale(second, norm_gains[2]).astype(jnp.bfloat16)

    def vocab_maxima(piece, start):
        return jnp.max(jnp.dot(piece, vocab_weight, preferred_element_type=jnp.float32), axis=1)

    received = {0: final}
    for distance in range(1, head_count):
        for direction in (1, -1):
            shift = direction * distance
            pairs = [
                (i, i + shift) for i in range(head_count) if 0 <= i + shift < head_count
            ]
            received[shift] = lax.ppermute(final, "head", pairs)
    block_maxima = {shift: vocab_maxima(rows, 0) for shift, rows in received.items()}
    owner_maxima = []
    for owner in range(head_count):
        picked = jnp.zeros((share_rows,), jnp.float32)
        for shift, maxima in block_maxima.items():
            picked = jnp.where(head_index - shift == owner, maxima, picked)
        owner_maxima.append(picked)
    row_maxima = jnp.concatenate(owner_maxima)
    logit_max = lax.pmax(row_maxima, "head")
    return (logit_max, state_rms)


def solution(mesh):
    in_specs = (
        P(("seq", "head"), None),
        P(None, None, "head"),
        P("head", None),
        P(None, None, "head"),
        P("head", None),
        P(None, "head"),
        P(None, None, "head"),
        P(),
        P("seq", "head"),
        P("seq", "head"),
        P("seq", "head"),
        P(),
    )
    out_specs = (P("seq"), P(None, "head"))
    return jax.shard_map(local, mesh=mesh, in_specs=in_specs, out_specs=out_specs, check_vma=False)
```

```python
import jax
import jax.numpy as jnp
from jax import lax
from jax.sharding import PartitionSpec as P

D = 1024
HS = 128
NPER = 16
SEG = 1024
CH = 64
SEQS = 4


eps_norm = 1e-05
eps_unit = 1e-06
score_scale = 10.0
masked_score = -1e30


def passed_along(array, axis, by):
    size = lax.axis_size(axis)
    pairs = [(i, i + by) for i in range(size) if 0 <= i + by < size]
    return lax.ppermute(array, axis, pairs)


def carried_in(part, axis, combine, identity):
    place = lax.axis_index(axis)
    gathered = jax.tree.map(lambda a: lax.all_gather(a, axis), part)
    state = jax.tree.map(lambda a, e: jnp.zeros_like(a) + jnp.asarray(e, a.dtype), part, identity)

    def one(step, state):
        return combine(
            state, jax.tree.map(lambda a: lax.dynamic_index_in_dim(a, step, 0, False), gathered)
        )

    return lax.fori_loop(0, place, one, state)


def rms_scale(values, gain):
    return values * lax.rsqrt(jnp.mean(values * values, axis=-1, keepdims=True) + eps_norm) * gain


def unit_rows(values):
    widened = values.astype(jnp.float32)
    return (
        widened * lax.rsqrt(jnp.sum(widened * widened, axis=-1, keepdims=True) + eps_unit)
    ).astype(jnp.bfloat16)


def segment_starts(positions, prompt_spans):
    prompt_ends = jnp.cumsum(prompt_spans)
    first_tokens = (prompt_ends - prompt_spans) * CH
    reached = positions[:, None] >= first_tokens[None, :]
    prompt_first = jnp.max(jnp.where(reached, first_tokens[None, :], 0), axis=1)
    return prompt_first + (positions - prompt_first) // SEG * SEG


def compose(later, earlier):
    return jnp.stack(
        [
            later[..., 0] * earlier[..., 0],
            later[..., 0] * earlier[..., 1] + later[..., 1] * earlier[..., 2],
            later[..., 2] * earlier[..., 2],
        ],
        axis=-1,
    )


def apply_map(coeffs, memory, moment):
    moved_memory = coeffs[:, 0, None, None] * memory + coeffs[:, 1, None, None] * moment
    return (moved_memory, coeffs[:, 2, None, None] * moment)


def chain_combine(earlier, later):
    moved_memory, moved_moment = apply_map(later[0], earlier[1], earlier[2])
    return (compose(later[0], earlier[0]), moved_memory + later[1], moved_moment + later[2])


def to_owners(local_rows, project):
    return project(lax.all_gather(local_rows, "head", axis=0, tiled=True), jnp.int32(0))


def from_owners(term, share_rows):
    return lax.psum_scatter(
        term(jnp.int32(0), share_rows * lax.axis_size("head")),
        "head",
        scatter_dimension=0,
        tiled=True,
    )


def local(
    tokens,
    qkv_weight,
    out_weight,
    up_weight,
    down_weight,
    vocab_weight,
    persistent,
    norm_gains,
    write_rate,
    forget,
    momentum,
    prompt_spans,
):
    share_rows = tokens.shape[0]
    head_count = lax.axis_size("head")
    seq_count = lax.axis_size("seq")
    block_rows = share_rows * head_count
    heads_here = write_rate.shape[1]
    current_width = heads_here * HS
    seq_index = lax.axis_index("seq")
    head_index = lax.axis_index("head")
    qkv_blocks = qkv_weight.reshape(D, 3, heads_here, HS)
    highest = lax.Precision.HIGHEST

    def token_project(piece, start):
        normed = rms_scale(piece.astype(jnp.float32), norm_gains[0]).astype(jnp.bfloat16)
        return jnp.einsum(
            "td,dshe->shte", normed, qkv_blocks, preferred_element_type=jnp.float32
        ).astype(jnp.bfloat16)

    projected = to_owners(tokens, token_project)
    out_full = lax.all_gather(
        out_weight + (projected[0, 0, 0, 0] * 0).astype(out_weight.dtype), "head", axis=0, tiled=True
    )
    query_unit = unit_rows(projected[0])
    key_unit = unit_rows(projected[1])
    value_rows = projected[2]
    moved_keys, moved_values = passed_along((key_unit, value_rows), "seq", 1)
    all_keys = jnp.concatenate([moved_keys, key_unit], axis=1)
    all_values = jnp.concatenate([moved_values, value_rows], axis=1)
    first_row = seq_index * block_rows
    query_positions = first_row + jnp.arange(block_rows, dtype=jnp.int32)
    key_positions = first_row - block_rows + jnp.arange(2 * block_rows, dtype=jnp.int32)
    query_segments = segment_starts(query_positions, prompt_spans)
    allowed = (key_positions[None, :] >= query_segments[:, None]) & (
        key_positions[None, :] <= query_positions[:, None]
    )
    persist_keys = persistent[0].reshape(NPER, heads_here, HS)
    persist_values = persistent[1].reshape(NPER, heads_here, HS)
    scores = score_scale * jnp.einsum(
        "hqd,hkd->hqk", query_unit, all_keys, preferred_element_type=jnp.float32
    )
    scores = jnp.where(allowed[None], scores, masked_score)
    extra = score_scale * jnp.einsum(
        "hqd,phd->hqp", query_unit, persist_keys, preferred_element_type=jnp.float32
    )
    top = jnp.maximum(jnp.max(scores, axis=-1), jnp.max(extra, axis=-1))[..., None]
    near = jnp.where(allowed[None], jnp.exp(scores - top), 0.0)
    far = jnp.exp(extra - top)
    total = jnp.sum(near, axis=-1, keepdims=True) + jnp.sum(far, axis=-1, keepdims=True)
    near_weights = (near / total).astype(jnp.bfloat16)
    far_weights = (far / total).astype(jnp.bfloat16)
    attended = jnp.einsum(
        "hqk,hkd->hqd", near_weights, all_values, preferred_element_type=jnp.float32
    )
    attended = attended + jnp.einsum(
        "hqp,phd->hqd", far_weights, persist_values, preferred_element_type=jnp.float32
    )
    total_spans = block_rows // CH
    span_queries = query_unit.reshape(heads_here, total_spans, CH, HS)
    span_keys = key_unit.reshape(heads_here, total_spans, CH, HS)
    span_values = value_rows.reshape(heads_here, total_spans, CH, HS)
    span_rates = jnp.transpose(write_rate).reshape(heads_here, total_spans, CH)
    prompt_ends = jnp.cumsum(prompt_spans)
    first_spans = prompt_ends - prompt_spans
    span_ids = seq_index * total_spans + jnp.arange(total_spans, dtype=jnp.int32)
    keep = jnp.where(jnp.any(span_ids[:, None] == first_spans[None, :], axis=1), 0.0, 1.0).astype(
        jnp.float32
    )
    causal = (jnp.arange(CH)[:, None] >= jnp.arange(CH)[None, :]).astype(jnp.float32)
    values_wide = span_values.astype(jnp.float32)
    written = jnp.einsum(
        "hcti,hctj->hcij",
        span_rates[..., None] * values_wide,
        span_keys.astype(jnp.float32),
        precision=highest,
    )
    affinity = jnp.einsum(
        "hctd,hcsd->hcts", span_queries, span_keys, preferred_element_type=jnp.float32
    )
    affinity = affinity * causal[None, None] * span_rates[:, :, None, :]
    local_recall = jnp.einsum("hcts,hcsi->hcti", affinity, values_wide, precision=highest)
    decay_memory = forget * keep[:, None]
    decay_moment = momentum * keep[:, None]
    span_index = jnp.arange(total_spans)
    inside = (span_index[None, None, :] > span_index[None, :, None]) & (
        span_index[None, None, :] <= span_index[:, None, None]
    )
    lower = span_index[None, :] <= span_index[:, None]

    def range_products(rates):
        picked = jnp.where(inside[..., None], rates[None, None], 1.0)
        return jnp.where(lower[..., None], jnp.prod(picked, axis=2), 0.0)

    memory_span = range_products(decay_memory)
    moment_span = range_products(decay_moment)
    memory_coeffs = jnp.sum(memory_span[:, :, None, :] * moment_span[None, :, :, :], axis=1)
    memory_from_start = jnp.prod(jnp.where(lower[..., None], decay_memory[None], 1.0), axis=1)
    moment_from_start = jnp.prod(jnp.where(lower[..., None], decay_moment[None], 1.0), axis=1)
    memory_from_moment = jnp.sum(memory_span * moment_from_start[None], axis=1)
    coeffs_state = jnp.stack([memory_from_start, memory_from_moment, moment_from_start], axis=-1)
    identity_coeffs = jnp.tile(jnp.array([1.0, 0.0, 1.0], jnp.float32), (heads_here, 1))
    zero_state = jnp.zeros((heads_here, HS, HS), jnp.float32)
    memory_states = jnp.einsum("cjh,hjab->hcab", memory_coeffs, written, precision=highest)
    last_moment = jnp.einsum("jh,hjab->hab", moment_span[-1], written, precision=highest)
    last_memory = memory_states[:, -1]
    last_coeffs = coeffs_state[-1]
    memory_before = jnp.concatenate([zero_state[:, None], memory_states[:, :-1]], axis=1)
    coeffs_before = jnp.transpose(
        jnp.concatenate([identity_coeffs[None], coeffs_state[:-1]], axis=0), (1, 0, 2)
    )

    def pack(state):
        coeff_rows = jnp.zeros((heads_here, 8, HS), jnp.float32).at[:, 0, :3].set(state[0])
        return jnp.concatenate([state[1], state[2], coeff_rows], axis=1)

    def unpack(packed):
        return (packed[:, 2 * HS, :3], packed[:, :HS], packed[:, HS : 2 * HS])

    identity_state = (identity_coeffs, zero_state, zero_state)
    identity_packed = pack(identity_state)

    def moved_by(packed, distance):
        moved = passed_along(packed, "seq", distance)
        return jnp.where(seq_index >= distance, moved, identity_packed)

    prefix = moved_by(pack((last_coeffs, last_memory, last_moment)), 1)
    distance = 1
    while distance < seq_count:
        prefix = pack(chain_combine(unpack(moved_by(prefix, distance)), unpack(prefix)))
        distance *= 2
    _, incoming_memory, incoming_moment = unpack(prefix)
    true_before = (
        memory_before
        + coeffs_before[..., 0, None, None] * incoming_memory[:, None]
        + coeffs_before[..., 1, None, None] * incoming_moment[:, None]
    )
    recalled = local_recall + jnp.einsum(
        "hcij,hctj->hcti",
        true_before * keep[None, :, None, None],
        span_queries.astype(jnp.float32),
        precision=highest,
    )
    memory_after = memory_states
    coeffs_after = jnp.transpose(coeffs_state, (1, 0, 2))
    true_after = (
        memory_after
        + coeffs_after[..., 0, None, None] * incoming_memory[:, None]
        + coeffs_after[..., 1, None, None] * incoming_moment[:, None]
    )
    spread = jnp.sqrt(jnp.mean(true_after * true_after, axis=(2, 3)))
    hit_spans = span_ids[None, :] == (prompt_ends - 1)[:, None]
    state_slots = jnp.sum(jnp.where(hit_spans[:, None, :], spread[None], 0.0), axis=2)
    mixed = (attended + recalled.reshape(heads_here, block_rows, HS)).astype(jnp.bfloat16)
    ff_here = down_weight.shape[0]
    gate_up = up_weight.reshape(D, 2 * ff_here)

    state_rms = jnp.sum(lax.all_gather(state_slots, "seq"), axis=0)

    def ffn_hidden(normed_rows):
        normed_rows = normed_rows + (state_rms[0, 0] * 0).astype(normed_rows.dtype)
        gated = jnp.dot(normed_rows, gate_up, preferred_element_type=jnp.float32)
        return (jax.nn.silu(gated[:, :ff_here]) * gated[:, ff_here:]).astype(jnp.bfloat16)

    def ffn_project(piece, start):
        return ffn_hidden(piece)

    pieces = jnp.transpose(mixed.reshape(heads_here, head_count, share_rows, HS), (1, 0, 2, 3))
    swapped = lax.all_to_all(pieces, "head", 0, 0, tiled=False)
    mixed_rows = jnp.transpose(swapped, (2, 0, 1, 3)).reshape(share_rows, head_count * current_width)
    residual = tokens.astype(jnp.float32) + jnp.dot(
        mixed_rows, out_full, preferred_element_type=jnp.float32
    )
    def shifted_pairs(shift):
        return [(i, i + shift) for i in range(head_count) if 0 <= i + shift < head_count]

    all_shifts = [d * sign for d in range(1, head_count) for sign in (1, -1)]
    ffn_in = rms_scale(residual, norm_gains[1]).astype(jnp.bfloat16)
    ffn_blocks = {shift: lax.ppermute(ffn_in, "head", shifted_pairs(shift)) for shift in all_shifts}
    down_sum = jnp.dot(ffn_hidden(ffn_in), down_weight, preferred_element_type=jnp.float32)
    for shift in all_shifts:
        partial = jnp.dot(
            ffn_hidden(ffn_blocks[shift]), down_weight, preferred_element_type=jnp.float32
        )
        back = lax.ppermute(partial.astype(jnp.bfloat16), "head", shifted_pairs(-shift))
        down_sum = down_sum + back.astype(jnp.float32)
    second = residual + down_sum
    final = rms_scale(second, norm_gains[2]).astype(jnp.bfloat16)

    def vocab_maxima(piece, start):
        return jnp.max(jnp.dot(piece, vocab_weight, preferred_element_type=jnp.float32), axis=1)

    received = {0: final}
    for distance in range(1, head_count):
        for direction in (1, -1):
            shift = direction * distance
            pairs = [
                (i, i + shift) for i in range(head_count) if 0 <= i + shift < head_count
            ]
            received[shift] = lax.ppermute(final, "head", pairs)
    block_maxima = {shift: vocab_maxima(rows, 0) for shift, rows in received.items()}
    owner_maxima = []
    for owner in range(head_count):
        picked = jnp.zeros((share_rows,), jnp.float32)
        for shift, maxima in block_maxima.items():
            picked = jnp.where(head_index - shift == owner, maxima, picked)
        owner_maxima.append(picked)
    row_maxima = jnp.concatenate(owner_maxima)
    logit_max = lax.pmax(row_maxima, "head")
    return (logit_max, state_rms)


def solution(mesh):
    in_specs = (
        P(("seq", "head"), None),
        P(None, None, "head"),
        P("head", None),
        P(None, None, "head"),
        P("head", None),
        P(None, "head"),
        P(None, None, "head"),
        P(),
        P("seq", "head"),
        P("seq", "head"),
        P("seq", "head"),
        P(),
    )
    out_specs = (P("seq"), P(None, "head"))
    return jax.shard_map(local, mesh=mesh, in_specs=in_specs, out_specs=out_specs, check_vma=False)
```

```python
import jax
import jax.numpy as jnp
from jax import lax
from jax.sharding import PartitionSpec as P

D = 1024
HS = 128
NPER = 16
SEG = 1024
CH = 64
SEQS = 4


eps_norm = 1e-05
eps_unit = 1e-06
score_scale = 10.0
masked_score = -1e30


def passed_along(array, axis, by):
    size = lax.axis_size(axis)
    pairs = [(i, i + by) for i in range(size) if 0 <= i + by < size]
    return lax.ppermute(array, axis, pairs)


def carried_in(part, axis, combine, identity):
    place = lax.axis_index(axis)
    gathered = jax.tree.map(lambda a: lax.all_gather(a, axis), part)
    state = jax.tree.map(lambda a, e: jnp.zeros_like(a) + jnp.asarray(e, a.dtype), part, identity)

    def one(step, state):
        return combine(
            state, jax.tree.map(lambda a: lax.dynamic_index_in_dim(a, step, 0, False), gathered)
        )

    return lax.fori_loop(0, place, one, state)


def rms_scale(values, gain):
    return values * lax.rsqrt(jnp.mean(values * values, axis=-1, keepdims=True) + eps_norm) * gain


def unit_rows(values):
    widened = values.astype(jnp.float32)
    return (
        widened * lax.rsqrt(jnp.sum(widened * widened, axis=-1, keepdims=True) + eps_unit)
    ).astype(jnp.bfloat16)


def segment_starts(positions, prompt_spans):
    prompt_ends = jnp.cumsum(prompt_spans)
    first_tokens = (prompt_ends - prompt_spans) * CH
    reached = positions[:, None] >= first_tokens[None, :]
    prompt_first = jnp.max(jnp.where(reached, first_tokens[None, :], 0), axis=1)
    return prompt_first + (positions - prompt_first) // SEG * SEG


def compose(later, earlier):
    return jnp.stack(
        [
            later[..., 0] * earlier[..., 0],
            later[..., 0] * earlier[..., 1] + later[..., 1] * earlier[..., 2],
            later[..., 2] * earlier[..., 2],
        ],
        axis=-1,
    )


def apply_map(coeffs, memory, moment):
    moved_memory = coeffs[:, 0, None, None] * memory + coeffs[:, 1, None, None] * moment
    return (moved_memory, coeffs[:, 2, None, None] * moment)


def chain_combine(earlier, later):
    moved_memory, moved_moment = apply_map(later[0], earlier[1], earlier[2])
    return (compose(later[0], earlier[0]), moved_memory + later[1], moved_moment + later[2])


def to_owners(local_rows, project):
    return project(lax.all_gather(local_rows, "head", axis=0, tiled=True), jnp.int32(0))


def from_owners(term, share_rows):
    return lax.psum_scatter(
        term(jnp.int32(0), share_rows * lax.axis_size("head")),
        "head",
        scatter_dimension=0,
        tiled=True,
    )


def local(
    tokens,
    qkv_weight,
    out_weight,
    up_weight,
    down_weight,
    vocab_weight,
    persistent,
    norm_gains,
    write_rate,
    forget,
    momentum,
    prompt_spans,
):
    share_rows = tokens.shape[0]
    head_count = lax.axis_size("head")
    seq_count = lax.axis_size("seq")
    block_rows = share_rows * head_count
    heads_here = write_rate.shape[1]
    current_width = heads_here * HS
    seq_index = lax.axis_index("seq")
    head_index = lax.axis_index("head")
    qkv_blocks = qkv_weight.reshape(D, 3, heads_here, HS)
    highest = lax.Precision.HIGHEST

    def token_project(piece, start):
        normed = rms_scale(piece.astype(jnp.float32), norm_gains[0]).astype(jnp.bfloat16)
        return jnp.einsum(
            "td,dshe->shte", normed, qkv_blocks, preferred_element_type=jnp.float32
        ).astype(jnp.bfloat16)

    projected = to_owners(tokens, token_project)
    out_full = lax.all_gather(
        out_weight + (projected[0, 0, 0, 0] * 0).astype(out_weight.dtype), "head", axis=0, tiled=True
    )
    query_unit = unit_rows(projected[0])
    key_unit = unit_rows(projected[1])
    value_rows = projected[2]
    moved_keys, moved_values = passed_along(jnp.stack([key_unit, value_rows]), "seq", 1)
    all_keys = jnp.concatenate([moved_keys, key_unit], axis=1)
    all_values = jnp.concatenate([moved_values, value_rows], axis=1)
    first_row = seq_index * block_rows
    query_positions = first_row + jnp.arange(block_rows, dtype=jnp.int32)
    key_positions = first_row - block_rows + jnp.arange(2 * block_rows, dtype=jnp.int32)
    query_segments = segment_starts(query_positions, prompt_spans)
    allowed = (key_positions[None, :] >= query_segments[:, None]) & (
        key_positions[None, :] <= query_positions[:, None]
    )
    persist_keys = persistent[0].reshape(NPER, heads_here, HS)
    persist_values = persistent[1].reshape(NPER, heads_here, HS)
    scores = score_scale * jnp.einsum(
        "hqd,hkd->hqk", query_unit, all_keys, preferred_element_type=jnp.float32
    )
    scores = jnp.where(allowed[None], scores, masked_score)
    extra = score_scale * jnp.einsum(
        "hqd,phd->hqp", query_unit, persist_keys, preferred_element_type=jnp.float32
    )
    top = jnp.maximum(jnp.max(scores, axis=-1), jnp.max(extra, axis=-1))[..., None]
    near = jnp.where(allowed[None], jnp.exp(scores - top), 0.0)
    far = jnp.exp(extra - top)
    total = jnp.sum(near, axis=-1, keepdims=True) + jnp.sum(far, axis=-1, keepdims=True)
    near_weights = (near / total).astype(jnp.bfloat16)
    far_weights = (far / total).astype(jnp.bfloat16)
    attended = jnp.einsum(
        "hqk,hkd->hqd", near_weights, all_values, preferred_element_type=jnp.float32
    )
    attended = attended + jnp.einsum(
        "hqp,phd->hqd", far_weights, persist_values, preferred_element_type=jnp.float32
    )
    total_spans = block_rows // CH
    span_queries = query_unit.reshape(heads_here, total_spans, CH, HS)
    span_keys = key_unit.reshape(heads_here, total_spans, CH, HS)
    span_values = value_rows.reshape(heads_here, total_spans, CH, HS)
    span_rates = jnp.transpose(write_rate).reshape(heads_here, total_spans, CH)
    prompt_ends = jnp.cumsum(prompt_spans)
    first_spans = prompt_ends - prompt_spans
    span_ids = seq_index * total_spans + jnp.arange(total_spans, dtype=jnp.int32)
    keep = jnp.where(jnp.any(span_ids[:, None] == first_spans[None, :], axis=1), 0.0, 1.0).astype(
        jnp.float32
    )
    causal = (jnp.arange(CH)[:, None] >= jnp.arange(CH)[None, :]).astype(jnp.float32)
    values_wide = span_values.astype(jnp.float32)
    written = jnp.einsum(
        "hcti,hctj->hcij",
        span_rates[..., None] * values_wide,
        span_keys.astype(jnp.float32),
        precision=highest,
    )
    affinity = jnp.einsum(
        "hctd,hcsd->hcts", span_queries, span_keys, preferred_element_type=jnp.float32
    )
    affinity = affinity * causal[None, None] * span_rates[:, :, None, :]
    local_recall = jnp.einsum("hcts,hcsi->hcti", affinity, values_wide, precision=highest)
    decay_memory = forget * keep[:, None]
    decay_moment = momentum * keep[:, None]
    span_index = jnp.arange(total_spans)
    inside = (span_index[None, None, :] > span_index[None, :, None]) & (
        span_index[None, None, :] <= span_index[:, None, None]
    )
    lower = span_index[None, :] <= span_index[:, None]

    def range_products(rates):
        picked = jnp.where(inside[..., None], rates[None, None], 1.0)
        return jnp.where(lower[..., None], jnp.prod(picked, axis=2), 0.0)

    memory_span = range_products(decay_memory)
    moment_span = range_products(decay_moment)
    memory_coeffs = jnp.sum(memory_span[:, :, None, :] * moment_span[None, :, :, :], axis=1)
    memory_from_start = jnp.prod(jnp.where(lower[..., None], decay_memory[None], 1.0), axis=1)
    moment_from_start = jnp.prod(jnp.where(lower[..., None], decay_moment[None], 1.0), axis=1)
    memory_from_moment = jnp.sum(memory_span * moment_from_start[None], axis=1)
    coeffs_state = jnp.stack([memory_from_start, memory_from_moment, moment_from_start], axis=-1)
    identity_coeffs = jnp.tile(jnp.array([1.0, 0.0, 1.0], jnp.float32), (heads_here, 1))
    zero_state = jnp.zeros((heads_here, HS, HS), jnp.float32)
    memory_states = jnp.einsum("cjh,hjab->hcab", memory_coeffs, written, precision=highest)
    last_moment = jnp.einsum("jh,hjab->hab", moment_span[-1], written, precision=highest)
    last_memory = memory_states[:, -1]
    last_coeffs = coeffs_state[-1]
    memory_before = jnp.concatenate([zero_state[:, None], memory_states[:, :-1]], axis=1)
    coeffs_before = jnp.transpose(
        jnp.concatenate([identity_coeffs[None], coeffs_state[:-1]], axis=0), (1, 0, 2)
    )

    def pack(state):
        coeff_rows = jnp.zeros((heads_here, 8, HS), jnp.float32).at[:, 0, :3].set(state[0])
        return jnp.concatenate([state[1], state[2], coeff_rows], axis=1)

    def unpack(packed):
        return (packed[:, 2 * HS, :3], packed[:, :HS], packed[:, HS : 2 * HS])

    identity_state = (identity_coeffs, zero_state, zero_state)
    identity_packed = pack(identity_state)

    def moved_by(packed, distance):
        moved = passed_along(packed, "seq", distance)
        return jnp.where(seq_index >= distance, moved, identity_packed)

    prefix = moved_by(pack((last_coeffs, last_memory, last_moment)), 1)
    distance = 1
    while distance < seq_count:
        prefix = pack(chain_combine(unpack(moved_by(prefix, distance)), unpack(prefix)))
        distance *= 2
    _, incoming_memory, incoming_moment = unpack(prefix)
    true_before = (
        memory_before
        + coeffs_before[..., 0, None, None] * incoming_memory[:, None]
        + coeffs_before[..., 1, None, None] * incoming_moment[:, None]
    )
    recalled = local_recall + jnp.einsum(
        "hcij,hctj->hcti",
        true_before * keep[None, :, None, None],
        span_queries.astype(jnp.float32),
        precision=highest,
    )
    memory_after = memory_states
    coeffs_after = jnp.transpose(coeffs_state, (1, 0, 2))
    true_after = (
        memory_after
        + coeffs_after[..., 0, None, None] * incoming_memory[:, None]
        + coeffs_after[..., 1, None, None] * incoming_moment[:, None]
    )
    spread = jnp.sqrt(jnp.mean(true_after * true_after, axis=(2, 3)))
    hit_spans = span_ids[None, :] == (prompt_ends - 1)[:, None]
    state_slots = jnp.sum(jnp.where(hit_spans[:, None, :], spread[None], 0.0), axis=2)
    mixed = (attended + recalled.reshape(heads_here, block_rows, HS)).astype(jnp.bfloat16)
    ff_here = down_weight.shape[0]
    gate_up = up_weight.reshape(D, 2 * ff_here)

    state_rms = jnp.sum(lax.all_gather(state_slots, "seq"), axis=0)

    def ffn_hidden(normed_rows):
        normed_rows = normed_rows + (state_rms[0, 0] * 0).astype(normed_rows.dtype)
        gated = jnp.dot(normed_rows, gate_up, preferred_element_type=jnp.float32)
        return (jax.nn.silu(gated[:, :ff_here]) * gated[:, ff_here:]).astype(jnp.bfloat16)

    def ffn_project(piece, start):
        return ffn_hidden(piece)

    pieces = jnp.transpose(mixed.reshape(heads_here, head_count, share_rows, HS), (1, 0, 2, 3))
    swapped = lax.all_to_all(pieces, "head", 0, 0, tiled=False)
    mixed_rows = jnp.transpose(swapped, (2, 0, 1, 3)).reshape(share_rows, head_count * current_width)
    residual = tokens.astype(jnp.float32) + jnp.dot(
        mixed_rows, out_full, preferred_element_type=jnp.float32
    )
    hidden = to_owners(rms_scale(residual, norm_gains[1]).astype(jnp.bfloat16), ffn_project)

    def down_term(start, count):
        return jnp.dot(hidden, down_weight, preferred_element_type=jnp.float32)

    down_sum = lax.psum_scatter(
        down_term(0, 0).astype(jnp.bfloat16), "head", scatter_dimension=0, tiled=True
    )
    second = residual + down_sum.astype(jnp.float32)
    final = rms_scale(second, norm_gains[2]).astype(jnp.bfloat16)

    def vocab_maxima(piece, start):
        return jnp.max(jnp.dot(piece, vocab_weight, preferred_element_type=jnp.float32), axis=1)

    received = {0: final}
    for distance in range(1, head_count):
        for direction in (1, -1):
            shift = direction * distance
            pairs = [
                (i, i + shift) for i in range(head_count) if 0 <= i + shift < head_count
            ]
            received[shift] = lax.ppermute(final, "head", pairs)
    block_maxima = {shift: vocab_maxima(rows, 0) for shift, rows in received.items()}
    owner_maxima = []
    for owner in range(head_count):
        picked = jnp.zeros((share_rows,), jnp.float32)
        for shift, maxima in block_maxima.items():
            picked = jnp.where(head_index - shift == owner, maxima, picked)
        owner_maxima.append(picked)
    row_maxima = jnp.concatenate(owner_maxima)
    logit_max = lax.pmax(row_maxima, "head")
    return (logit_max, state_rms)


def solution(mesh):
    in_specs = (
        P(("seq", "head"), None),
        P(None, None, "head"),
        P("head", None),
        P(None, None, "head"),
        P("head", None),
        P(None, "head"),
        P(None, None, "head"),
        P(),
        P("seq", "head"),
        P("seq", "head"),
        P("seq", "head"),
        P(),
    )
    out_specs = (P("seq"), P(None, "head"))
    return jax.shard_map(local, mesh=mesh, in_specs=in_specs, out_specs=out_specs, check_vma=False)
```

```python
import jax
import jax.numpy as jnp
from jax import lax
from jax.sharding import PartitionSpec as P

D = 1024
HS = 128
NPER = 16
SEG = 1024
CH = 64
SEQS = 4


eps_norm = 1e-05
eps_unit = 1e-06
score_scale = 10.0
masked_score = -1e30


def passed_along(array, axis, by):
    size = lax.axis_size(axis)
    pairs = [(i, i + by) for i in range(size) if 0 <= i + by < size]
    return lax.ppermute(array, axis, pairs)


def carried_in(part, axis, combine, identity):
    place = lax.axis_index(axis)
    gathered = jax.tree.map(lambda a: lax.all_gather(a, axis), part)
    state = jax.tree.map(lambda a, e: jnp.zeros_like(a) + jnp.asarray(e, a.dtype), part, identity)

    def one(step, state):
        return combine(
            state, jax.tree.map(lambda a: lax.dynamic_index_in_dim(a, step, 0, False), gathered)
        )

    return lax.fori_loop(0, place, one, state)


def rms_scale(values, gain):
    return values * lax.rsqrt(jnp.mean(values * values, axis=-1, keepdims=True) + eps_norm) * gain


def unit_rows(values):
    widened = values.astype(jnp.float32)
    return (
        widened * lax.rsqrt(jnp.sum(widened * widened, axis=-1, keepdims=True) + eps_unit)
    ).astype(jnp.bfloat16)


def segment_starts(positions, prompt_spans):
    prompt_ends = jnp.cumsum(prompt_spans)
    first_tokens = (prompt_ends - prompt_spans) * CH
    reached = positions[:, None] >= first_tokens[None, :]
    prompt_first = jnp.max(jnp.where(reached, first_tokens[None, :], 0), axis=1)
    return prompt_first + (positions - prompt_first) // SEG * SEG


def compose(later, earlier):
    return jnp.stack(
        [
            later[..., 0] * earlier[..., 0],
            later[..., 0] * earlier[..., 1] + later[..., 1] * earlier[..., 2],
            later[..., 2] * earlier[..., 2],
        ],
        axis=-1,
    )


def apply_map(coeffs, memory, moment):
    moved_memory = coeffs[:, 0, None, None] * memory + coeffs[:, 1, None, None] * moment
    return (moved_memory, coeffs[:, 2, None, None] * moment)


def chain_combine(earlier, later):
    moved_memory, moved_moment = apply_map(later[0], earlier[1], earlier[2])
    return (compose(later[0], earlier[0]), moved_memory + later[1], moved_moment + later[2])


def to_owners(local_rows, project):
    return project(lax.all_gather(local_rows, "head", axis=0, tiled=True), jnp.int32(0))


def from_owners(term, share_rows):
    return lax.psum_scatter(
        term(jnp.int32(0), share_rows * lax.axis_size("head")),
        "head",
        scatter_dimension=0,
        tiled=True,
    )


def local(
    tokens,
    qkv_weight,
    out_weight,
    up_weight,
    down_weight,
    vocab_weight,
    persistent,
    norm_gains,
    write_rate,
    forget,
    momentum,
    prompt_spans,
):
    share_rows = tokens.shape[0]
    head_count = lax.axis_size("head")
    seq_count = lax.axis_size("seq")
    block_rows = share_rows * head_count
    heads_here = write_rate.shape[1]
    current_width = heads_here * HS
    seq_index = lax.axis_index("seq")
    head_index = lax.axis_index("head")
    qkv_blocks = qkv_weight.reshape(D, 3, heads_here, HS)
    highest = lax.Precision.HIGHEST

    def token_project(piece, start):
        normed = rms_scale(piece.astype(jnp.float32), norm_gains[0]).astype(jnp.bfloat16)
        return jnp.einsum(
            "td,dshe->shte", normed, qkv_blocks, preferred_element_type=jnp.float32
        ).astype(jnp.bfloat16)

    token_shifts = [d * sign for d in range(1, head_count) for sign in (1, -1)]
    token_blocks = {0: tokens}
    for shift in token_shifts:
        token_blocks[shift] = passed_along(tokens, "head", shift)
    projected = jnp.zeros((3, heads_here, block_rows + share_rows, HS), jnp.bfloat16)
    for shift, rows in token_blocks.items():
        source = head_index - shift
        valid = (source >= 0) & (source < head_count)
        slot = jnp.where(valid, source, head_count) * share_rows
        projected = lax.dynamic_update_slice(
            projected, token_project(rows, 0), (0, 0, slot, 0)
        )
    projected = projected[:, :, :block_rows]
    out_full = lax.all_gather(
        out_weight + (projected[0, 0, 0, 0] * 0).astype(out_weight.dtype), "head", axis=0, tiled=True
    )
    query_unit = unit_rows(projected[0])
    key_unit = unit_rows(projected[1])
    value_rows = projected[2]
    moved_keys, moved_values = passed_along((key_unit, value_rows), "seq", 1)
    all_keys = jnp.concatenate([moved_keys, key_unit], axis=1)
    all_values = jnp.concatenate([moved_values, value_rows], axis=1)
    first_row = seq_index * block_rows
    query_positions = first_row + jnp.arange(block_rows, dtype=jnp.int32)
    key_positions = first_row - block_rows + jnp.arange(2 * block_rows, dtype=jnp.int32)
    query_segments = segment_starts(query_positions, prompt_spans)
    allowed = (key_positions[None, :] >= query_segments[:, None]) & (
        key_positions[None, :] <= query_positions[:, None]
    )
    persist_keys = persistent[0].reshape(NPER, heads_here, HS)
    persist_values = persistent[1].reshape(NPER, heads_here, HS)
    scores = score_scale * jnp.einsum(
        "hqd,hkd->hqk", query_unit, all_keys, preferred_element_type=jnp.float32
    )
    scores = jnp.where(allowed[None], scores, masked_score)
    extra = score_scale * jnp.einsum(
        "hqd,phd->hqp", query_unit, persist_keys, preferred_element_type=jnp.float32
    )
    top = jnp.maximum(jnp.max(scores, axis=-1), jnp.max(extra, axis=-1))[..., None]
    near = jnp.where(allowed[None], jnp.exp(scores - top), 0.0)
    far = jnp.exp(extra - top)
    total = jnp.sum(near, axis=-1, keepdims=True) + jnp.sum(far, axis=-1, keepdims=True)
    near_weights = (near / total).astype(jnp.bfloat16)
    far_weights = (far / total).astype(jnp.bfloat16)
    attended = jnp.einsum(
        "hqk,hkd->hqd", near_weights, all_values, preferred_element_type=jnp.float32
    )
    attended = attended + jnp.einsum(
        "hqp,phd->hqd", far_weights, persist_values, preferred_element_type=jnp.float32
    )
    total_spans = block_rows // CH
    span_queries = query_unit.reshape(heads_here, total_spans, CH, HS)
    span_keys = key_unit.reshape(heads_here, total_spans, CH, HS)
    span_values = value_rows.reshape(heads_here, total_spans, CH, HS)
    span_rates = jnp.transpose(write_rate).reshape(heads_here, total_spans, CH)
    prompt_ends = jnp.cumsum(prompt_spans)
    first_spans = prompt_ends - prompt_spans
    span_ids = seq_index * total_spans + jnp.arange(total_spans, dtype=jnp.int32)
    keep = jnp.where(jnp.any(span_ids[:, None] == first_spans[None, :], axis=1), 0.0, 1.0).astype(
        jnp.float32
    )
    causal = (jnp.arange(CH)[:, None] >= jnp.arange(CH)[None, :]).astype(jnp.float32)
    values_wide = span_values.astype(jnp.float32)
    written = jnp.einsum(
        "hcti,hctj->hcij",
        span_rates[..., None] * values_wide,
        span_keys.astype(jnp.float32),
        precision=highest,
    )
    affinity = jnp.einsum(
        "hctd,hcsd->hcts", span_queries, span_keys, preferred_element_type=jnp.float32
    )
    affinity = affinity * causal[None, None] * span_rates[:, :, None, :]
    local_recall = jnp.einsum("hcts,hcsi->hcti", affinity, values_wide, precision=highest)
    decay_memory = forget * keep[:, None]
    decay_moment = momentum * keep[:, None]
    span_index = jnp.arange(total_spans)
    inside = (span_index[None, None, :] > span_index[None, :, None]) & (
        span_index[None, None, :] <= span_index[:, None, None]
    )
    lower = span_index[None, :] <= span_index[:, None]

    def range_products(rates):
        picked = jnp.where(inside[..., None], rates[None, None], 1.0)
        return jnp.where(lower[..., None], jnp.prod(picked, axis=2), 0.0)

    memory_span = range_products(decay_memory)
    moment_span = range_products(decay_moment)
    memory_coeffs = jnp.sum(memory_span[:, :, None, :] * moment_span[None, :, :, :], axis=1)
    memory_from_start = jnp.prod(jnp.where(lower[..., None], decay_memory[None], 1.0), axis=1)
    moment_from_start = jnp.prod(jnp.where(lower[..., None], decay_moment[None], 1.0), axis=1)
    memory_from_moment = jnp.sum(memory_span * moment_from_start[None], axis=1)
    coeffs_state = jnp.stack([memory_from_start, memory_from_moment, moment_from_start], axis=-1)
    identity_coeffs = jnp.tile(jnp.array([1.0, 0.0, 1.0], jnp.float32), (heads_here, 1))
    zero_state = jnp.zeros((heads_here, HS, HS), jnp.float32)
    memory_states = jnp.einsum("cjh,hjab->hcab", memory_coeffs, written, precision=highest)
    last_moment = jnp.einsum("jh,hjab->hab", moment_span[-1], written, precision=highest)
    last_memory = memory_states[:, -1]
    last_coeffs = coeffs_state[-1]
    memory_before = jnp.concatenate([zero_state[:, None], memory_states[:, :-1]], axis=1)
    coeffs_before = jnp.transpose(
        jnp.concatenate([identity_coeffs[None], coeffs_state[:-1]], axis=0), (1, 0, 2)
    )

    def pack(state):
        coeff_rows = jnp.zeros((heads_here, 8, HS), jnp.float32).at[:, 0, :3].set(state[0])
        return jnp.concatenate([state[1], state[2], coeff_rows], axis=1)

    def unpack(packed):
        return (packed[:, 2 * HS, :3], packed[:, :HS], packed[:, HS : 2 * HS])

    identity_state = (identity_coeffs, zero_state, zero_state)
    identity_packed = pack(identity_state)

    def moved_by(packed, distance):
        moved = passed_along(packed, "seq", distance)
        return jnp.where(seq_index >= distance, moved, identity_packed)

    prefix = moved_by(pack((last_coeffs, last_memory, last_moment)), 1)
    distance = 1
    while distance < seq_count:
        prefix = pack(chain_combine(unpack(moved_by(prefix, distance)), unpack(prefix)))
        distance *= 2
    _, incoming_memory, incoming_moment = unpack(prefix)
    true_before = (
        memory_before
        + coeffs_before[..., 0, None, None] * incoming_memory[:, None]
        + coeffs_before[..., 1, None, None] * incoming_moment[:, None]
    )
    recalled = local_recall + jnp.einsum(
        "hcij,hctj->hcti",
        true_before * keep[None, :, None, None],
        span_queries.astype(jnp.float32),
        precision=highest,
    )
    memory_after = memory_states
    coeffs_after = jnp.transpose(coeffs_state, (1, 0, 2))
    true_after = (
        memory_after
        + coeffs_after[..., 0, None, None] * incoming_memory[:, None]
        + coeffs_after[..., 1, None, None] * incoming_moment[:, None]
    )
    spread = jnp.sqrt(jnp.mean(true_after * true_after, axis=(2, 3)))
    hit_spans = span_ids[None, :] == (prompt_ends - 1)[:, None]
    state_slots = jnp.sum(jnp.where(hit_spans[:, None, :], spread[None], 0.0), axis=2)
    mixed = (attended + recalled.reshape(heads_here, block_rows, HS)).astype(jnp.bfloat16)
    ff_here = down_weight.shape[0]
    gate_up = up_weight.reshape(D, 2 * ff_here)

    state_rms = jnp.sum(lax.all_gather(state_slots, "seq"), axis=0)

    def ffn_hidden(normed_rows):
        normed_rows = normed_rows + (state_rms[0, 0] * 0).astype(normed_rows.dtype)
        gated = jnp.dot(normed_rows, gate_up, preferred_element_type=jnp.float32)
        return (jax.nn.silu(gated[:, :ff_here]) * gated[:, ff_here:]).astype(jnp.bfloat16)

    def ffn_project(piece, start):
        return ffn_hidden(piece)

    pieces = jnp.transpose(mixed.reshape(heads_here, head_count, share_rows, HS), (1, 0, 2, 3))
    swapped = lax.all_to_all(pieces, "head", 0, 0, tiled=False)
    mixed_rows = jnp.transpose(swapped, (2, 0, 1, 3)).reshape(share_rows, head_count * current_width)
    residual = tokens.astype(jnp.float32) + jnp.dot(
        mixed_rows, out_full, preferred_element_type=jnp.float32
    )
    hidden = to_owners(rms_scale(residual, norm_gains[1]).astype(jnp.bfloat16), ffn_project)

    def down_term(start, count):
        return jnp.dot(hidden, down_weight, preferred_element_type=jnp.float32)

    down_sum = lax.psum_scatter(
        down_term(0, 0).astype(jnp.bfloat16), "head", scatter_dimension=0, tiled=True
    )
    second = residual + down_sum.astype(jnp.float32)
    final = rms_scale(second, norm_gains[2]).astype(jnp.bfloat16)

    def vocab_maxima(piece, start):
        return jnp.max(jnp.dot(piece, vocab_weight, preferred_element_type=jnp.float32), axis=1)

    received = {0: final}
    for distance in range(1, head_count):
        for direction in (1, -1):
            shift = direction * distance
            pairs = [
                (i, i + shift) for i in range(head_count) if 0 <= i + shift < head_count
            ]
            received[shift] = lax.ppermute(final, "head", pairs)
    block_maxima = {shift: vocab_maxima(rows, 0) for shift, rows in received.items()}
    owner_maxima = []
    for owner in range(head_count):
        picked = jnp.zeros((share_rows,), jnp.float32)
        for shift, maxima in block_maxima.items():
            picked = jnp.where(head_index - shift == owner, maxima, picked)
        owner_maxima.append(picked)
    row_maxima = jnp.concatenate(owner_maxima)
    logit_max = lax.pmax(row_maxima, "head")
    return (logit_max, state_rms)


def solution(mesh):
    in_specs = (
        P(("seq", "head"), None),
        P(None, None, "head"),
        P("head", None),
        P(None, None, "head"),
        P("head", None),
        P(None, "head"),
        P(None, None, "head"),
        P(),
        P("seq", "head"),
        P("seq", "head"),
        P("seq", "head"),
        P(),
    )
    out_specs = (P("seq"), P(None, "head"))
    return jax.shard_map(local, mesh=mesh, in_specs=in_specs, out_specs=out_specs, check_vma=False)
```

```python
import jax
import jax.numpy as jnp
from jax import lax
from jax.sharding import PartitionSpec as P

D = 1024
HS = 128
NPER = 16
SEG = 1024
CH = 64
SEQS = 4


eps_norm = 1e-05
eps_unit = 1e-06
score_scale = 10.0
masked_score = -1e30


def passed_along(array, axis, by):
    size = lax.axis_size(axis)
    pairs = [(i, i + by) for i in range(size) if 0 <= i + by < size]
    return lax.ppermute(array, axis, pairs)


def carried_in(part, axis, combine, identity):
    place = lax.axis_index(axis)
    gathered = jax.tree.map(lambda a: lax.all_gather(a, axis), part)
    state = jax.tree.map(lambda a, e: jnp.zeros_like(a) + jnp.asarray(e, a.dtype), part, identity)

    def one(step, state):
        return combine(
            state, jax.tree.map(lambda a: lax.dynamic_index_in_dim(a, step, 0, False), gathered)
        )

    return lax.fori_loop(0, place, one, state)


def rms_scale(values, gain):
    return values * lax.rsqrt(jnp.mean(values * values, axis=-1, keepdims=True) + eps_norm) * gain


def unit_rows(values):
    widened = values.astype(jnp.float32)
    return (
        widened * lax.rsqrt(jnp.sum(widened * widened, axis=-1, keepdims=True) + eps_unit)
    ).astype(jnp.bfloat16)


def segment_starts(positions, prompt_spans):
    prompt_ends = jnp.cumsum(prompt_spans)
    first_tokens = (prompt_ends - prompt_spans) * CH
    reached = positions[:, None] >= first_tokens[None, :]
    prompt_first = jnp.max(jnp.where(reached, first_tokens[None, :], 0), axis=1)
    return prompt_first + (positions - prompt_first) // SEG * SEG


def compose(later, earlier):
    return jnp.stack(
        [
            later[..., 0] * earlier[..., 0],
            later[..., 0] * earlier[..., 1] + later[..., 1] * earlier[..., 2],
            later[..., 2] * earlier[..., 2],
        ],
        axis=-1,
    )


def apply_map(coeffs, memory, moment):
    moved_memory = coeffs[:, 0, None, None] * memory + coeffs[:, 1, None, None] * moment
    return (moved_memory, coeffs[:, 2, None, None] * moment)


def chain_combine(earlier, later):
    moved_memory, moved_moment = apply_map(later[0], earlier[1], earlier[2])
    return (compose(later[0], earlier[0]), moved_memory + later[1], moved_moment + later[2])


def to_owners(local_rows, project):
    return project(lax.all_gather(local_rows, "head", axis=0, tiled=True), jnp.int32(0))


def from_owners(term, share_rows):
    return lax.psum_scatter(
        term(jnp.int32(0), share_rows * lax.axis_size("head")),
        "head",
        scatter_dimension=0,
        tiled=True,
    )


def local(
    tokens,
    qkv_weight,
    out_weight,
    up_weight,
    down_weight,
    vocab_weight,
    persistent,
    norm_gains,
    write_rate,
    forget,
    momentum,
    prompt_spans,
):
    share_rows = tokens.shape[0]
    head_count = lax.axis_size("head")
    seq_count = lax.axis_size("seq")
    block_rows = share_rows * head_count
    heads_here = write_rate.shape[1]
    current_width = heads_here * HS
    seq_index = lax.axis_index("seq")
    head_index = lax.axis_index("head")
    qkv_blocks = qkv_weight.reshape(D, 3, heads_here, HS)
    highest = lax.Precision.HIGHEST

    def token_project(piece, start):
        normed = rms_scale(piece.astype(jnp.float32), norm_gains[0]).astype(jnp.bfloat16)
        return jnp.einsum(
            "td,dshe->shte", normed, qkv_blocks, preferred_element_type=jnp.float32
        ).astype(jnp.bfloat16)

    projected = to_owners(tokens, token_project)
    out_full = lax.all_gather(
        out_weight + (projected[0, 0, 0, 0] * 0).astype(out_weight.dtype), "head", axis=0, tiled=True
    )
    query_unit = unit_rows(projected[0])
    key_unit = unit_rows(projected[1])
    value_rows = projected[2]
    moved_keys, moved_values = passed_along((key_unit, value_rows), "seq", 1)
    all_keys = jnp.concatenate([moved_keys, key_unit], axis=1)
    all_values = jnp.concatenate([moved_values, value_rows], axis=1)
    first_row = seq_index * block_rows
    query_positions = first_row + jnp.arange(block_rows, dtype=jnp.int32)
    key_positions = first_row - block_rows + jnp.arange(2 * block_rows, dtype=jnp.int32)
    query_segments = segment_starts(query_positions, prompt_spans)
    allowed = (key_positions[None, :] >= query_segments[:, None]) & (
        key_positions[None, :] <= query_positions[:, None]
    )
    persist_keys = persistent[0].reshape(NPER, heads_here, HS)
    persist_values = persistent[1].reshape(NPER, heads_here, HS)
    scores = score_scale * jnp.einsum(
        "hqd,hkd->hqk", query_unit, all_keys, preferred_element_type=jnp.float32
    )
    scores = jnp.where(allowed[None], scores, masked_score)
    extra = score_scale * jnp.einsum(
        "hqd,phd->hqp", query_unit, persist_keys, preferred_element_type=jnp.float32
    )
    top = jnp.maximum(jnp.max(scores, axis=-1), jnp.max(extra, axis=-1))[..., None]
    near = jnp.where(allowed[None], jnp.exp(scores - top), 0.0)
    far = jnp.exp(extra - top)
    total = jnp.sum(near, axis=-1, keepdims=True) + jnp.sum(far, axis=-1, keepdims=True)
    near_weights = (near / total).astype(jnp.bfloat16)
    far_weights = (far / total).astype(jnp.bfloat16)
    attended = jnp.einsum(
        "hqk,hkd->hqd", near_weights, all_values, preferred_element_type=jnp.float32
    )
    attended = attended + jnp.einsum(
        "hqp,phd->hqd", far_weights, persist_values, preferred_element_type=jnp.float32
    )
    total_spans = block_rows // CH
    span_queries = query_unit.reshape(heads_here, total_spans, CH, HS)
    span_keys = key_unit.reshape(heads_here, total_spans, CH, HS)
    span_values = value_rows.reshape(heads_here, total_spans, CH, HS)
    span_rates = jnp.transpose(write_rate).reshape(heads_here, total_spans, CH)
    prompt_ends = jnp.cumsum(prompt_spans)
    first_spans = prompt_ends - prompt_spans
    span_ids = seq_index * total_spans + jnp.arange(total_spans, dtype=jnp.int32)
    keep = jnp.where(jnp.any(span_ids[:, None] == first_spans[None, :], axis=1), 0.0, 1.0).astype(
        jnp.float32
    )
    causal = (jnp.arange(CH)[:, None] >= jnp.arange(CH)[None, :]).astype(jnp.float32)
    values_wide = span_values.astype(jnp.float32)
    written = jnp.einsum(
        "hcti,hctj->hcij",
        span_rates[..., None] * values_wide,
        span_keys.astype(jnp.float32),
        precision=highest,
    )
    affinity = jnp.einsum(
        "hctd,hcsd->hcts", span_queries, span_keys, preferred_element_type=jnp.float32
    )
    affinity = affinity * causal[None, None] * span_rates[:, :, None, :]
    local_recall = jnp.einsum("hcts,hcsi->hcti", affinity, values_wide, precision=highest)
    decay_memory = forget * keep[:, None]
    decay_moment = momentum * keep[:, None]
    span_index = jnp.arange(total_spans)
    inside = (span_index[None, None, :] > span_index[None, :, None]) & (
        span_index[None, None, :] <= span_index[:, None, None]
    )
    lower = span_index[None, :] <= span_index[:, None]

    def range_products(rates):
        picked = jnp.where(inside[..., None], rates[None, None], 1.0)
        return jnp.where(lower[..., None], jnp.prod(picked, axis=2), 0.0)

    memory_span = range_products(decay_memory)
    moment_span = range_products(decay_moment)
    memory_coeffs = jnp.sum(memory_span[:, :, None, :] * moment_span[None, :, :, :], axis=1)
    memory_from_start = jnp.prod(jnp.where(lower[..., None], decay_memory[None], 1.0), axis=1)
    moment_from_start = jnp.prod(jnp.where(lower[..., None], decay_moment[None], 1.0), axis=1)
    memory_from_moment = jnp.sum(memory_span * moment_from_start[None], axis=1)
    coeffs_state = jnp.stack([memory_from_start, memory_from_moment, moment_from_start], axis=-1)
    identity_coeffs = jnp.tile(jnp.array([1.0, 0.0, 1.0], jnp.float32), (heads_here, 1))
    zero_state = jnp.zeros((heads_here, HS, HS), jnp.float32)
    memory_states = jnp.einsum("cjh,hjab->hcab", memory_coeffs, written, precision=highest)
    last_moment = jnp.einsum("jh,hjab->hab", moment_span[-1], written, precision=highest)
    last_memory = memory_states[:, -1]
    last_coeffs = coeffs_state[-1]
    memory_before = jnp.concatenate([zero_state[:, None], memory_states[:, :-1]], axis=1)
    coeffs_before = jnp.transpose(
        jnp.concatenate([identity_coeffs[None], coeffs_state[:-1]], axis=0), (1, 0, 2)
    )

    def pack(state):
        coeff_rows = jnp.zeros((heads_here, 8, HS), jnp.float32).at[:, 0, :3].set(state[0])
        return jnp.concatenate([state[1], state[2], coeff_rows], axis=1)

    def unpack(packed):
        return (packed[:, 2 * HS, :3], packed[:, :HS], packed[:, HS : 2 * HS])

    identity_state = (identity_coeffs, zero_state, zero_state)
    identity_packed = pack(identity_state)

    def moved_by(packed, distance):
        moved = passed_along(packed, "seq", distance)
        return jnp.where(seq_index >= distance, moved, identity_packed)

    prefix = moved_by(pack((last_coeffs, last_memory, last_moment)), 1)
    distance = 1
    while distance < seq_count:
        prefix = pack(chain_combine(unpack(moved_by(prefix, distance)), unpack(prefix)))
        distance *= 2
    _, incoming_memory, incoming_moment = unpack(prefix)
    true_before = (
        memory_before
        + coeffs_before[..., 0, None, None] * incoming_memory[:, None]
        + coeffs_before[..., 1, None, None] * incoming_moment[:, None]
    )
    recalled = local_recall + jnp.einsum(
        "hcij,hctj->hcti",
        true_before * keep[None, :, None, None],
        span_queries.astype(jnp.float32),
        precision=highest,
    )
    memory_after = memory_states
    coeffs_after = jnp.transpose(coeffs_state, (1, 0, 2))
    true_after = (
        memory_after
        + coeffs_after[..., 0, None, None] * incoming_memory[:, None]
        + coeffs_after[..., 1, None, None] * incoming_moment[:, None]
    )
    spread = jnp.sqrt(jnp.mean(true_after * true_after, axis=(2, 3)))
    hit_spans = span_ids[None, :] == (prompt_ends - 1)[:, None]
    state_slots = jnp.sum(jnp.where(hit_spans[:, None, :], spread[None], 0.0), axis=2)
    mixed = (attended + recalled.reshape(heads_here, block_rows, HS)).astype(jnp.bfloat16)
    ff_here = down_weight.shape[0]
    gate_up = up_weight.reshape(D, 2 * ff_here)

    state_rms = jnp.sum(lax.all_gather(state_slots, "seq"), axis=0)

    def ffn_hidden(normed_rows):
        normed_rows = normed_rows + (state_rms[0, 0] * 0).astype(normed_rows.dtype)
        gated = jnp.dot(normed_rows, gate_up, preferred_element_type=jnp.float32)
        return (jax.nn.silu(gated[:, :ff_here]) * gated[:, ff_here:]).astype(jnp.bfloat16)

    def ffn_project(piece, start):
        return ffn_hidden(piece)

    pieces = jnp.transpose(mixed.reshape(heads_here, head_count, share_rows, HS), (1, 0, 2, 3))
    swapped = lax.all_to_all(pieces, "head", 0, 0, tiled=False)
    mixed_rows = jnp.transpose(swapped, (2, 0, 1, 3)).reshape(share_rows, head_count * current_width)
    residual = tokens.astype(jnp.float32) + jnp.dot(
        mixed_rows, out_full, preferred_element_type=jnp.float32
    )
    hidden = to_owners(rms_scale(residual, norm_gains[1]).astype(jnp.bfloat16), ffn_project)

    def down_term(start, count):
        return jnp.dot(hidden, down_weight, preferred_element_type=jnp.float32)

    down_sum = lax.psum_scatter(
        down_term(0, 0).astype(jnp.bfloat16), "head", scatter_dimension=0, tiled=True
    )
    second = residual + down_sum.astype(jnp.float32)
    final = rms_scale(second, norm_gains[2]).astype(jnp.bfloat16)

    def vocab_maxima(piece, start):
        return jnp.max(jnp.dot(piece, vocab_weight, preferred_element_type=jnp.float32), axis=1)

    received = {0: final}
    for distance in range(1, head_count):
        for direction in (1, -1):
            shift = direction * distance
            pairs = [
                (i, i + shift) for i in range(head_count) if 0 <= i + shift < head_count
            ]
            received[shift] = lax.ppermute(final, "head", pairs)
    block_maxima = {0: vocab_maxima(final, 0)}
    for distance in range(1, head_count):
        paired = vocab_maxima(
            jnp.concatenate([received[distance], received[-distance]], axis=0), 0
        )
        block_maxima[distance] = paired[:share_rows]
        block_maxima[-distance] = paired[share_rows:]
    owner_maxima = []
    for owner in range(head_count):
        picked = jnp.zeros((share_rows,), jnp.float32)
        for shift, maxima in block_maxima.items():
            picked = jnp.where(head_index - shift == owner, maxima, picked)
        owner_maxima.append(picked)
    row_maxima = jnp.concatenate(owner_maxima)
    logit_max = lax.pmax(row_maxima, "head")
    return (logit_max, state_rms)


def solution(mesh):
    in_specs = (
        P(("seq", "head"), None),
        P(None, None, "head"),
        P("head", None),
        P(None, None, "head"),
        P("head", None),
        P(None, "head"),
        P(None, None, "head"),
        P(),
        P("seq", "head"),
        P("seq", "head"),
        P("seq", "head"),
        P(),
    )
    out_specs = (P("seq"), P(None, "head"))
    return jax.shard_map(local, mesh=mesh, in_specs=in_specs, out_specs=out_specs, check_vma=False)
```

```python
import jax
import jax.numpy as jnp
from jax import lax
from jax.sharding import PartitionSpec as P

D = 1024
HS = 128
NPER = 16
SEG = 1024
CH = 64
SEQS = 4


eps_norm = 1e-05
eps_unit = 1e-06
score_scale = 10.0
masked_score = -1e30


def passed_along(array, axis, by):
    size = lax.axis_size(axis)
    pairs = [(i, i + by) for i in range(size) if 0 <= i + by < size]
    return lax.ppermute(array, axis, pairs)


def carried_in(part, axis, combine, identity):
    place = lax.axis_index(axis)
    gathered = jax.tree.map(lambda a: lax.all_gather(a, axis), part)
    state = jax.tree.map(lambda a, e: jnp.zeros_like(a) + jnp.asarray(e, a.dtype), part, identity)

    def one(step, state):
        return combine(
            state, jax.tree.map(lambda a: lax.dynamic_index_in_dim(a, step, 0, False), gathered)
        )

    return lax.fori_loop(0, place, one, state)


def rms_scale(values, gain):
    return values * lax.rsqrt(jnp.mean(values * values, axis=-1, keepdims=True) + eps_norm) * gain


def unit_rows(values):
    widened = values.astype(jnp.float32)
    return (
        widened * lax.rsqrt(jnp.sum(widened * widened, axis=-1, keepdims=True) + eps_unit)
    ).astype(jnp.bfloat16)


def segment_starts(positions, prompt_spans):
    prompt_ends = jnp.cumsum(prompt_spans)
    first_tokens = (prompt_ends - prompt_spans) * CH
    reached = positions[:, None] >= first_tokens[None, :]
    prompt_first = jnp.max(jnp.where(reached, first_tokens[None, :], 0), axis=1)
    return prompt_first + (positions - prompt_first) // SEG * SEG


def compose(later, earlier):
    return jnp.stack(
        [
            later[..., 0] * earlier[..., 0],
            later[..., 0] * earlier[..., 1] + later[..., 1] * earlier[..., 2],
            later[..., 2] * earlier[..., 2],
        ],
        axis=-1,
    )


def apply_map(coeffs, memory, moment):
    moved_memory = coeffs[:, 0, None, None] * memory + coeffs[:, 1, None, None] * moment
    return (moved_memory, coeffs[:, 2, None, None] * moment)


def chain_combine(earlier, later):
    moved_memory, moved_moment = apply_map(later[0], earlier[1], earlier[2])
    return (compose(later[0], earlier[0]), moved_memory + later[1], moved_moment + later[2])


def to_owners(local_rows, project):
    return project(lax.all_gather(local_rows, "head", axis=0, tiled=True), jnp.int32(0))


def from_owners(term, share_rows):
    return lax.psum_scatter(
        term(jnp.int32(0), share_rows * lax.axis_size("head")),
        "head",
        scatter_dimension=0,
        tiled=True,
    )


def local(
    tokens,
    qkv_weight,
    out_weight,
    up_weight,
    down_weight,
    vocab_weight,
    persistent,
    norm_gains,
    write_rate,
    forget,
    momentum,
    prompt_spans,
):
    share_rows = tokens.shape[0]
    head_count = lax.axis_size("head")
    seq_count = lax.axis_size("seq")
    block_rows = share_rows * head_count
    heads_here = write_rate.shape[1]
    current_width = heads_here * HS
    seq_index = lax.axis_index("seq")
    head_index = lax.axis_index("head")
    qkv_blocks = qkv_weight.reshape(D, 3, heads_here, HS)
    highest = lax.Precision.HIGHEST

    def token_project(piece, start):
        normed = rms_scale(piece.astype(jnp.float32), norm_gains[0]).astype(jnp.bfloat16)
        return jnp.einsum(
            "td,dshe->shte", normed, qkv_blocks, preferred_element_type=jnp.float32
        ).astype(jnp.bfloat16)

    projected = to_owners(tokens, token_project)
    out_full = lax.all_gather(
        out_weight + (projected[0, 0, 0, 0] * 0).astype(out_weight.dtype), "head", axis=0, tiled=True
    )
    query_unit = unit_rows(projected[0])
    key_unit = unit_rows(projected[1])
    value_rows = projected[2]
    moved_keys, moved_values = passed_along((key_unit, value_rows), "seq", 1)
    all_keys = jnp.concatenate([moved_keys, key_unit], axis=1)
    all_values = jnp.concatenate([moved_values, value_rows], axis=1)
    first_row = seq_index * block_rows
    query_positions = first_row + jnp.arange(block_rows, dtype=jnp.int32)
    key_positions = first_row - block_rows + jnp.arange(2 * block_rows, dtype=jnp.int32)
    query_segments = segment_starts(query_positions, prompt_spans)
    allowed = (key_positions[None, :] >= query_segments[:, None]) & (
        key_positions[None, :] <= query_positions[:, None]
    )
    persist_keys = persistent[0].reshape(NPER, heads_here, HS)
    persist_values = persistent[1].reshape(NPER, heads_here, HS)
    scores = score_scale * jnp.einsum(
        "hqd,hkd->hqk", query_unit, all_keys, preferred_element_type=jnp.float32
    )
    scores = jnp.where(allowed[None], scores, masked_score)
    extra = score_scale * jnp.einsum(
        "hqd,phd->hqp", query_unit, persist_keys, preferred_element_type=jnp.float32
    )
    top = jnp.maximum(jnp.max(scores, axis=-1), jnp.max(extra, axis=-1))[..., None]
    near = jnp.where(allowed[None], jnp.exp(scores - top), 0.0)
    far = jnp.exp(extra - top)
    total = jnp.sum(near, axis=-1, keepdims=True) + jnp.sum(far, axis=-1, keepdims=True)
    near_weights = (near / total).astype(jnp.bfloat16)
    far_weights = (far / total).astype(jnp.bfloat16)
    attended = jnp.einsum(
        "hqk,hkd->hqd", near_weights, all_values, preferred_element_type=jnp.float32
    )
    attended = attended + jnp.einsum(
        "hqp,phd->hqd", far_weights, persist_values, preferred_element_type=jnp.float32
    )
    total_spans = block_rows // CH
    span_queries = query_unit.reshape(heads_here, total_spans, CH, HS)
    span_keys = key_unit.reshape(heads_here, total_spans, CH, HS)
    span_values = value_rows.reshape(heads_here, total_spans, CH, HS)
    span_rates = jnp.transpose(write_rate).reshape(heads_here, total_spans, CH)
    prompt_ends = jnp.cumsum(prompt_spans)
    first_spans = prompt_ends - prompt_spans
    span_ids = seq_index * total_spans + jnp.arange(total_spans, dtype=jnp.int32)
    keep = jnp.where(jnp.any(span_ids[:, None] == first_spans[None, :], axis=1), 0.0, 1.0).astype(
        jnp.float32
    )
    causal = (jnp.arange(CH)[:, None] >= jnp.arange(CH)[None, :]).astype(jnp.float32)
    values_wide = span_values.astype(jnp.float32)
    written = jnp.einsum(
        "hcti,hctj->hcij",
        span_rates[..., None] * values_wide,
        span_keys.astype(jnp.float32),
        precision=highest,
    )
    affinity = jnp.einsum(
        "hctd,hcsd->hcts", span_queries, span_keys, preferred_element_type=jnp.float32
    )
    affinity = affinity * causal[None, None] * span_rates[:, :, None, :]
    local_recall = jnp.einsum("hcts,hcsi->hcti", affinity, values_wide, precision=highest)
    decay_memory = forget * keep[:, None]
    decay_moment = momentum * keep[:, None]
    span_index = jnp.arange(total_spans)
    inside = (span_index[None, None, :] > span_index[None, :, None]) & (
        span_index[None, None, :] <= span_index[:, None, None]
    )
    lower = span_index[None, :] <= span_index[:, None]

    def range_products(rates):
        picked = jnp.where(inside[..., None], rates[None, None], 1.0)
        return jnp.where(lower[..., None], jnp.prod(picked, axis=2), 0.0)

    memory_span = range_products(decay_memory)
    moment_span = range_products(decay_moment)
    memory_coeffs = jnp.sum(memory_span[:, :, None, :] * moment_span[None, :, :, :], axis=1)
    memory_from_start = jnp.prod(jnp.where(lower[..., None], decay_memory[None], 1.0), axis=1)
    moment_from_start = jnp.prod(jnp.where(lower[..., None], decay_moment[None], 1.0), axis=1)
    memory_from_moment = jnp.sum(memory_span * moment_from_start[None], axis=1)
    coeffs_state = jnp.stack([memory_from_start, memory_from_moment, moment_from_start], axis=-1)
    identity_coeffs = jnp.tile(jnp.array([1.0, 0.0, 1.0], jnp.float32), (heads_here, 1))
    zero_state = jnp.zeros((heads_here, HS, HS), jnp.float32)
    memory_states = jnp.einsum("cjh,hjab->hcab", memory_coeffs, written, precision=highest)
    last_moment = jnp.einsum("jh,hjab->hab", moment_span[-1], written, precision=highest)
    last_memory = memory_states[:, -1]
    last_coeffs = coeffs_state[-1]
    memory_before = jnp.concatenate([zero_state[:, None], memory_states[:, :-1]], axis=1)
    coeffs_before = jnp.transpose(
        jnp.concatenate([identity_coeffs[None], coeffs_state[:-1]], axis=0), (1, 0, 2)
    )

    def pack(state):
        coeff_rows = jnp.zeros((heads_here, 8, HS), jnp.float32).at[:, 0, :3].set(state[0])
        return jnp.concatenate([state[1], state[2], coeff_rows], axis=1)

    def unpack(packed):
        return (packed[:, 2 * HS, :3], packed[:, :HS], packed[:, HS : 2 * HS])

    identity_state = (identity_coeffs, zero_state, zero_state)
    identity_packed = pack(identity_state)

    def moved_by(packed, distance):
        moved = passed_along(packed, "seq", distance)
        return jnp.where(seq_index >= distance, moved, identity_packed)

    prefix = moved_by(pack((last_coeffs, last_memory, last_moment)), 1)
    distance = 1
    while distance < seq_count:
        prefix = pack(chain_combine(unpack(moved_by(prefix, distance)), unpack(prefix)))
        distance *= 2
    _, incoming_memory, incoming_moment = unpack(prefix)
    true_before = (
        memory_before
        + coeffs_before[..., 0, None, None] * incoming_memory[:, None]
        + coeffs_before[..., 1, None, None] * incoming_moment[:, None]
    )
    recalled = local_recall + jnp.einsum(
        "hcij,hctj->hcti",
        true_before * keep[None, :, None, None],
        span_queries.astype(jnp.float32),
        precision=highest,
    )
    memory_after = memory_states
    coeffs_after = jnp.transpose(coeffs_state, (1, 0, 2))
    true_after = (
        memory_after
        + coeffs_after[..., 0, None, None] * incoming_memory[:, None]
        + coeffs_after[..., 1, None, None] * incoming_moment[:, None]
    )
    spread = jnp.sqrt(jnp.mean(true_after * true_after, axis=(2, 3)))
    hit_spans = span_ids[None, :] == (prompt_ends - 1)[:, None]
    state_slots = jnp.sum(jnp.where(hit_spans[:, None, :], spread[None], 0.0), axis=2)
    mixed = (attended + recalled.reshape(heads_here, block_rows, HS)).astype(jnp.bfloat16)
    ff_here = down_weight.shape[0]
    gate_up = up_weight.reshape(D, 2 * ff_here)

    state_rms = jnp.sum(lax.all_gather(state_slots, "seq"), axis=0)

    def ffn_hidden(normed_rows):
        normed_rows = normed_rows + (state_rms[0, 0] * 0).astype(normed_rows.dtype)
        gated = jnp.dot(normed_rows, gate_up, preferred_element_type=jnp.float32)
        return (jax.nn.silu(gated[:, :ff_here]) * gated[:, ff_here:]).astype(jnp.bfloat16)

    def ffn_project(piece, start):
        return ffn_hidden(piece)

    pieces = jnp.transpose(mixed.reshape(heads_here, head_count, share_rows, HS), (1, 0, 2, 3))
    swapped = lax.all_to_all(pieces, "head", 0, 0, tiled=False)
    mixed_rows = jnp.transpose(swapped, (2, 0, 1, 3)).reshape(share_rows, head_count * current_width)
    residual = tokens.astype(jnp.float32) + jnp.dot(
        mixed_rows, out_full, preferred_element_type=jnp.float32
    )
    hidden = to_owners(rms_scale(residual, norm_gains[1]).astype(jnp.bfloat16), ffn_project)

    def down_term(start, count):
        return jnp.dot(hidden, down_weight, preferred_element_type=jnp.float32)

    down_sum = lax.psum_scatter(
        down_term(0, 0).astype(jnp.bfloat16), "head", scatter_dimension=0, tiled=True
    )
    second = residual + down_sum.astype(jnp.float32)
    final = rms_scale(second, norm_gains[2]).astype(jnp.bfloat16)

    def vocab_maxima(piece, start):
        return jnp.max(jnp.dot(piece, vocab_weight, preferred_element_type=jnp.float32), axis=1)

    received = {0: final}
    for distance in reversed(range(1, head_count)):
        for direction in (1, -1):
            shift = direction * distance
            pairs = [
                (i, i + shift) for i in range(head_count) if 0 <= i + shift < head_count
            ]
            received[shift] = lax.ppermute(final, "head", pairs)
    block_maxima = {0: vocab_maxima(final, 0)}
    for distance in range(1, head_count):
        for direction in (1, -1):
            block_maxima[direction * distance] = vocab_maxima(received[direction * distance], 0)
    owner_maxima = []
    for owner in range(head_count):
        picked = jnp.zeros((share_rows,), jnp.float32)
        for shift, maxima in block_maxima.items():
            picked = jnp.where(head_index - shift == owner, maxima, picked)
        owner_maxima.append(picked)
    row_maxima = jnp.concatenate(owner_maxima)
    logit_max = lax.pmax(row_maxima, "head")
    return (logit_max, state_rms)


def solution(mesh):
    in_specs = (
        P(("seq", "head"), None),
        P(None, None, "head"),
        P("head", None),
        P(None, None, "head"),
        P("head", None),
        P(None, "head"),
        P(None, None, "head"),
        P(),
        P("seq", "head"),
        P("seq", "head"),
        P("seq", "head"),
        P(),
    )
    out_specs = (P("seq"), P(None, "head"))
    return jax.shard_map(local, mesh=mesh, in_specs=in_specs, out_specs=out_specs, check_vma=False)
```

```python
import jax
import jax.numpy as jnp
from jax import lax
from jax.sharding import PartitionSpec as P

D = 1024
HS = 128
NPER = 16
SEG = 1024
CH = 64
SEQS = 4


eps_norm = 1e-05
eps_unit = 1e-06
score_scale = 10.0
masked_score = -1e30


def passed_along(array, axis, by):
    size = lax.axis_size(axis)
    pairs = [(i, i + by) for i in range(size) if 0 <= i + by < size]
    return lax.ppermute(array, axis, pairs)


def carried_in(part, axis, combine, identity):
    place = lax.axis_index(axis)
    gathered = jax.tree.map(lambda a: lax.all_gather(a, axis), part)
    state = jax.tree.map(lambda a, e: jnp.zeros_like(a) + jnp.asarray(e, a.dtype), part, identity)

    def one(step, state):
        return combine(
            state, jax.tree.map(lambda a: lax.dynamic_index_in_dim(a, step, 0, False), gathered)
        )

    return lax.fori_loop(0, place, one, state)


def rms_scale(values, gain):
    return values * lax.rsqrt(jnp.mean(values * values, axis=-1, keepdims=True) + eps_norm) * gain


def unit_rows(values):
    widened = values.astype(jnp.float32)
    return (
        widened * lax.rsqrt(jnp.sum(widened * widened, axis=-1, keepdims=True) + eps_unit)
    ).astype(jnp.bfloat16)


def segment_starts(positions, prompt_spans):
    prompt_ends = jnp.cumsum(prompt_spans)
    first_tokens = (prompt_ends - prompt_spans) * CH
    reached = positions[:, None] >= first_tokens[None, :]
    prompt_first = jnp.max(jnp.where(reached, first_tokens[None, :], 0), axis=1)
    return prompt_first + (positions - prompt_first) // SEG * SEG


def compose(later, earlier):
    return jnp.stack(
        [
            later[..., 0] * earlier[..., 0],
            later[..., 0] * earlier[..., 1] + later[..., 1] * earlier[..., 2],
            later[..., 2] * earlier[..., 2],
        ],
        axis=-1,
    )


def apply_map(coeffs, memory, moment):
    moved_memory = coeffs[:, 0, None, None] * memory + coeffs[:, 1, None, None] * moment
    return (moved_memory, coeffs[:, 2, None, None] * moment)


def chain_combine(earlier, later):
    moved_memory, moved_moment = apply_map(later[0], earlier[1], earlier[2])
    return (compose(later[0], earlier[0]), moved_memory + later[1], moved_moment + later[2])


def to_owners(local_rows, project):
    return project(lax.all_gather(local_rows, "head", axis=0, tiled=True), jnp.int32(0))


def from_owners(term, share_rows):
    return lax.psum_scatter(
        term(jnp.int32(0), share_rows * lax.axis_size("head")),
        "head",
        scatter_dimension=0,
        tiled=True,
    )


def local(
    tokens,
    qkv_weight,
    out_weight,
    up_weight,
    down_weight,
    vocab_weight,
    persistent,
    norm_gains,
    write_rate,
    forget,
    momentum,
    prompt_spans,
):
    share_rows = tokens.shape[0]
    head_count = lax.axis_size("head")
    seq_count = lax.axis_size("seq")
    block_rows = share_rows * head_count
    heads_here = write_rate.shape[1]
    current_width = heads_here * HS
    seq_index = lax.axis_index("seq")
    head_index = lax.axis_index("head")
    qkv_blocks = qkv_weight.reshape(D, 3, heads_here, HS)
    highest = lax.Precision.HIGHEST

    def token_project(piece, start):
        normed = rms_scale(piece.astype(jnp.float32), norm_gains[0]).astype(jnp.bfloat16)
        return jnp.einsum(
            "td,dshe->shte", normed, qkv_blocks, preferred_element_type=jnp.float32
        ).astype(jnp.bfloat16)

    projected = to_owners(tokens, token_project)
    out_full = lax.all_gather(
        out_weight + (projected[0, 0, 0, 0] * 0).astype(out_weight.dtype), "head", axis=0, tiled=True
    )
    query_unit = unit_rows(projected[0])
    key_unit = unit_rows(projected[1])
    value_rows = projected[2]
    moved_keys, moved_values = passed_along((key_unit, value_rows), "seq", 1)
    all_keys = jnp.concatenate([moved_keys, key_unit], axis=1)
    all_values = jnp.concatenate([moved_values, value_rows], axis=1)
    first_row = seq_index * block_rows
    query_positions = first_row + jnp.arange(block_rows, dtype=jnp.int32)
    key_positions = first_row - block_rows + jnp.arange(2 * block_rows, dtype=jnp.int32)
    query_segments = segment_starts(query_positions, prompt_spans)
    allowed = (key_positions[None, :] >= query_segments[:, None]) & (
        key_positions[None, :] <= query_positions[:, None]
    )
    persist_keys = persistent[0].reshape(NPER, heads_here, HS)
    persist_values = persistent[1].reshape(NPER, heads_here, HS)
    scores = score_scale * jnp.einsum(
        "hqd,hkd->hqk", query_unit, all_keys, preferred_element_type=jnp.float32
    )
    scores = jnp.where(allowed[None], scores, masked_score)
    extra = score_scale * jnp.einsum(
        "hqd,phd->hqp", query_unit, persist_keys, preferred_element_type=jnp.float32
    )
    top = jnp.maximum(jnp.max(scores, axis=-1), jnp.max(extra, axis=-1))[..., None]
    near = jnp.where(allowed[None], jnp.exp(scores - top), 0.0)
    far = jnp.exp(extra - top)
    total = jnp.sum(near, axis=-1, keepdims=True) + jnp.sum(far, axis=-1, keepdims=True)
    near_weights = (near / total).astype(jnp.bfloat16)
    far_weights = (far / total).astype(jnp.bfloat16)
    attended = jnp.einsum(
        "hqk,hkd->hqd", near_weights, all_values, preferred_element_type=jnp.float32
    )
    attended = attended + jnp.einsum(
        "hqp,phd->hqd", far_weights, persist_values, preferred_element_type=jnp.float32
    )
    total_spans = block_rows // CH
    span_queries = query_unit.reshape(heads_here, total_spans, CH, HS)
    span_keys = key_unit.reshape(heads_here, total_spans, CH, HS)
    span_values = value_rows.reshape(heads_here, total_spans, CH, HS)
    span_rates = jnp.transpose(write_rate).reshape(heads_here, total_spans, CH)
    prompt_ends = jnp.cumsum(prompt_spans)
    first_spans = prompt_ends - prompt_spans
    span_ids = seq_index * total_spans + jnp.arange(total_spans, dtype=jnp.int32)
    keep = jnp.where(jnp.any(span_ids[:, None] == first_spans[None, :], axis=1), 0.0, 1.0).astype(
        jnp.float32
    )
    causal = (jnp.arange(CH)[:, None] >= jnp.arange(CH)[None, :]).astype(jnp.float32)
    values_wide = span_values.astype(jnp.float32)
    written = jnp.einsum(
        "hcti,hctj->hcij",
        span_rates[..., None] * values_wide,
        span_keys.astype(jnp.float32),
        precision=highest,
    )
    affinity = jnp.einsum(
        "hctd,hcsd->hcts", span_queries, span_keys, preferred_element_type=jnp.float32
    )
    affinity = affinity * causal[None, None] * span_rates[:, :, None, :]
    local_recall = jnp.einsum("hcts,hcsi->hcti", affinity, values_wide, precision=highest)
    decay_memory = forget * keep[:, None]
    decay_moment = momentum * keep[:, None]
    span_index = jnp.arange(total_spans)
    inside = (span_index[None, None, :] > span_index[None, :, None]) & (
        span_index[None, None, :] <= span_index[:, None, None]
    )
    lower = span_index[None, :] <= span_index[:, None]

    def range_products(rates):
        picked = jnp.where(inside[..., None], rates[None, None], 1.0)
        return jnp.where(lower[..., None], jnp.prod(picked, axis=2), 0.0)

    memory_span = range_products(decay_memory)
    moment_span = range_products(decay_moment)
    memory_coeffs = jnp.sum(memory_span[:, :, None, :] * moment_span[None, :, :, :], axis=1)
    memory_from_start = jnp.prod(jnp.where(lower[..., None], decay_memory[None], 1.0), axis=1)
    moment_from_start = jnp.prod(jnp.where(lower[..., None], decay_moment[None], 1.0), axis=1)
    memory_from_moment = jnp.sum(memory_span * moment_from_start[None], axis=1)
    coeffs_state = jnp.stack([memory_from_start, memory_from_moment, moment_from_start], axis=-1)
    identity_coeffs = jnp.tile(jnp.array([1.0, 0.0, 1.0], jnp.float32), (heads_here, 1))
    zero_state = jnp.zeros((heads_here, HS, HS), jnp.float32)
    memory_states = jnp.einsum("cjh,hjab->hcab", memory_coeffs, written, precision=highest)
    last_moment = jnp.einsum("jh,hjab->hab", moment_span[-1], written, precision=highest)
    last_memory = memory_states[:, -1]
    last_coeffs = coeffs_state[-1]
    memory_before = jnp.concatenate([zero_state[:, None], memory_states[:, :-1]], axis=1)
    coeffs_before = jnp.transpose(
        jnp.concatenate([identity_coeffs[None], coeffs_state[:-1]], axis=0), (1, 0, 2)
    )

    def pack(state):
        coeff_rows = jnp.zeros((heads_here, 8, HS), jnp.float32).at[:, 0, :3].set(state[0])
        return jnp.concatenate([state[1], state[2], coeff_rows], axis=1)

    def unpack(packed):
        return (packed[:, 2 * HS, :3], packed[:, :HS], packed[:, HS : 2 * HS])

    identity_state = (identity_coeffs, zero_state, zero_state)
    identity_packed = pack(identity_state)

    def moved_by(packed, distance):
        moved = passed_along(packed, "seq", distance)
        return jnp.where(seq_index >= distance, moved, identity_packed)

    prefix = moved_by(pack((last_coeffs, last_memory, last_moment)), 1)
    distance = 1
    while distance < seq_count:
        prefix = pack(chain_combine(unpack(moved_by(prefix, distance)), unpack(prefix)))
        distance *= 2
    _, incoming_memory, incoming_moment = unpack(prefix)
    true_before = (
        memory_before
        + coeffs_before[..., 0, None, None] * incoming_memory[:, None]
        + coeffs_before[..., 1, None, None] * incoming_moment[:, None]
    )
    recalled = local_recall + jnp.einsum(
        "hcij,hctj->hcti",
        true_before * keep[None, :, None, None],
        span_queries.astype(jnp.float32),
        precision=highest,
    )
    memory_after = memory_states
    coeffs_after = jnp.transpose(coeffs_state, (1, 0, 2))
    true_after = (
        memory_after
        + coeffs_after[..., 0, None, None] * incoming_memory[:, None]
        + coeffs_after[..., 1, None, None] * incoming_moment[:, None]
    )
    spread = jnp.sqrt(jnp.mean(true_after * true_after, axis=(2, 3)))
    hit_spans = span_ids[None, :] == (prompt_ends - 1)[:, None]
    state_slots = jnp.sum(jnp.where(hit_spans[:, None, :], spread[None], 0.0), axis=2)
    mixed = (attended + recalled.reshape(heads_here, block_rows, HS)).astype(jnp.bfloat16)
    ff_here = down_weight.shape[0]
    gate_up = up_weight.reshape(D, 2 * ff_here)

    state_rms = jnp.sum(lax.all_gather(state_slots, "seq"), axis=0)

    def ffn_hidden(normed_rows):
        normed_rows = normed_rows + (state_rms[0, 0] * 0).astype(normed_rows.dtype)
        gated = jnp.dot(normed_rows, gate_up, preferred_element_type=jnp.float32)
        return (jax.nn.silu(gated[:, :ff_here]) * gated[:, ff_here:]).astype(jnp.bfloat16)

    def ffn_project(piece, start):
        return ffn_hidden(piece)

    pieces = jnp.transpose(mixed.reshape(heads_here, head_count, share_rows, HS), (1, 0, 2, 3))
    swapped = lax.all_to_all(pieces, "head", 0, 0, tiled=False)
    mixed_rows = jnp.transpose(swapped, (2, 0, 1, 3)).reshape(share_rows, head_count * current_width)
    residual = tokens.astype(jnp.float32) + jnp.dot(
        mixed_rows, out_full, preferred_element_type=jnp.float32
    )
    ffn_in = rms_scale(residual, norm_gains[1]).astype(jnp.bfloat16)
    hidden = jnp.zeros((block_rows + share_rows, ff_here), jnp.bfloat16)
    hidden = lax.dynamic_update_slice(hidden, ffn_hidden(ffn_in), (head_index * share_rows, 0))
    for distance in range(1, head_count):
        for direction in (1, -1):
            shift = direction * distance
            rows = passed_along(ffn_in, "head", shift)
            source = head_index - shift
            valid = (source >= 0) & (source < head_count)
            slot = jnp.where(valid, source, head_count) * share_rows
            hidden = lax.dynamic_update_slice(hidden, ffn_hidden(rows), (slot, 0))
    hidden = hidden[:block_rows]

    def down_term(start, count):
        return jnp.dot(hidden, down_weight, preferred_element_type=jnp.float32)

    down_sum = lax.psum_scatter(
        down_term(0, 0).astype(jnp.bfloat16), "head", scatter_dimension=0, tiled=True
    )
    second = residual + down_sum.astype(jnp.float32)
    final = rms_scale(second, norm_gains[2]).astype(jnp.bfloat16)

    def vocab_maxima(piece, start):
        return jnp.max(jnp.dot(piece, vocab_weight, preferred_element_type=jnp.float32), axis=1)

    received = {0: final}
    for distance in range(1, head_count):
        for direction in (1, -1):
            shift = direction * distance
            pairs = [
                (i, i + shift) for i in range(head_count) if 0 <= i + shift < head_count
            ]
            received[shift] = lax.ppermute(final, "head", pairs)
    block_maxima = {shift: vocab_maxima(rows, 0) for shift, rows in received.items()}
    owner_maxima = []
    for owner in range(head_count):
        picked = jnp.zeros((share_rows,), jnp.float32)
        for shift, maxima in block_maxima.items():
            picked = jnp.where(head_index - shift == owner, maxima, picked)
        owner_maxima.append(picked)
    row_maxima = jnp.concatenate(owner_maxima)
    logit_max = lax.pmax(row_maxima, "head")
    return (logit_max, state_rms)


def solution(mesh):
    in_specs = (
        P(("seq", "head"), None),
        P(None, None, "head"),
        P("head", None),
        P(None, None, "head"),
        P("head", None),
        P(None, "head"),
        P(None, None, "head"),
        P(),
        P("seq", "head"),
        P("seq", "head"),
        P("seq", "head"),
        P(),
    )
    out_specs = (P("seq"), P(None, "head"))
    return jax.shard_map(local, mesh=mesh, in_specs=in_specs, out_specs=out_specs, check_vma=False)
```

```python
import jax
import jax.numpy as jnp
from jax import lax
from jax.sharding import PartitionSpec as P

D = 1024
HS = 128
NPER = 16
SEG = 1024
CH = 64
SEQS = 4


eps_norm = 1e-05
eps_unit = 1e-06
score_scale = 10.0
masked_score = -1e30


def passed_along(array, axis, by):
    size = lax.axis_size(axis)
    pairs = [(i, i + by) for i in range(size) if 0 <= i + by < size]
    return lax.ppermute(array, axis, pairs)


def carried_in(part, axis, combine, identity):
    place = lax.axis_index(axis)
    gathered = jax.tree.map(lambda a: lax.all_gather(a, axis), part)
    state = jax.tree.map(lambda a, e: jnp.zeros_like(a) + jnp.asarray(e, a.dtype), part, identity)

    def one(step, state):
        return combine(
            state, jax.tree.map(lambda a: lax.dynamic_index_in_dim(a, step, 0, False), gathered)
        )

    return lax.fori_loop(0, place, one, state)


def rms_scale(values, gain):
    return values * lax.rsqrt(jnp.mean(values * values, axis=-1, keepdims=True) + eps_norm) * gain


def unit_rows(values):
    widened = values.astype(jnp.float32)
    return (
        widened * lax.rsqrt(jnp.sum(widened * widened, axis=-1, keepdims=True) + eps_unit)
    ).astype(jnp.bfloat16)


def segment_starts(positions, prompt_spans):
    prompt_ends = jnp.cumsum(prompt_spans)
    first_tokens = (prompt_ends - prompt_spans) * CH
    reached = positions[:, None] >= first_tokens[None, :]
    prompt_first = jnp.max(jnp.where(reached, first_tokens[None, :], 0), axis=1)
    return prompt_first + (positions - prompt_first) // SEG * SEG


def compose(later, earlier):
    return jnp.stack(
        [
            later[..., 0] * earlier[..., 0],
            later[..., 0] * earlier[..., 1] + later[..., 1] * earlier[..., 2],
            later[..., 2] * earlier[..., 2],
        ],
        axis=-1,
    )


def apply_map(coeffs, memory, moment):
    moved_memory = coeffs[:, 0, None, None] * memory + coeffs[:, 1, None, None] * moment
    return (moved_memory, coeffs[:, 2, None, None] * moment)


def chain_combine(earlier, later):
    moved_memory, moved_moment = apply_map(later[0], earlier[1], earlier[2])
    return (compose(later[0], earlier[0]), moved_memory + later[1], moved_moment + later[2])


def to_owners(local_rows, project):
    return project(lax.all_gather(local_rows, "head", axis=0, tiled=True), jnp.int32(0))


def from_owners(term, share_rows):
    return lax.psum_scatter(
        term(jnp.int32(0), share_rows * lax.axis_size("head")),
        "head",
        scatter_dimension=0,
        tiled=True,
    )


def local(
    tokens,
    qkv_weight,
    out_weight,
    up_weight,
    down_weight,
    vocab_weight,
    persistent,
    norm_gains,
    write_rate,
    forget,
    momentum,
    prompt_spans,
):
    share_rows = tokens.shape[0]
    head_count = lax.axis_size("head")
    seq_count = lax.axis_size("seq")
    block_rows = share_rows * head_count
    heads_here = write_rate.shape[1]
    current_width = heads_here * HS
    seq_index = lax.axis_index("seq")
    head_index = lax.axis_index("head")
    qkv_blocks = qkv_weight.reshape(D, 3, heads_here, HS)
    highest = lax.Precision.HIGHEST

    def token_project(piece, start):
        normed = rms_scale(piece.astype(jnp.float32), norm_gains[0]).astype(jnp.bfloat16)
        return jnp.einsum(
            "td,dshe->shte", normed, qkv_blocks, preferred_element_type=jnp.float32
        ).astype(jnp.bfloat16)

    projected = to_owners(tokens, token_project)
    out_full = lax.all_gather(
        out_weight + (projected[0, 0, 0, 0] * 0).astype(out_weight.dtype), "head", axis=0, tiled=True
    )
    query_unit = unit_rows(projected[0])
    key_unit = unit_rows(projected[1])
    value_rows = projected[2]
    moved_keys, moved_values = passed_along((key_unit, value_rows), "seq", 1)
    all_keys = jnp.concatenate([moved_keys, key_unit], axis=1)
    all_values = jnp.concatenate([moved_values, value_rows], axis=1)
    first_row = seq_index * block_rows
    query_positions = first_row + jnp.arange(block_rows, dtype=jnp.int32)
    key_positions = first_row - block_rows + jnp.arange(2 * block_rows, dtype=jnp.int32)
    query_segments = segment_starts(query_positions, prompt_spans)
    allowed = (key_positions[None, :] >= query_segments[:, None]) & (
        key_positions[None, :] <= query_positions[:, None]
    )
    persist_keys = persistent[0].reshape(NPER, heads_here, HS)
    persist_values = persistent[1].reshape(NPER, heads_here, HS)
    scores = score_scale * jnp.einsum(
        "hqd,hkd->hqk", query_unit, all_keys, preferred_element_type=jnp.float32
    )
    scores = jnp.where(allowed[None], scores, masked_score)
    extra = score_scale * jnp.einsum(
        "hqd,phd->hqp", query_unit, persist_keys, preferred_element_type=jnp.float32
    )
    top = jnp.maximum(jnp.max(scores, axis=-1), jnp.max(extra, axis=-1))[..., None]
    near = jnp.where(allowed[None], jnp.exp(scores - top), 0.0)
    far = jnp.exp(extra - top)
    total = jnp.sum(near, axis=-1, keepdims=True) + jnp.sum(far, axis=-1, keepdims=True)
    near_weights = (near / total).astype(jnp.bfloat16)
    far_weights = (far / total).astype(jnp.bfloat16)
    attended = jnp.einsum(
        "hqk,hkd->hqd", near_weights, all_values, preferred_element_type=jnp.float32
    )
    attended = attended + jnp.einsum(
        "hqp,phd->hqd", far_weights, persist_values, preferred_element_type=jnp.float32
    )
    total_spans = block_rows // CH
    span_queries = query_unit.reshape(heads_here, total_spans, CH, HS)
    span_keys = key_unit.reshape(heads_here, total_spans, CH, HS)
    span_values = value_rows.reshape(heads_here, total_spans, CH, HS)
    span_rates = jnp.transpose(write_rate).reshape(heads_here, total_spans, CH)
    prompt_ends = jnp.cumsum(prompt_spans)
    first_spans = prompt_ends - prompt_spans
    span_ids = seq_index * total_spans + jnp.arange(total_spans, dtype=jnp.int32)
    keep = jnp.where(jnp.any(span_ids[:, None] == first_spans[None, :], axis=1), 0.0, 1.0).astype(
        jnp.float32
    )
    causal = (jnp.arange(CH)[:, None] >= jnp.arange(CH)[None, :]).astype(jnp.float32)
    values_wide = span_values.astype(jnp.float32)
    written = jnp.einsum(
        "hcti,hctj->hcij",
        span_rates[..., None] * values_wide,
        span_keys.astype(jnp.float32),
        precision=highest,
    )
    affinity = jnp.einsum(
        "hctd,hcsd->hcts", span_queries, span_keys, preferred_element_type=jnp.float32
    )
    affinity = affinity * causal[None, None] * span_rates[:, :, None, :]
    local_recall = jnp.einsum("hcts,hcsi->hcti", affinity, values_wide, precision=highest)
    decay_memory = forget * keep[:, None]
    decay_moment = momentum * keep[:, None]
    span_index = jnp.arange(total_spans)
    inside = (span_index[None, None, :] > span_index[None, :, None]) & (
        span_index[None, None, :] <= span_index[:, None, None]
    )
    lower = span_index[None, :] <= span_index[:, None]

    def range_products(rates):
        picked = jnp.where(inside[..., None], rates[None, None], 1.0)
        return jnp.where(lower[..., None], jnp.prod(picked, axis=2), 0.0)

    memory_span = range_products(decay_memory)
    moment_span = range_products(decay_moment)
    memory_coeffs = jnp.sum(memory_span[:, :, None, :] * moment_span[None, :, :, :], axis=1)
    memory_from_start = jnp.prod(jnp.where(lower[..., None], decay_memory[None], 1.0), axis=1)
    moment_from_start = jnp.prod(jnp.where(lower[..., None], decay_moment[None], 1.0), axis=1)
    memory_from_moment = jnp.sum(memory_span * moment_from_start[None], axis=1)
    coeffs_state = jnp.stack([memory_from_start, memory_from_moment, moment_from_start], axis=-1)
    identity_coeffs = jnp.tile(jnp.array([1.0, 0.0, 1.0], jnp.float32), (heads_here, 1))
    zero_state = jnp.zeros((heads_here, HS, HS), jnp.float32)
    memory_states = jnp.einsum("cjh,hjab->hcab", memory_coeffs, written, precision=highest)
    last_moment = jnp.einsum("jh,hjab->hab", moment_span[-1], written, precision=highest)
    last_memory = memory_states[:, -1]
    last_coeffs = coeffs_state[-1]
    memory_before = jnp.concatenate([zero_state[:, None], memory_states[:, :-1]], axis=1)
    coeffs_before = jnp.transpose(
        jnp.concatenate([identity_coeffs[None], coeffs_state[:-1]], axis=0), (1, 0, 2)
    )

    def pack(state):
        coeff_rows = jnp.zeros((heads_here, 8, HS), jnp.float32).at[:, 0, :3].set(state[0])
        return jnp.concatenate([state[1], state[2], coeff_rows], axis=1)

    def unpack(packed):
        return (packed[:, 2 * HS, :3], packed[:, :HS], packed[:, HS : 2 * HS])

    identity_state = (identity_coeffs, zero_state, zero_state)
    identity_packed = pack(identity_state)

    def moved_by(packed, distance):
        moved = passed_along(packed, "seq", distance)
        return jnp.where(seq_index >= distance, moved, identity_packed)

    prefix = moved_by(pack((last_coeffs, last_memory, last_moment)), 1)
    distance = 1
    while distance < seq_count:
        prefix = pack(chain_combine(unpack(moved_by(prefix, distance)), unpack(prefix)))
        distance *= 2
    _, incoming_memory, incoming_moment = unpack(prefix)
    true_before = (
        memory_before
        + coeffs_before[..., 0, None, None] * incoming_memory[:, None]
        + coeffs_before[..., 1, None, None] * incoming_moment[:, None]
    )
    recalled = local_recall + jnp.einsum(
        "hcij,hctj->hcti",
        true_before * keep[None, :, None, None],
        span_queries.astype(jnp.float32),
        precision=highest,
    )
    memory_after = memory_states
    coeffs_after = jnp.transpose(coeffs_state, (1, 0, 2))
    true_after = (
        memory_after
        + coeffs_after[..., 0, None, None] * incoming_memory[:, None]
        + coeffs_after[..., 1, None, None] * incoming_moment[:, None]
    )
    spread = jnp.sqrt(jnp.mean(true_after * true_after, axis=(2, 3)))
    hit_spans = span_ids[None, :] == (prompt_ends - 1)[:, None]
    state_slots = jnp.sum(jnp.where(hit_spans[:, None, :], spread[None], 0.0), axis=2)
    mixed = (attended + recalled.reshape(heads_here, block_rows, HS)).astype(jnp.bfloat16)
    ff_here = down_weight.shape[0]
    gate_up = up_weight.reshape(D, 2 * ff_here)

    state_rms = jnp.sum(lax.all_gather(state_slots, "seq"), axis=0)

    def ffn_hidden(normed_rows):
        normed_rows = normed_rows + (state_rms[0, 0] * 0).astype(normed_rows.dtype)
        gated = jnp.dot(normed_rows, gate_up, preferred_element_type=jnp.float32)
        return (jax.nn.silu(gated[:, :ff_here]) * gated[:, ff_here:]).astype(jnp.bfloat16)

    def ffn_project(piece, start):
        return ffn_hidden(piece)

    pieces = jnp.transpose(mixed.reshape(heads_here, head_count, share_rows, HS), (1, 0, 2, 3))
    swapped = lax.all_to_all(pieces, "head", 0, 0, tiled=False)
    mixed_rows = jnp.transpose(swapped, (2, 0, 1, 3)).reshape(share_rows, head_count * current_width)
    residual = tokens.astype(jnp.float32) + jnp.dot(
        mixed_rows, out_full, preferred_element_type=jnp.float32
    )
    hidden = to_owners(rms_scale(residual, norm_gains[1]).astype(jnp.bfloat16), ffn_project)

    def down_term(start, count):
        return jnp.dot(hidden, down_weight, preferred_element_type=jnp.float32)

    down_sum = lax.psum_scatter(
        down_term(0, 0).astype(jnp.bfloat16), "head", scatter_dimension=0, tiled=True
    )
    second = residual + down_sum.astype(jnp.float32)
    final = rms_scale(second, norm_gains[2]).astype(jnp.bfloat16)

    def vocab_maxima(piece, start):
        return jnp.max(jnp.dot(piece, vocab_weight, preferred_element_type=jnp.float32), axis=1)

    received = {0: final}
    for distance in range(1, head_count):
        for direction in (1, -1):
            shift = direction * distance
            pairs = [
                (i, i + shift) for i in range(head_count) if 0 <= i + shift < head_count
            ]
            received[shift] = lax.ppermute(final, "head", pairs)
    block_maxima = {shift: vocab_maxima(rows, 0) for shift, rows in received.items()}
    owner_maxima = []
    for owner in range(head_count):
        picked = jnp.zeros((share_rows,), jnp.float32)
        for shift, maxima in block_maxima.items():
            picked = jnp.where(head_index - shift == owner, maxima, picked)
        owner_maxima.append(picked)
    row_maxima = jnp.concatenate(owner_maxima)
    logit_max = jnp.max(lax.all_gather(row_maxima, "head"), axis=0)
    return (logit_max, state_rms)


def solution(mesh):
    in_specs = (
        P(("seq", "head"), None),
        P(None, None, "head"),
        P("head", None),
        P(None, None, "head"),
        P("head", None),
        P(None, "head"),
        P(None, None, "head"),
        P(),
        P("seq", "head"),
        P("seq", "head"),
        P("seq", "head"),
        P(),
    )
    out_specs = (P("seq"), P(None, "head"))
    return jax.shard_map(local, mesh=mesh, in_specs=in_specs, out_specs=out_specs, check_vma=False)
```
